32 devices in a mesh: grp: 2 (over x), smp: 16 (over z, y, core).
Axes of the slice: x: 2, y: 2, z: 4, core: 2. Of those that a mesh axis runs over, the one named last changes fastest.
Arguments:
- state: bfloat16 [512, 16, 1024], P(('grp', 'smp')), parts along dimension 0, may hold values from -40 to 40
- unit_slot: int32 [512, 64], P(('grp', 'smp')), parts along dimension 0, may hold values from 0 to 511
- token_count: int32 [512], P(('grp', 'smp')), parts along dimension 0, may hold values from 48 to 64, as said below
- session: int32 [512], P(('grp', 'smp')), parts along dimension 0, may hold values from 0 to 15, as said below
- session_row: int32 [32], P('grp'), parts along dimension 0, may hold values from 0 to 15, as said below
- unit_count: int32 [16], replicated, may hold values from 128 to 512, as said below
- panels: bfloat16 [16, 512, 1024], P('smp'), may hold values from -40 to 40
- memory_key: bfloat16 [512, 1024], P(('grp', 'smp')), parts along dimension 0, may hold values from -240 to 240
- memory_value: bfloat16 [512, 1024], P(('grp', 'smp')), parts along dimension 0, may hold values from -24 to 24
- q1_weight: bfloat16 [1024, 1024], replicated, may hold values from -0.1875 to 0.1875
- o1_weight: bfloat16 [1024, 1024], replicated, may hold values from -0.1875 to 0.1875
- kv_weight: bfloat16 [1024, 2048], replicated, may hold values from -6 to 6
- q2_weight: bfloat16 [1024, 1024], replicated, may hold values from -0.1875 to 0.1875
- o2_weight: bfloat16 [1024, 1024], replicated, may hold values from -0.1875 to 0.1875
Outputs:
- latent_out: bfloat16 [512, 16, 1024], P(('grp', 'smp')), parts along dimension 0
The draws below stay inside these ranges and needn't reach their ends.
There are 2 independent parts, one for each index of `grp`. The reference program is written for one: setup_inputs(seed, part) draws one part's arguments, and reference() takes and returns one part's arrays. A program takes and returns all parts, laid end to end along the dimension named above; an argument that names none is the same for every part. Nothing has to cross between parts.
Inputs may be any that keep to these rules, and one draw needn't show every extreme that they name: The panel row of session s is session_row[s]; it lies on the device of index session_row[s]. session_row is a permutation. The 16 samples of one device have sessions on 16 different devices; one device holds the session of one sample on every device. `token_count`: some sample on every device has 64 tokens. `unit_count`: some panel row has 512 units.
All inputs are finite; a program needn't handle non-finite values.
Results may differ from the reference program's by a relative error of at most 0.007.
The reference program's roundings to bfloat16 on the way count: a program that leaves them out, or rounds other values in their place, can miss the bound.
Values may be sent and summed in bfloat16 or wider, within the bound.
No kernel may reach another device: no remote copies, remote signals or barrier semaphores. Data moves between devices by JAX's collectives and lax.ppermute only.
A program may use at most 128 MiB of HBM per device.

```python
import math
import jax
import jax.numpy as jnp
from jax import lax

HEADS = 16
HEAD_DIM = 64
D = 1024
UNITS = 512
SESS_DEV = 1
B_DEV = 16
TOKS = 64
LAT = 16
SAMPLES = 256
SESSIONS = 16
MEMORY = 256
N_SMP = 16


def spread_field(key, shape):
    first, second, third = jax.random.split(key, 3)
    values_base = jnp.clip(jax.random.normal(first, shape, jnp.float32), -4.0, 4.0)
    row_shape = tuple(shape[:-1]) + (1,)
    row_scale = jnp.exp(jax.random.uniform(second, row_shape, jnp.float32, math.log(0.3), math.log(3.0)))
    col_scale = jnp.exp(jax.random.uniform(third, (shape[-1],), jnp.float32, math.log(0.3), math.log(3.0)))
    return values_base * row_scale * col_scale


def sample_plan(key):
    devices = SAMPLES // B_DEV
    shuffled = jax.random.permutation(jax.random.fold_in(key, 11), SESSIONS).astype(jnp.int32)
    inverse = jnp.argsort(shuffled, stable=True).astype(jnp.int32)
    hot_owner = jax.random.randint(jax.random.fold_in(key, 12), (), 0, devices)
    columns = jnp.arange(devices, dtype=jnp.int32)
    ranking = jax.random.randint(jax.random.fold_in(key, 13), (devices, devices), 0, 1 << 20) * devices + columns[None, :]
    ranking = jnp.where(columns[None, :] == hot_owner, -1, ranking)
    owner_sorted = jnp.argsort(ranking, axis=1, stable=True)[:, :B_DEV].astype(jnp.int32)
    places = jnp.arange(B_DEV, dtype=jnp.int32)
    mixing = jax.random.randint(jax.random.fold_in(key, 14), (devices, B_DEV), 0, 1 << 20) * B_DEV + places[None, :]
    order = jnp.argsort(mixing, axis=1, stable=True).astype(jnp.int32)
    owners = jnp.take_along_axis(owner_sorted, order, axis=1)
    slot_pick = jax.random.randint(jax.random.fold_in(key, 15), (devices, B_DEV), 0, SESS_DEV)
    sessions = inverse[owners * SESS_DEV + slot_pick].reshape(SAMPLES).astype(jnp.int32)
    counts = jax.random.randint(jax.random.fold_in(key, 16), (devices, B_DEV), 3 * TOKS // 4, TOKS + 1)
    counts = jnp.where(owners == hot_owner, TOKS, counts).reshape(SAMPLES).astype(jnp.int32)
    return (shuffled, sessions, counts)


def draw_state(key, part):
    return spread_field(key, (SAMPLES, LAT, D)).astype(jnp.bfloat16)


def draw_panels(key, part):
    return spread_field(key, (SESSIONS, UNITS, D)).astype(jnp.bfloat16)


def draw_memory_key(key, part):
    first = jax.random.fold_in(key, 0)
    values_base = jnp.clip(jax.random.normal(first, (MEMORY, D), jnp.float32), -4.0, 4.0)
    return values_base.astype(jnp.bfloat16)


def draw_kv_weight(key, part):
    first = jax.random.fold_in(key, 0)
    values_base = jnp.clip(jax.random.normal(first, (D, 2 * D), jnp.float32), -4.0, 4.0) * D ** (-0.5)
    return values_base.astype(jnp.bfloat16)


def draw_unit_count(key, part):
    counts = jax.random.randint(key, (SESSIONS,), UNITS // 4, UNITS + 1)
    chosen = jax.random.randint(jax.random.fold_in(key, 3), (), 0, SESSIONS)
    return jnp.where(jnp.arange(SESSIONS, dtype=jnp.int32) == chosen, UNITS, counts).astype(jnp.int32)


def draw_session_row(key, part):
    return sample_plan(key)[0]


def draw_session(key, part):
    return sample_plan(key)[1]


def draw_token_count(key, part):
    return sample_plan(key)[2]


def place_ends(array, rng, low, top_value):
    longest = array.shape.index(max(array.shape))
    spots = []
    for shift in (0, 1):
        where = [jax.random.randint(jax.random.fold_in(rng, axis), (), 0, length) for axis, length in enumerate(array.shape)]
        where[longest] = (where[longest] + shift) % array.shape[longest]
        spots.append(tuple(where))
    return array.at[spots[0]].set(low).at[spots[1]].set(top_value)


def shard_levels(key, shape, cuts, smallest, top_value):
    factor_of, own = 1.0, jax.random.fold_in(key, 6)
    for position, blocks in cuts:
        draws = jnp.exp(jax.random.uniform(jax.random.fold_in(own, position), (blocks,), jnp.float32, smallest / len(cuts), top_value / len(cuts)))
        factor_of = factor_of * jnp.repeat(draws, shape[position] // blocks).reshape([-1 if axis == position else 1 for axis in range(len(shape))])
    return factor_of


def bell_draw(own_key, extent, scale, bound, shards=(), kind=jnp.bfloat16):
    loudness = shard_levels(own_key, extent, shards, -0.22, 0.18) if shards else 1.0
    entries = jax.random.normal(own_key, extent, jnp.float32) * scale * loudness
    return jnp.minimum(jnp.maximum(entries, -bound), bound).astype(kind)


def setup_inputs(seed: int = 0, part: int = 0) -> dict:
    key_of = jax.random.split(jax.random.key(seed), 15)
    part_keys = jax.random.split(jax.random.fold_in(key_of[14], part), 15)
    state = draw_state(jax.random.fold_in(jax.random.fold_in(key_of[14], part), 71), part)
    unit_slot = place_ends(jax.random.randint(part_keys[1], (SAMPLES, TOKS), 0, UNITS), jax.random.fold_in(part_keys[1], 1), 0, UNITS - 1).astype(jnp.int32)
    token_count = draw_token_count(jax.random.fold_in(jax.random.fold_in(key_of[14], part), 71), part)
    session = draw_session(jax.random.fold_in(jax.random.fold_in(key_of[14], part), 71), part)
    session_row = draw_session_row(jax.random.fold_in(jax.random.fold_in(key_of[14], part), 71), part)
    unit_count = draw_unit_count(jax.random.fold_in(key_of[14], 71), part)
    panels = draw_panels(jax.random.fold_in(key_of[14], 71), part)
    memory_key = draw_memory_key(jax.random.fold_in(jax.random.fold_in(key_of[14], part), 71), part)
    memory_value = bell_draw(part_keys[8], (MEMORY, D), 4.0, 24.0, ((0, 16),))
    q1_weight = bell_draw(key_of[9], (D, D), D ** -0.5, 0.1875)
    o1_weight = bell_draw(key_of[10], (D, D), D ** -0.5, 0.1875)
    kv_weight = draw_kv_weight(jax.random.fold_in(key_of[14], 71), part)
    q2_weight = bell_draw(key_of[12], (D, D), D ** -0.5, 0.1875)
    o2_weight = bell_draw(key_of[13], (D, D), D ** -0.5, 0.1875)
    return {"state": state, "unit_slot": unit_slot, "token_count": token_count, "session": session, "session_row": session_row, "unit_count": unit_count, "panels": panels, "memory_key": memory_key, "memory_value": memory_value, "q1_weight": q1_weight, "o1_weight": o1_weight, "kv_weight": kv_weight, "q2_weight": q2_weight, "o2_weight": o2_weight}


masked_score = -1e+30

def normed(values):
    wide = values.astype(jnp.float32)
    return (wide * lax.rsqrt(lax.optimization_barrier(jnp.mean(wide * wide, axis=-1, keepdims=True)) + 1e-05)).astype(jnp.bfloat16)

def reference(state, unit_slot, token_count, session, session_row, unit_count, panels, memory_key, memory_value, q1_weight, o1_weight, kv_weight, q2_weight, o2_weight):
    score_scale = HEAD_DIM ** (-0.5)
    panel_table = panels.reshape(SESSIONS * UNITS, D)
    kv_table = jnp.dot(normed(panel_table), kv_weight, preferred_element_type=jnp.float32).astype(jnp.bfloat16)
    panel_row = session_row[session].astype(jnp.int32)
    unit_limit = unit_count[panel_row]
    token_index = (panel_row[:, None] * UNITS + unit_slot % unit_limit[:, None]).astype(jnp.int32)
    memory_keys = memory_key.astype(jnp.float32).reshape(MEMORY, HEADS, HEAD_DIM)
    memory_values = memory_value.astype(jnp.float32).reshape(MEMORY, HEADS, HEAD_DIM)

    def one_block(block_args):
        block_state, block_index, block_count = block_args
        flat_state = block_state.reshape(B_DEV * LAT, D)
        queries = jnp.dot(normed(flat_state), q1_weight, preferred_element_type=jnp.float32).astype(jnp.bfloat16)
        queries = queries.reshape(B_DEV * LAT, HEADS, HEAD_DIM)
        scores = jnp.einsum('rhd,khd->hrk', queries.astype(jnp.float32), memory_keys) * score_scale
        row_max = lax.optimization_barrier(jnp.max(scores, axis=-1, keepdims=True))
        exponent = jnp.exp(scores - row_max)
        weights = lax.optimization_barrier(exponent.astype(jnp.bfloat16)).astype(jnp.float32)
        weighted = jnp.einsum('hrk,khd->hrd', weights, memory_values) / lax.optimization_barrier(jnp.sum(exponent, axis=-1, keepdims=True))
        read_mem = jnp.transpose(weighted, (1, 0, 2)).reshape(B_DEV * LAT, D).astype(jnp.bfloat16)
        hidden = (flat_state.astype(jnp.float32) + jnp.dot(read_mem, o1_weight, preferred_element_type=jnp.float32)).astype(jnp.bfloat16)
        queries2 = jnp.dot(normed(hidden), q2_weight, preferred_element_type=jnp.float32).astype(jnp.bfloat16)
        queries2 = queries2.reshape(B_DEV, LAT, HEADS, HEAD_DIM).astype(jnp.float32)
        key_value = kv_table[block_index]
        key_rows = key_value[:, :, :D].astype(jnp.float32).reshape(B_DEV, TOKS, HEADS, HEAD_DIM)
        value_rows = key_value[:, :, D:].astype(jnp.float32).reshape(B_DEV, TOKS, HEADS, HEAD_DIM)
        live_tokens = jnp.arange(TOKS, dtype=jnp.int32)[None, :] < block_count[:, None]
        spike_scores = jnp.einsum('blhd,bkhd->bhlk', queries2, key_rows) * score_scale
        spike_scores = jnp.where(live_tokens[:, None, None, :], spike_scores, masked_score)
        spike_max = lax.optimization_barrier(jnp.max(spike_scores, axis=-1, keepdims=True))
        spike_exp = jnp.exp(spike_scores - spike_max)
        spike_weights = lax.optimization_barrier(spike_exp.astype(jnp.bfloat16)).astype(jnp.float32)
        denominator = jnp.transpose(lax.optimization_barrier(jnp.sum(spike_exp, axis=-1, keepdims=True)), (0, 2, 1, 3))
        spike_mix = jnp.einsum('bhlk,bkhd->blhd', spike_weights, value_rows) / denominator
        read_spike = spike_mix.reshape(B_DEV * LAT, D).astype(jnp.bfloat16)
        result = hidden.astype(jnp.float32) + jnp.dot(read_spike, o2_weight, preferred_element_type=jnp.float32)
        return result.astype(jnp.bfloat16).reshape(B_DEV, LAT, D)
    blocks = lax.map(one_block, (state.reshape(N_SMP, B_DEV, LAT, D), token_index.reshape(N_SMP, B_DEV, TOKS), token_count.reshape(N_SMP, B_DEV)))
    return blocks.reshape(SAMPLES, LAT, D)
```

```python
import jax
import jax.numpy as jnp
from jax import lax
from jax.sharding import PartitionSpec as P

HEAD_DIM = 64


masked_score = -1e30


def normed(values):
    wide = values.astype(jnp.float32)
    return (wide * lax.rsqrt(jnp.mean(wide * wide, axis=-1, keepdims=True) + 1e-05)).astype(
        jnp.bfloat16
    )


def attend(queries, key_rows, value_rows, live_tokens):
    samples, latents, head_count, head_size = queries.shape
    spike_scores = jnp.einsum(
        "blhd,bkhd->bhlk", queries, key_rows, preferred_element_type=jnp.float32
    ) * HEAD_DIM ** (-0.5)
    spike_scores = jnp.where(live_tokens[:, None, None, :], spike_scores, masked_score)
    spike_max = jnp.max(spike_scores, axis=-1, keepdims=True)
    spike_exp = jnp.exp(spike_scores - spike_max)
    denominator = jnp.transpose(jnp.sum(spike_exp, axis=-1, keepdims=True), (0, 2, 1, 3))
    spike_mix = (
        jnp.einsum(
            "bhlk,bkhd->blhd",
            spike_exp.astype(jnp.bfloat16),
            value_rows,
            preferred_element_type=jnp.float32,
        )
        / denominator
    )
    return spike_mix.reshape(samples, latents, head_count * head_size).astype(jnp.bfloat16)


def per_device(
    state,
    unit_slot,
    token_count,
    session,
    session_row,
    unit_count,
    panels,
    memory_key,
    memory_value,
    q1_weight,
    o1_weight,
    kv_weight,
    q2_weight,
    o2_weight,
):
    local_samples, latents, model_width = state.shape
    token_total = unit_slot.shape[1]
    owners = lax.axis_size("smp")
    sess_dev, unit_total = (panels.shape[0], panels.shape[1])
    head_count = model_width // HEAD_DIM
    session_ids = jnp.arange(session_row.shape[0], dtype=jnp.int32)
    panel_row = jnp.sum(
        jnp.where(session[:, None] == session_ids[None, :], session_row[None, :], 0), axis=1
    )
    unit_limit = jnp.sum(
        jnp.where(panel_row[:, None] == session_ids[None, :], unit_count[None, :], 0), axis=1
    )
    owner_rank = panel_row // sess_dev
    token_index = (panel_row % sess_dev * unit_total)[:, None] + unit_slot % unit_limit[:, None]
    slot_pick = owner_rank[None, :] == jnp.arange(owners, dtype=jnp.int32)[:, None]
    request = jnp.sum(jnp.where(slot_pick[:, :, None], token_index[None, :, :], 0), axis=1)
    live_tokens = jnp.arange(token_total, dtype=jnp.int32)[None, :] < token_count[:, None]
    panel_table = panels.reshape(sess_dev * unit_total, model_width)
    arrived = lax.all_to_all(
        panel_table[lax.all_to_all(request, "smp", split_axis=0, concat_axis=0, tiled=True)],
        "smp",
        split_axis=0,
        concat_axis=0,
        tiled=True,
    )
    row_total = local_samples * latents
    flat_state = state.reshape(row_total, model_width)
    queries = jnp.dot(normed(flat_state), q1_weight, preferred_element_type=jnp.float32).astype(
        jnp.bfloat16
    )
    queries = queries.reshape(row_total, head_count, HEAD_DIM)
    running_max = jnp.full((head_count, row_total), masked_score, jnp.float32)
    memory_rows = lax.all_gather(
        jnp.concatenate([memory_key, memory_value], axis=1), "smp", axis=0, tiled=True
    )
    key_rows = memory_rows[:, :model_width].reshape(-1, head_count, HEAD_DIM)
    value_rows = memory_rows[:, model_width:].reshape(-1, head_count, HEAD_DIM)
    scores = jnp.einsum(
        "rhd,khd->hrk", queries, key_rows, preferred_element_type=jnp.float32
    ) * HEAD_DIM ** (-0.5)
    new_max = jnp.maximum(running_max, jnp.max(scores, axis=-1))
    exponent = jnp.exp(scores - new_max[:, :, None])
    denominator = jnp.sum(exponent, axis=-1)
    weighted = jnp.einsum(
        "hrk,khd->hrd",
        exponent.astype(jnp.bfloat16),
        value_rows,
        preferred_element_type=jnp.float32,
    )
    running_max, denominator, weighted = (new_max, denominator, weighted)
    read_mem = (
        jnp.transpose(weighted / denominator[:, :, None], (1, 0, 2))
        .reshape(row_total, model_width)
        .astype(jnp.bfloat16)
    )
    hidden = (
        flat_state.astype(jnp.float32)
        + jnp.dot(read_mem, o1_weight, preferred_element_type=jnp.float32)
    ).astype(jnp.bfloat16)
    queries2 = jnp.dot(normed(hidden), q2_weight, preferred_element_type=jnp.float32).astype(
        jnp.bfloat16
    )
    queries2 = queries2.reshape(local_samples, latents, model_width)
    embed = arrived[owner_rank]
    key_value = jnp.dot(
        normed(embed.reshape(local_samples * token_total, model_width)),
        kv_weight,
        preferred_element_type=jnp.float32,
    ).astype(jnp.bfloat16)
    key_value = key_value.reshape(local_samples, token_total, 2 * model_width)
    key_rows = key_value[:, :, :model_width].reshape(
        local_samples, token_total, head_count, HEAD_DIM
    )
    value_rows = key_value[:, :, model_width:].reshape(
        local_samples, token_total, head_count, HEAD_DIM
    )
    read_spike = attend(
        queries2.reshape(local_samples, latents, head_count, HEAD_DIM),
        key_rows,
        value_rows,
        live_tokens,
    )
    result = hidden.astype(jnp.float32) + jnp.dot(
        read_spike.reshape(row_total, model_width), o2_weight, preferred_element_type=jnp.float32
    )
    return result.astype(jnp.bfloat16).reshape(local_samples, latents, model_width)


def solution(mesh):
    in_specs = (
        P(("grp", "smp"), None, None),
        P(("grp", "smp"), None),
        P(("grp", "smp")),
        P(("grp", "smp")),
        P("grp"),
        P(),
        P("smp", None, None),
        P(("grp", "smp"), None),
        P(("grp", "smp"), None),
        P(),
        P(),
        P(),
        P(),
        P(),
    )
    out_specs = P(("grp", "smp"), None, None)
    return jax.shard_map(
        per_device, mesh=mesh, in_specs=in_specs, out_specs=out_specs, check_vma=False
    )
```

```python
import jax
import jax.numpy as jnp
from jax import lax
from jax.sharding import PartitionSpec as P

HEAD_DIM = 64


masked_score = -1e30


def normed(values):
    wide = values.astype(jnp.float32)
    return (wide * lax.rsqrt(jnp.mean(wide * wide, axis=-1, keepdims=True) + 1e-05)).astype(
        jnp.bfloat16
    )


def attend(queries, key_rows, value_rows, live_tokens):
    samples, latents, head_count, head_size = queries.shape
    spike_scores = jnp.einsum(
        "blhd,bkhd->bhlk", queries, key_rows, preferred_element_type=jnp.float32
    ) * HEAD_DIM ** (-0.5)
    spike_scores = jnp.where(live_tokens[:, None, None, :], spike_scores, masked_score)
    spike_max = jnp.max(spike_scores, axis=-1, keepdims=True)
    spike_exp = jnp.exp(spike_scores - spike_max)
    denominator = jnp.transpose(jnp.sum(spike_exp, axis=-1, keepdims=True), (0, 2, 1, 3))
    spike_mix = (
        jnp.einsum(
            "bhlk,bkhd->blhd",
            spike_exp.astype(jnp.bfloat16),
            value_rows,
            preferred_element_type=jnp.float32,
        )
        / denominator
    )
    return spike_mix.reshape(samples, latents, head_count * head_size).astype(jnp.bfloat16)


def per_device(
    state,
    unit_slot,
    token_count,
    session,
    session_row,
    unit_count,
    panels,
    memory_key,
    memory_value,
    q1_weight,
    o1_weight,
    kv_weight,
    q2_weight,
    o2_weight,
):
    local_samples, latents, model_width = state.shape
    token_total = unit_slot.shape[1]
    owners = lax.axis_size("smp")
    sess_dev, unit_total = (panels.shape[0], panels.shape[1])
    head_count = model_width // HEAD_DIM
    session_ids = jnp.arange(session_row.shape[0], dtype=jnp.int32)
    panel_row = jnp.sum(
        jnp.where(session[:, None] == session_ids[None, :], session_row[None, :], 0), axis=1
    )
    unit_limit = jnp.sum(
        jnp.where(panel_row[:, None] == session_ids[None, :], unit_count[None, :], 0), axis=1
    )
    owner_rank = panel_row // sess_dev
    token_index = (panel_row % sess_dev * unit_total)[:, None] + unit_slot % unit_limit[:, None]
    slot_pick = owner_rank[None, :] == jnp.arange(owners, dtype=jnp.int32)[:, None]
    request = jnp.sum(jnp.where(slot_pick[:, :, None], token_index[None, :, :], 0), axis=1)
    live_tokens = jnp.arange(token_total, dtype=jnp.int32)[None, :] < token_count[:, None]
    panel_table = panels.reshape(sess_dev * unit_total, model_width)
    arrived = lax.all_to_all(
        panel_table[lax.all_to_all(request, "smp", split_axis=0, concat_axis=0, tiled=True)],
        "smp",
        split_axis=0,
        concat_axis=0,
        tiled=True,
    )
    row_total = local_samples * latents
    flat_state = state.reshape(row_total, model_width)
    queries = jnp.dot(normed(flat_state), q1_weight, preferred_element_type=jnp.float32).astype(
        jnp.bfloat16
    )
    queries = queries.reshape(row_total, head_count, HEAD_DIM)
    running_max = jnp.full((head_count, row_total), masked_score, jnp.float32)
    memory_pair = jnp.concatenate([memory_key, memory_value], axis=1)
    memory_rows = lax.all_to_all(
        jnp.broadcast_to(memory_pair[None], (owners,) + memory_pair.shape),
        "smp",
        split_axis=0,
        concat_axis=0,
        tiled=True,
    ).reshape(-1, 2 * model_width)
    key_rows = memory_rows[:, :model_width].reshape(-1, head_count, HEAD_DIM)
    value_rows = memory_rows[:, model_width:].reshape(-1, head_count, HEAD_DIM)
    scores = jnp.einsum(
        "rhd,khd->hrk", queries, key_rows, preferred_element_type=jnp.float32
    ) * HEAD_DIM ** (-0.5)
    new_max = jnp.maximum(running_max, jnp.max(scores, axis=-1))
    exponent = jnp.exp(scores - new_max[:, :, None])
    denominator = jnp.sum(exponent, axis=-1)
    weighted = jnp.einsum(
        "hrk,khd->hrd",
        exponent.astype(jnp.bfloat16),
        value_rows,
        preferred_element_type=jnp.float32,
    )
    running_max, denominator, weighted = (new_max, denominator, weighted)
    read_mem = (
        jnp.transpose(weighted / denominator[:, :, None], (1, 0, 2))
        .reshape(row_total, model_width)
        .astype(jnp.bfloat16)
    )
    hidden = (
        flat_state.astype(jnp.float32)
        + jnp.dot(read_mem, o1_weight, preferred_element_type=jnp.float32)
    ).astype(jnp.bfloat16)
    queries2 = jnp.dot(normed(hidden), q2_weight, preferred_element_type=jnp.float32).astype(
        jnp.bfloat16
    )
    queries2 = queries2.reshape(local_samples, latents, model_width)
    embed = arrived[owner_rank]
    key_value = jnp.dot(
        normed(embed.reshape(local_samples * token_total, model_width)),
        kv_weight,
        preferred_element_type=jnp.float32,
    ).astype(jnp.bfloat16)
    key_value = key_value.reshape(local_samples, token_total, 2 * model_width)
    key_rows = key_value[:, :, :model_width].reshape(
        local_samples, token_total, head_count, HEAD_DIM
    )
    value_rows = key_value[:, :, model_width:].reshape(
        local_samples, token_total, head_count, HEAD_DIM
    )
    read_spike = attend(
        queries2.reshape(local_samples, latents, head_count, HEAD_DIM),
        key_rows,
        value_rows,
        live_tokens,
    )
    result = hidden.astype(jnp.float32) + jnp.dot(
        read_spike.reshape(row_total, model_width), o2_weight, preferred_element_type=jnp.float32
    )
    return result.astype(jnp.bfloat16).reshape(local_samples, latents, model_width)


def solution(mesh):
    in_specs = (
        P(("grp", "smp"), None, None),
        P(("grp", "smp"), None),
        P(("grp", "smp")),
        P(("grp", "smp")),
        P("grp"),
        P(),
        P("smp", None, None),
        P(("grp", "smp"), None),
        P(("grp", "smp"), None),
        P(),
        P(),
        P(),
        P(),
        P(),
    )
    out_specs = P(("grp", "smp"), None, None)
    return jax.shard_map(
        per_device, mesh=mesh, in_specs=in_specs, out_specs=out_specs, check_vma=False
    )
```

```python
import jax
import jax.numpy as jnp
from jax import lax
from jax.sharding import PartitionSpec as P

HEAD_DIM = 64


masked_score = -1e30


def normed(values):
    wide = values.astype(jnp.float32)
    return (wide * lax.rsqrt(jnp.mean(wide * wide, axis=-1, keepdims=True) + 1e-05)).astype(
        jnp.bfloat16
    )


def attend(queries, key_rows, value_rows, live_tokens):
    samples, latents, head_count, head_size = queries.shape
    spike_scores = jnp.einsum(
        "blhd,bkhd->bhlk", queries, key_rows, preferred_element_type=jnp.float32
    ) * HEAD_DIM ** (-0.5)
    spike_scores = jnp.where(live_tokens[:, None, None, :], spike_scores, masked_score)
    spike_max = jnp.max(spike_scores, axis=-1, keepdims=True)
    spike_exp = jnp.exp(spike_scores - spike_max)
    denominator = jnp.transpose(jnp.sum(spike_exp, axis=-1, keepdims=True), (0, 2, 1, 3))
    spike_mix = (
        jnp.einsum(
            "bhlk,bkhd->blhd",
            spike_exp.astype(jnp.bfloat16),
            value_rows,
            preferred_element_type=jnp.float32,
        )
        / denominator
    )
    return spike_mix.reshape(samples, latents, head_count * head_size).astype(jnp.bfloat16)


def per_device(
    state,
    unit_slot,
    token_count,
    session,
    session_row,
    unit_count,
    panels,
    memory_key,
    memory_value,
    q1_weight,
    o1_weight,
    kv_weight,
    q2_weight,
    o2_weight,
):
    local_samples, latents, model_width = state.shape
    token_total = unit_slot.shape[1]
    owners = lax.axis_size("smp")
    sess_dev, unit_total = (panels.shape[0], panels.shape[1])
    head_count = model_width // HEAD_DIM
    session_ids = jnp.arange(session_row.shape[0], dtype=jnp.int32)
    panel_row = jnp.sum(
        jnp.where(session[:, None] == session_ids[None, :], session_row[None, :], 0), axis=1
    )
    unit_limit = jnp.sum(
        jnp.where(panel_row[:, None] == session_ids[None, :], unit_count[None, :], 0), axis=1
    )
    owner_rank = panel_row // sess_dev
    token_index = (panel_row % sess_dev * unit_total)[:, None] + unit_slot % unit_limit[:, None]
    slot_pick = owner_rank[None, :] == jnp.arange(owners, dtype=jnp.int32)[:, None]
    request = jnp.sum(jnp.where(slot_pick[:, :, None], token_index[None, :, :], 0), axis=1)
    count_pick = jnp.sum(jnp.where(slot_pick, token_count[None, :], 0), axis=1)
    sample_pick = jnp.sum(
        jnp.where(slot_pick, jnp.arange(local_samples, dtype=jnp.int32)[None, :], 0), axis=1
    )
    served = lax.all_to_all(
        jnp.concatenate([request, count_pick[:, None]], axis=1),
        "smp",
        split_axis=0,
        concat_axis=0,
        tiled=True,
    )
    served_index = served[:, :token_total]
    live_tokens = jnp.arange(token_total, dtype=jnp.int32)[None, :] < served[:, token_total:]
    panel_table = panels.reshape(sess_dev * unit_total, model_width)
    served_embed = panel_table[served_index.reshape(-1)]
    row_total = local_samples * latents
    flat_state = state.reshape(row_total, model_width)
    queries = jnp.dot(normed(flat_state), q1_weight, preferred_element_type=jnp.float32).astype(
        jnp.bfloat16
    )
    queries = queries.reshape(row_total, head_count, HEAD_DIM)
    running_max = jnp.full((head_count, row_total), masked_score, jnp.float32)
    memory_pair = jnp.concatenate([memory_key, memory_value], axis=1)
    memory_rows = lax.all_to_all(
        jnp.broadcast_to(memory_pair[None], (owners,) + memory_pair.shape),
        "smp",
        split_axis=0,
        concat_axis=0,
        tiled=True,
    ).reshape(-1, 2 * model_width)
    key_rows = memory_rows[:, :model_width].reshape(-1, head_count, HEAD_DIM)
    value_rows = memory_rows[:, model_width:].reshape(-1, head_count, HEAD_DIM)
    scores = jnp.einsum(
        "rhd,khd->hrk", queries, key_rows, preferred_element_type=jnp.float32
    ) * HEAD_DIM ** (-0.5)
    new_max = jnp.maximum(running_max, jnp.max(scores, axis=-1))
    exponent = jnp.exp(scores - new_max[:, :, None])
    denominator = jnp.sum(exponent, axis=-1)
    weighted = jnp.einsum(
        "hrk,khd->hrd",
        exponent.astype(jnp.bfloat16),
        value_rows,
        preferred_element_type=jnp.float32,
    )
    running_max, denominator, weighted = (new_max, denominator, weighted)
    read_mem = (
        jnp.transpose(weighted / denominator[:, :, None], (1, 0, 2))
        .reshape(row_total, model_width)
        .astype(jnp.bfloat16)
    )
    hidden = (
        flat_state.astype(jnp.float32)
        + jnp.dot(read_mem, o1_weight, preferred_element_type=jnp.float32)
    ).astype(jnp.bfloat16)
    queries2 = jnp.dot(normed(hidden), q2_weight, preferred_element_type=jnp.float32).astype(
        jnp.bfloat16
    )
    queries2 = queries2.reshape(local_samples, latents, model_width)
    served_queries = lax.all_to_all(
        queries2[sample_pick], "smp", split_axis=0, concat_axis=0, tiled=True
    )
    key_value = jnp.dot(
        normed(served_embed),
        kv_weight,
        preferred_element_type=jnp.float32,
    ).astype(jnp.bfloat16)
    key_value = key_value.reshape(owners, token_total, 2 * model_width)
    key_rows = key_value[:, :, :model_width].reshape(owners, token_total, head_count, HEAD_DIM)
    value_rows = key_value[:, :, model_width:].reshape(owners, token_total, head_count, HEAD_DIM)
    served_read = attend(
        served_queries.reshape(owners, latents, head_count, HEAD_DIM),
        key_rows,
        value_rows,
        live_tokens,
    )
    read_spike = lax.all_to_all(
        served_read.reshape(owners, latents, model_width),
        "smp",
        split_axis=0,
        concat_axis=0,
        tiled=True,
    )[owner_rank]
    result = hidden.astype(jnp.float32) + jnp.dot(
        read_spike.reshape(row_total, model_width), o2_weight, preferred_element_type=jnp.float32
    )
    return result.astype(jnp.bfloat16).reshape(local_samples, latents, model_width)


def solution(mesh):
    in_specs = (
        P(("grp", "smp"), None, None),
        P(("grp", "smp"), None),
        P(("grp", "smp")),
        P(("grp", "smp")),
        P("grp"),
        P(),
        P("smp", None, None),
        P(("grp", "smp"), None),
        P(("grp", "smp"), None),
        P(),
        P(),
        P(),
        P(),
        P(),
    )
    out_specs = P(("grp", "smp"), None, None)
    return jax.shard_map(
        per_device, mesh=mesh, in_specs=in_specs, out_specs=out_specs, check_vma=False
    )
```

```python
import jax
import jax.numpy as jnp
from jax import lax
from jax.experimental import pallas as pl
from jax.experimental.pallas import tpu as pltpu
from jax.sharding import PartitionSpec as P

HEAD_DIM = 64


masked_score = -1e30


def normed(values):
    wide = values.astype(jnp.float32)
    return (wide * lax.rsqrt(jnp.mean(wide * wide, axis=-1, keepdims=True) + 1e-05)).astype(
        jnp.bfloat16
    )


def attend(queries, key_rows, value_rows, live_tokens):
    samples, latents, head_count, head_size = queries.shape
    spike_scores = jnp.einsum(
        "blhd,bkhd->bhlk", queries, key_rows, preferred_element_type=jnp.float32
    ) * HEAD_DIM ** (-0.5)
    spike_scores = jnp.where(live_tokens[:, None, None, :], spike_scores, masked_score)
    spike_max = jnp.max(spike_scores, axis=-1, keepdims=True)
    spike_exp = jnp.exp(spike_scores - spike_max)
    denominator = jnp.transpose(jnp.sum(spike_exp, axis=-1, keepdims=True), (0, 2, 1, 3))
    spike_mix = (
        jnp.einsum(
            "bhlk,bkhd->blhd",
            spike_exp.astype(jnp.bfloat16),
            value_rows,
            preferred_element_type=jnp.float32,
        )
        / denominator
    )
    return spike_mix.reshape(samples, latents, head_count * head_size).astype(jnp.bfloat16)


def attend_block(counts_ref, query_ref, key_ref, value_ref, out_ref):
    group = pl.program_id(0)
    latents = query_ref.shape[1]
    tokens = key_ref.shape[1]
    live = lax.broadcasted_iota(jnp.int32, (latents, tokens), 1) < counts_ref[group]
    first_head = lax.broadcasted_iota(jnp.int32, (1, 2 * HEAD_DIM), 1) < HEAD_DIM
    for pair in range(query_ref.shape[2] // (2 * HEAD_DIM)):
        cols = pl.ds(pair * 2 * HEAD_DIM, 2 * HEAD_DIM)
        query = query_ref[0, :, cols]
        key = key_ref[0, :, cols]
        value = value_ref[0, :, cols]
        mixes = []
        for half in (first_head, jnp.logical_not(first_head)):
            scores = lax.dot_general(
                jnp.where(half, query, jnp.zeros_like(query)),
                key,
                (((1,), (1,)), ((), ())),
                preferred_element_type=jnp.float32,
            ) * HEAD_DIM ** (-0.5)
            scores = jnp.where(live, scores, masked_score)
            row_max = jnp.max(scores, axis=1, keepdims=True)
            exponent = jnp.exp(scores - row_max)
            denominator = jnp.sum(exponent, axis=1, keepdims=True)
            mix = jnp.dot(
                exponent.astype(jnp.bfloat16), value, preferred_element_type=jnp.float32
            )
            mixes.append(mix / denominator)
        out_ref[0, :, cols] = jnp.where(first_head, mixes[0], mixes[1]).astype(jnp.bfloat16)


def attend_kernel(queries, key_value, counts):
    groups, latents, width = queries.shape
    tokens = key_value.shape[1]
    return pl.pallas_call(
        attend_block,
        grid_spec=pltpu.PrefetchScalarGridSpec(
            num_scalar_prefetch=1,
            grid=(groups,),
            in_specs=[
                pl.BlockSpec((1, latents, width), lambda g, c: (g, 0, 0)),
                pl.BlockSpec((1, tokens, width), lambda g, c: (g, 0, 0)),
                pl.BlockSpec((1, tokens, width), lambda g, c: (g, 0, 1)),
            ],
            out_specs=pl.BlockSpec((1, latents, width), lambda g, c: (g, 0, 0)),
        ),
        out_shape=jax.ShapeDtypeStruct((groups, latents, width), jnp.bfloat16),
    )(counts, queries, key_value, key_value)


def per_device(
    state,
    unit_slot,
    token_count,
    session,
    session_row,
    unit_count,
    panels,
    memory_key,
    memory_value,
    q1_weight,
    o1_weight,
    kv_weight,
    q2_weight,
    o2_weight,
):
    local_samples, latents, model_width = state.shape
    token_total = unit_slot.shape[1]
    owners = lax.axis_size("smp")
    sess_dev, unit_total = (panels.shape[0], panels.shape[1])
    head_count = model_width // HEAD_DIM
    session_ids = jnp.arange(session_row.shape[0], dtype=jnp.int32)
    panel_row = jnp.sum(
        jnp.where(session[:, None] == session_ids[None, :], session_row[None, :], 0), axis=1
    )
    unit_limit = jnp.sum(
        jnp.where(panel_row[:, None] == session_ids[None, :], unit_count[None, :], 0), axis=1
    )
    owner_rank = panel_row // sess_dev
    token_index = (panel_row % sess_dev * unit_total)[:, None] + unit_slot % unit_limit[:, None]
    slot_pick = owner_rank[None, :] == jnp.arange(owners, dtype=jnp.int32)[:, None]
    request = jnp.sum(jnp.where(slot_pick[:, :, None], token_index[None, :, :], 0), axis=1)
    count_pick = jnp.sum(jnp.where(slot_pick, token_count[None, :], 0), axis=1)
    sample_pick = jnp.sum(
        jnp.where(slot_pick, jnp.arange(local_samples, dtype=jnp.int32)[None, :], 0), axis=1
    )
    served = lax.all_to_all(
        jnp.concatenate([request, count_pick[:, None]], axis=1),
        "smp",
        split_axis=0,
        concat_axis=0,
        tiled=True,
    )
    served_index = served[:, :token_total]
    panel_table = panels.reshape(sess_dev * unit_total, model_width)
    served_embed = panel_table[served_index.reshape(-1)]
    row_total = local_samples * latents
    flat_state = state.reshape(row_total, model_width)
    queries = jnp.dot(normed(flat_state), q1_weight, preferred_element_type=jnp.float32).astype(
        jnp.bfloat16
    )
    memory_pair = jnp.concatenate([memory_key, memory_value], axis=1)
    memory_rows = lax.all_to_all(
        jnp.broadcast_to(memory_pair[None], (owners,) + memory_pair.shape),
        "smp",
        split_axis=0,
        concat_axis=0,
        tiled=True,
    ).reshape(1, -1, 2 * model_width)
    memory_total = memory_rows.shape[1]
    read_mem = attend_kernel(
        queries.reshape(1, row_total, model_width),
        memory_rows,
        jnp.full((1,), memory_total, jnp.int32),
    ).reshape(row_total, model_width)
    hidden = (
        flat_state.astype(jnp.float32)
        + jnp.dot(read_mem, o1_weight, preferred_element_type=jnp.float32)
    ).astype(jnp.bfloat16)
    queries2 = jnp.dot(normed(hidden), q2_weight, preferred_element_type=jnp.float32).astype(
        jnp.bfloat16
    )
    queries2 = queries2.reshape(local_samples, latents, model_width)
    served_queries = lax.all_to_all(
        queries2[sample_pick], "smp", split_axis=0, concat_axis=0, tiled=True
    )
    key_value = jnp.dot(
        normed(served_embed),
        kv_weight,
        preferred_element_type=jnp.float32,
    ).astype(jnp.bfloat16)
    key_value = key_value.reshape(owners, token_total, 2 * model_width)
    served_read = attend_kernel(served_queries, key_value, served[:, token_total])
    read_spike = lax.all_to_all(
        served_read.reshape(owners, latents, model_width),
        "smp",
        split_axis=0,
        concat_axis=0,
        tiled=True,
    )[owner_rank]
    result = hidden.astype(jnp.float32) + jnp.dot(
        read_spike.reshape(row_total, model_width), o2_weight, preferred_element_type=jnp.float32
    )
    return result.astype(jnp.bfloat16).reshape(local_samples, latents, model_width)


def solution(mesh):
    in_specs = (
        P(("grp", "smp"), None, None),
        P(("grp", "smp"), None),
        P(("grp", "smp")),
        P(("grp", "smp")),
        P("grp"),
        P(),
        P("smp", None, None),
        P(("grp", "smp"), None),
        P(("grp", "smp"), None),
        P(),
        P(),
        P(),
        P(),
        P(),
    )
    out_specs = P(("grp", "smp"), None, None)
    return jax.shard_map(
        per_device, mesh=mesh, in_specs=in_specs, out_specs=out_specs, check_vma=False
    )
```

```python
import jax
import jax.numpy as jnp
from jax import lax
from jax.experimental import pallas as pl
from jax.experimental.pallas import tpu as pltpu
from jax.sharding import PartitionSpec as P

HEAD_DIM = 64


masked_score = -1e30


def normed(values):
    wide = values.astype(jnp.float32)
    return (wide * lax.rsqrt(jnp.mean(wide * wide, axis=-1, keepdims=True) + 1e-05)).astype(
        jnp.bfloat16
    )


def attend(queries, key_rows, value_rows, live_tokens):
    samples, latents, head_count, head_size = queries.shape
    spike_scores = jnp.einsum(
        "blhd,bkhd->bhlk", queries, key_rows, preferred_element_type=jnp.float32
    ) * HEAD_DIM ** (-0.5)
    spike_scores = jnp.where(live_tokens[:, None, None, :], spike_scores, masked_score)
    spike_max = jnp.max(spike_scores, axis=-1, keepdims=True)
    spike_exp = jnp.exp(spike_scores - spike_max)
    denominator = jnp.transpose(jnp.sum(spike_exp, axis=-1, keepdims=True), (0, 2, 1, 3))
    spike_mix = (
        jnp.einsum(
            "bhlk,bkhd->blhd",
            spike_exp.astype(jnp.bfloat16),
            value_rows,
            preferred_element_type=jnp.float32,
        )
        / denominator
    )
    return spike_mix.reshape(samples, latents, head_count * head_size).astype(jnp.bfloat16)


def attend_block(counts_ref, query_ref, key_ref, value_ref, out_ref):
    group = pl.program_id(0)
    latents = query_ref.shape[1]
    tokens = key_ref.shape[1]
    live = lax.broadcasted_iota(jnp.int32, (latents, tokens), 1) < counts_ref[group]
    first_head = lax.broadcasted_iota(jnp.int32, (1, 2 * HEAD_DIM), 1) < HEAD_DIM
    for pair in range(query_ref.shape[2] // (2 * HEAD_DIM)):
        cols = pl.ds(pair * 2 * HEAD_DIM, 2 * HEAD_DIM)
        query = query_ref[0, :, cols]
        key = key_ref[0, :, cols]
        value = value_ref[0, :, cols]
        mixes = []
        for half in (first_head, jnp.logical_not(first_head)):
            scores = lax.dot_general(
                jnp.where(half, query, jnp.zeros_like(query)),
                key,
                (((1,), (1,)), ((), ())),
                preferred_element_type=jnp.float32,
            ) * HEAD_DIM ** (-0.5)
            scores = jnp.where(live, scores, masked_score)
            row_max = jnp.max(scores, axis=1, keepdims=True)
            exponent = jnp.exp(scores - row_max)
            denominator = jnp.sum(exponent, axis=1, keepdims=True)
            mix = jnp.dot(
                exponent.astype(jnp.bfloat16), value, preferred_element_type=jnp.float32
            )
            mixes.append(mix / denominator)
        out_ref[0, :, cols] = jnp.where(first_head, mixes[0], mixes[1]).astype(jnp.bfloat16)


def attend_kernel(queries, key_value, counts):
    groups, latents, width = queries.shape
    tokens = key_value.shape[1]
    return pl.pallas_call(
        attend_block,
        grid_spec=pltpu.PrefetchScalarGridSpec(
            num_scalar_prefetch=1,
            grid=(groups,),
            in_specs=[
                pl.BlockSpec((1, latents, width), lambda g, c: (g, 0, 0)),
                pl.BlockSpec((1, tokens, width), lambda g, c: (g, 0, 0)),
                pl.BlockSpec((1, tokens, width), lambda g, c: (g, 0, 1)),
            ],
            out_specs=pl.BlockSpec((1, latents, width), lambda g, c: (g, 0, 0)),
        ),
        out_shape=jax.ShapeDtypeStruct((groups, latents, width), jnp.bfloat16),
    )(counts, queries, key_value, key_value)


def per_device(
    state,
    unit_slot,
    token_count,
    session,
    session_row,
    unit_count,
    panels,
    memory_key,
    memory_value,
    q1_weight,
    o1_weight,
    kv_weight,
    q2_weight,
    o2_weight,
):
    local_samples, latents, model_width = state.shape
    token_total = unit_slot.shape[1]
    owners = lax.axis_size("smp")
    sess_dev, unit_total = (panels.shape[0], panels.shape[1])
    head_count = model_width // HEAD_DIM
    session_ids = jnp.arange(session_row.shape[0], dtype=jnp.int32)
    panel_row = jnp.sum(
        jnp.where(session[:, None] == session_ids[None, :], session_row[None, :], 0), axis=1
    )
    unit_limit = jnp.sum(
        jnp.where(panel_row[:, None] == session_ids[None, :], unit_count[None, :], 0), axis=1
    )
    owner_rank = panel_row // sess_dev
    token_index = (panel_row % sess_dev * unit_total)[:, None] + unit_slot % unit_limit[:, None]
    slot_pick = owner_rank[None, :] == jnp.arange(owners, dtype=jnp.int32)[:, None]
    request = jnp.sum(jnp.where(slot_pick[:, :, None], token_index[None, :, :], 0), axis=1)
    count_pick = jnp.sum(jnp.where(slot_pick, token_count[None, :], 0), axis=1)
    sample_pick = jnp.sum(
        jnp.where(slot_pick, jnp.arange(local_samples, dtype=jnp.int32)[None, :], 0), axis=1
    )
    served = lax.all_to_all(
        jnp.concatenate([request, count_pick[:, None]], axis=1),
        "smp",
        split_axis=0,
        concat_axis=0,
        tiled=True,
    )
    served_index = served[:, :token_total]
    panel_table = panels.reshape(sess_dev * unit_total, model_width)
    served_embed = panel_table[served_index.reshape(-1)]
    row_total = local_samples * latents
    flat_state = state.reshape(row_total, model_width)
    queries = jnp.dot(normed(flat_state), q1_weight, preferred_element_type=jnp.float32).astype(
        jnp.bfloat16
    )
    memory_pair = jnp.concatenate([memory_key, memory_value], axis=1)
    memory_rows = lax.all_to_all(
        jnp.broadcast_to(memory_pair[None], (owners,) + memory_pair.shape),
        "smp",
        split_axis=0,
        concat_axis=0,
        tiled=True,
    ).reshape(1, -1, 2 * model_width)
    memory_total = memory_rows.shape[1]
    read_mem = attend_kernel(
        queries.reshape(1, row_total, model_width),
        memory_rows,
        jnp.full((1,), memory_total, jnp.int32),
    ).reshape(row_total, model_width)
    hidden = (
        flat_state.astype(jnp.float32)
        + jnp.dot(read_mem, o1_weight, preferred_element_type=jnp.float32)
    ).astype(jnp.bfloat16)
    queries2 = jnp.dot(normed(hidden), q2_weight, preferred_element_type=jnp.float32).astype(
        jnp.bfloat16
    )
    queries2 = queries2.reshape(local_samples, latents, model_width)
    served_queries = lax.all_to_all(
        queries2[sample_pick], "smp", split_axis=0, concat_axis=0, tiled=True
    )
    key_value = jnp.dot(
        normed(served_embed),
        kv_weight,
        preferred_element_type=jnp.float32,
    ).astype(jnp.bfloat16)
    key_value = key_value.reshape(owners, token_total, 2 * model_width)
    key_rows = key_value[:, :, :model_width].reshape(owners, token_total, head_count, HEAD_DIM)
    value_rows = key_value[:, :, model_width:].reshape(owners, token_total, head_count, HEAD_DIM)
    live_tokens = jnp.arange(token_total, dtype=jnp.int32)[None, :] < served[:, token_total:]
    served_read = attend(
        served_queries.reshape(owners, latents, head_count, HEAD_DIM),
        key_rows,
        value_rows,
        live_tokens,
    )
    read_spike = lax.all_to_all(
        served_read.reshape(owners, latents, model_width),
        "smp",
        split_axis=0,
        concat_axis=0,
        tiled=True,
    )[owner_rank]
    result = hidden.astype(jnp.float32) + jnp.dot(
        read_spike.reshape(row_total, model_width), o2_weight, preferred_element_type=jnp.float32
    )
    return result.astype(jnp.bfloat16).reshape(local_samples, latents, model_width)


def solution(mesh):
    in_specs = (
        P(("grp", "smp"), None, None),
        P(("grp", "smp"), None),
        P(("grp", "smp")),
        P(("grp", "smp")),
        P("grp"),
        P(),
        P("smp", None, None),
        P(("grp", "smp"), None),
        P(("grp", "smp"), None),
        P(),
        P(),
        P(),
        P(),
        P(),
    )
    out_specs = P(("grp", "smp"), None, None)
    return jax.shard_map(
        per_device, mesh=mesh, in_specs=in_specs, out_specs=out_specs, check_vma=False
    )
```

```python
import jax
import jax.numpy as jnp
from jax import lax
from jax.experimental import pallas as pl
from jax.experimental.pallas import tpu as pltpu
from jax.sharding import PartitionSpec as P

HEAD_DIM = 64


masked_score = -1e30


def normed(values):
    wide = values.astype(jnp.float32)
    return (wide * lax.rsqrt(jnp.mean(wide * wide, axis=-1, keepdims=True) + 1e-05)).astype(
        jnp.bfloat16
    )


def attend(queries, key_rows, value_rows, live_tokens):
    samples, latents, head_count, head_size = queries.shape
    spike_scores = jnp.einsum(
        "blhd,bkhd->bhlk", queries, key_rows, preferred_element_type=jnp.float32
    ) * HEAD_DIM ** (-0.5)
    spike_scores = jnp.where(live_tokens[:, None, None, :], spike_scores, masked_score)
    spike_max = jnp.max(spike_scores, axis=-1, keepdims=True)
    spike_exp = jnp.exp(spike_scores - spike_max)
    denominator = jnp.transpose(jnp.sum(spike_exp, axis=-1, keepdims=True), (0, 2, 1, 3))
    spike_mix = (
        jnp.einsum(
            "bhlk,bkhd->blhd",
            spike_exp.astype(jnp.bfloat16),
            value_rows,
            preferred_element_type=jnp.float32,
        )
        / denominator
    )
    return spike_mix.reshape(samples, latents, head_count * head_size).astype(jnp.bfloat16)


def attend_block(counts_ref, query_ref, key_ref, value_ref, out_ref):
    group = pl.program_id(0)
    latents = query_ref.shape[1]
    tokens = key_ref.shape[1]
    live = lax.broadcasted_iota(jnp.int32, (latents, tokens), 1) < counts_ref[group]
    first_head = lax.broadcasted_iota(jnp.int32, (1, 2 * HEAD_DIM), 1) < HEAD_DIM
    for pair in range(query_ref.shape[2] // (2 * HEAD_DIM)):
        cols = pl.ds(pair * 2 * HEAD_DIM, 2 * HEAD_DIM)
        query = query_ref[0, :, cols]
        key = key_ref[0, :, cols]
        value = value_ref[0, :, cols]
        mixes = []
        for half in (first_head, jnp.logical_not(first_head)):
            scores = lax.dot_general(
                jnp.where(half, query, jnp.zeros_like(query)),
                key,
                (((1,), (1,)), ((), ())),
                preferred_element_type=jnp.float32,
            ) * HEAD_DIM ** (-0.5)
            scores = jnp.where(live, scores, masked_score)
            row_max = jnp.max(scores, axis=1, keepdims=True)
            exponent = jnp.exp(scores - row_max)
            denominator = jnp.sum(exponent, axis=1, keepdims=True)
            mix = jnp.dot(
                exponent.astype(jnp.bfloat16), value, preferred_element_type=jnp.float32
            )
            mixes.append(mix / denominator)
        out_ref[0, :, cols] = jnp.where(first_head, mixes[0], mixes[1]).astype(jnp.bfloat16)


def attend_kernel(queries, key_value, counts):
    groups, latents, width = queries.shape
    tokens = key_value.shape[1]
    return pl.pallas_call(
        attend_block,
        grid_spec=pltpu.PrefetchScalarGridSpec(
            num_scalar_prefetch=1,
            grid=(groups,),
            in_specs=[
                pl.BlockSpec((1, latents, width), lambda g, c: (g, 0, 0)),
                pl.BlockSpec((1, tokens, width), lambda g, c: (g, 0, 0)),
                pl.BlockSpec((1, tokens, width), lambda g, c: (g, 0, 1)),
            ],
            out_specs=pl.BlockSpec((1, latents, width), lambda g, c: (g, 0, 0)),
        ),
        out_shape=jax.ShapeDtypeStruct((groups, latents, width), jnp.bfloat16),
    )(counts, queries, key_value, key_value)


def per_device(
    state,
    unit_slot,
    token_count,
    session,
    session_row,
    unit_count,
    panels,
    memory_key,
    memory_value,
    q1_weight,
    o1_weight,
    kv_weight,
    q2_weight,
    o2_weight,
):
    local_samples, latents, model_width = state.shape
    token_total = unit_slot.shape[1]
    owners = lax.axis_size("smp")
    sess_dev, unit_total = (panels.shape[0], panels.shape[1])
    head_count = model_width // HEAD_DIM
    session_ids = jnp.arange(session_row.shape[0], dtype=jnp.int32)
    panel_row = jnp.sum(
        jnp.where(session[:, None] == session_ids[None, :], session_row[None, :], 0), axis=1
    )
    unit_limit = jnp.sum(
        jnp.where(panel_row[:, None] == session_ids[None, :], unit_count[None, :], 0), axis=1
    )
    owner_rank = panel_row // sess_dev
    token_index = (panel_row % sess_dev * unit_total)[:, None] + unit_slot % unit_limit[:, None]
    slot_pick = owner_rank[None, :] == jnp.arange(owners, dtype=jnp.int32)[:, None]
    request = jnp.sum(jnp.where(slot_pick[:, :, None], token_index[None, :, :], 0), axis=1)
    count_pick = jnp.sum(jnp.where(slot_pick, token_count[None, :], 0), axis=1)
    sample_pick = jnp.sum(
        jnp.where(slot_pick, jnp.arange(local_samples, dtype=jnp.int32)[None, :], 0), axis=1
    )
    served = lax.all_to_all(
        jnp.concatenate([request, count_pick[:, None]], axis=1),
        "smp",
        split_axis=0,
        concat_axis=0,
        tiled=True,
    )
    served_index = served[:, :token_total]
    panel_table = panels.reshape(sess_dev * unit_total, model_width)
    served_embed = panel_table[served_index.reshape(-1)]
    row_total = local_samples * latents
    flat_state = state.reshape(row_total, model_width)
    queries = jnp.dot(normed(flat_state), q1_weight, preferred_element_type=jnp.float32).astype(
        jnp.bfloat16
    )
    memory_pair = jnp.concatenate([memory_key, memory_value], axis=1)
    memory_rows = lax.all_to_all(
        jnp.broadcast_to(memory_pair[None], (owners,) + memory_pair.shape),
        "smp",
        split_axis=0,
        concat_axis=0,
        tiled=True,
    ).reshape(1, -1, 2 * model_width)
    key_value = jnp.dot(
        normed(served_embed),
        kv_weight,
        preferred_element_type=jnp.float32,
    ).astype(jnp.bfloat16)
    key_value = key_value.reshape(owners, token_total, 2 * model_width)
    key_rows = key_value[:, :, :model_width].reshape(owners, token_total, head_count, HEAD_DIM)
    value_rows = key_value[:, :, model_width:].reshape(owners, token_total, head_count, HEAD_DIM)
    live_tokens = jnp.arange(token_total, dtype=jnp.int32)[None, :] < served[:, token_total:]
    key_rows, value_rows, live_tokens, memory_rows = lax.optimization_barrier(
        (key_rows, value_rows, live_tokens, memory_rows)
    )
    memory_total = memory_rows.shape[1]
    read_mem = attend_kernel(
        queries.reshape(1, row_total, model_width),
        memory_rows,
        jnp.full((1,), memory_total, jnp.int32),
    ).reshape(row_total, model_width)
    hidden = (
        flat_state.astype(jnp.float32)
        + jnp.dot(read_mem, o1_weight, preferred_element_type=jnp.float32)
    ).astype(jnp.bfloat16)
    queries2 = jnp.dot(normed(hidden), q2_weight, preferred_element_type=jnp.float32).astype(
        jnp.bfloat16
    )
    queries2 = queries2.reshape(local_samples, latents, model_width)
    served_queries = lax.all_to_all(
        queries2[sample_pick], "smp", split_axis=0, concat_axis=0, tiled=True
    )
    served_read = attend(
        served_queries.reshape(owners, latents, head_count, HEAD_DIM),
        key_rows,
        value_rows,
        live_tokens,
    )
    read_spike = lax.all_to_all(
        served_read.reshape(owners, latents, model_width),
        "smp",
        split_axis=0,
        concat_axis=0,
        tiled=True,
    )[owner_rank]
    result = hidden.astype(jnp.float32) + jnp.dot(
        read_spike.reshape(row_total, model_width), o2_weight, preferred_element_type=jnp.float32
    )
    return result.astype(jnp.bfloat16).reshape(local_samples, latents, model_width)


def solution(mesh):
    in_specs = (
        P(("grp", "smp"), None, None),
        P(("grp", "smp"), None),
        P(("grp", "smp")),
        P(("grp", "smp")),
        P("grp"),
        P(),
        P("smp", None, None),
        P(("grp", "smp"), None),
        P(("grp", "smp"), None),
        P(),
        P(),
        P(),
        P(),
        P(),
    )
    out_specs = P(("grp", "smp"), None, None)
    return jax.shard_map(
        per_device, mesh=mesh, in_specs=in_specs, out_specs=out_specs, check_vma=False
    )
```

```python
import jax
import jax.numpy as jnp
from jax import lax
from jax.experimental import pallas as pl
from jax.experimental.pallas import tpu as pltpu
from jax.sharding import PartitionSpec as P

HEAD_DIM = 64


masked_score = -1e30


def normed(values):
    wide = values.astype(jnp.float32)
    return (wide * lax.rsqrt(jnp.mean(wide * wide, axis=-1, keepdims=True) + 1e-05)).astype(
        jnp.bfloat16
    )


def attend(queries, key_rows, value_rows, live_tokens):
    samples, latents, head_count, head_size = queries.shape
    spike_scores = jnp.einsum(
        "blhd,bkhd->bhlk", queries, key_rows, preferred_element_type=jnp.float32
    ) * HEAD_DIM ** (-0.5)
    spike_scores = jnp.where(live_tokens[:, None, None, :], spike_scores, masked_score)
    spike_max = jnp.max(spike_scores, axis=-1, keepdims=True)
    spike_exp = jnp.exp(spike_scores - spike_max)
    denominator = jnp.transpose(jnp.sum(spike_exp, axis=-1, keepdims=True), (0, 2, 1, 3))
    spike_mix = (
        jnp.einsum(
            "bhlk,bkhd->blhd",
            spike_exp.astype(jnp.bfloat16),
            value_rows,
            preferred_element_type=jnp.float32,
        )
        / denominator
    )
    return spike_mix.reshape(samples, latents, head_count * head_size).astype(jnp.bfloat16)


def attend_heads(queries, key_rows, value_rows, live_tokens):
    samples, latents, head_count, head_size = queries.shape
    spike_scores = jnp.einsum(
        "blhd,bhkd->bhlk", queries, key_rows, preferred_element_type=jnp.float32
    ) * HEAD_DIM ** (-0.5)
    spike_scores = jnp.where(live_tokens[:, None, None, :], spike_scores, masked_score)
    spike_max = jnp.max(spike_scores, axis=-1, keepdims=True)
    spike_exp = jnp.exp(spike_scores - spike_max)
    denominator = jnp.transpose(jnp.sum(spike_exp, axis=-1, keepdims=True), (0, 2, 1, 3))
    spike_mix = (
        jnp.einsum(
            "bhlk,bhkd->blhd",
            spike_exp.astype(jnp.bfloat16),
            value_rows,
            preferred_element_type=jnp.float32,
        )
        / denominator
    )
    return spike_mix.reshape(samples, latents, head_count * head_size).astype(jnp.bfloat16)


def attend_block(counts_ref, query_ref, key_ref, value_ref, out_ref):
    group = pl.program_id(0)
    latents = query_ref.shape[1]
    tokens = key_ref.shape[1]
    live = lax.broadcasted_iota(jnp.int32, (latents, tokens), 1) < counts_ref[group]
    first_head = lax.broadcasted_iota(jnp.int32, (1, 2 * HEAD_DIM), 1) < HEAD_DIM
    for pair in range(query_ref.shape[2] // (2 * HEAD_DIM)):
        cols = pl.ds(pair * 2 * HEAD_DIM, 2 * HEAD_DIM)
        query = query_ref[0, :, cols]
        key = key_ref[0, :, cols]
        value = value_ref[0, :, cols]
        mixes = []
        for half in (first_head, jnp.logical_not(first_head)):
            scores = lax.dot_general(
                jnp.where(half, query, jnp.zeros_like(query)),
                key,
                (((1,), (1,)), ((), ())),
                preferred_element_type=jnp.float32,
            ) * HEAD_DIM ** (-0.5)
            scores = jnp.where(live, scores, masked_score)
            row_max = jnp.max(scores, axis=1, keepdims=True)
            exponent = jnp.exp(scores - row_max)
            denominator = jnp.sum(exponent, axis=1, keepdims=True)
            mix = jnp.dot(
                exponent.astype(jnp.bfloat16), value, preferred_element_type=jnp.float32
            )
            mixes.append(mix / denominator)
        out_ref[0, :, cols] = jnp.where(first_head, mixes[0], mixes[1]).astype(jnp.bfloat16)


def attend_kernel(queries, key_value, counts):
    groups, latents, width = queries.shape
    tokens = key_value.shape[1]
    return pl.pallas_call(
        attend_block,
        grid_spec=pltpu.PrefetchScalarGridSpec(
            num_scalar_prefetch=1,
            grid=(groups,),
            in_specs=[
                pl.BlockSpec((1, latents, width), lambda g, c: (g, 0, 0)),
                pl.BlockSpec((1, tokens, width), lambda g, c: (g, 0, 0)),
                pl.BlockSpec((1, tokens, width), lambda g, c: (g, 0, 1)),
            ],
            out_specs=pl.BlockSpec((1, latents, width), lambda g, c: (g, 0, 0)),
        ),
        out_shape=jax.ShapeDtypeStruct((groups, latents, width), jnp.bfloat16),
    )(counts, queries, key_value, key_value)


def per_device(
    state,
    unit_slot,
    token_count,
    session,
    session_row,
    unit_count,
    panels,
    memory_key,
    memory_value,
    q1_weight,
    o1_weight,
    kv_weight,
    q2_weight,
    o2_weight,
):
    local_samples, latents, model_width = state.shape
    token_total = unit_slot.shape[1]
    owners = lax.axis_size("smp")
    sess_dev, unit_total = (panels.shape[0], panels.shape[1])
    head_count = model_width // HEAD_DIM
    session_ids = jnp.arange(session_row.shape[0], dtype=jnp.int32)
    panel_row = jnp.sum(
        jnp.where(session[:, None] == session_ids[None, :], session_row[None, :], 0), axis=1
    )
    unit_limit = jnp.sum(
        jnp.where(panel_row[:, None] == session_ids[None, :], unit_count[None, :], 0), axis=1
    )
    owner_rank = panel_row // sess_dev
    token_index = (panel_row % sess_dev * unit_total)[:, None] + unit_slot % unit_limit[:, None]
    slot_pick = owner_rank[None, :] == jnp.arange(owners, dtype=jnp.int32)[:, None]
    request = jnp.sum(jnp.where(slot_pick[:, :, None], token_index[None, :, :], 0), axis=1)
    count_pick = jnp.sum(jnp.where(slot_pick, token_count[None, :], 0), axis=1)
    sample_pick = jnp.sum(
        jnp.where(slot_pick, jnp.arange(local_samples, dtype=jnp.int32)[None, :], 0), axis=1
    )
    served = lax.all_to_all(
        jnp.concatenate([request, count_pick[:, None]], axis=1),
        "smp",
        split_axis=0,
        concat_axis=0,
        tiled=True,
    )
    served_index = served[:, :token_total]
    panel_table = panels.reshape(sess_dev * unit_total, model_width)
    served_embed = panel_table[served_index.reshape(-1)]
    row_total = local_samples * latents
    flat_state = state.reshape(row_total, model_width)
    queries = jnp.dot(normed(flat_state), q1_weight, preferred_element_type=jnp.float32).astype(
        jnp.bfloat16
    )
    memory_pair = jnp.concatenate([memory_key, memory_value], axis=1)
    memory_rows = lax.all_to_all(
        jnp.broadcast_to(memory_pair[None], (owners,) + memory_pair.shape),
        "smp",
        split_axis=0,
        concat_axis=0,
        tiled=True,
    ).reshape(1, -1, 2 * model_width)
    embed_normed = normed(served_embed).reshape(owners, token_total, model_width)
    embed_normed, memory_rows = lax.optimization_barrier((embed_normed, memory_rows))
    memory_total = memory_rows.shape[1]
    read_mem = attend_kernel(
        queries.reshape(1, row_total, model_width),
        memory_rows,
        jnp.full((1,), memory_total, jnp.int32),
    ).reshape(row_total, model_width)
    hidden = (
        flat_state.astype(jnp.float32)
        + jnp.dot(read_mem, o1_weight, preferred_element_type=jnp.float32)
    ).astype(jnp.bfloat16)
    queries2 = jnp.dot(normed(hidden), q2_weight, preferred_element_type=jnp.float32).astype(
        jnp.bfloat16
    )
    queries2 = queries2.reshape(local_samples, latents, model_width)
    served_queries = lax.all_to_all(
        queries2[sample_pick], "smp", split_axis=0, concat_axis=0, tiled=True
    )
    key_rows = jnp.einsum(
        "btc,chd->bhtd",
        embed_normed,
        kv_weight[:, :model_width].reshape(model_width, head_count, HEAD_DIM),
        preferred_element_type=jnp.float32,
    ).astype(jnp.bfloat16)
    value_rows = jnp.einsum(
        "btc,chd->bhtd",
        embed_normed,
        kv_weight[:, model_width:].reshape(model_width, head_count, HEAD_DIM),
        preferred_element_type=jnp.float32,
    ).astype(jnp.bfloat16)
    key_rows, value_rows = lax.optimization_barrier((key_rows, value_rows))
    live_tokens = jnp.arange(token_total, dtype=jnp.int32)[None, :] < served[:, token_total:]
    served_read = attend_heads(
        served_queries.reshape(owners, latents, head_count, HEAD_DIM),
        key_rows,
        value_rows,
        live_tokens,
    )
    read_spike = lax.all_to_all(
        served_read.reshape(owners, latents, model_width),
        "smp",
        split_axis=0,
        concat_axis=0,
        tiled=True,
    )[owner_rank]
    result = hidden.astype(jnp.float32) + jnp.dot(
        read_spike.reshape(row_total, model_width), o2_weight, preferred_element_type=jnp.float32
    )
    return result.astype(jnp.bfloat16).reshape(local_samples, latents, model_width)


def solution(mesh):
    in_specs = (
        P(("grp", "smp"), None, None),
        P(("grp", "smp"), None),
        P(("grp", "smp")),
        P(("grp", "smp")),
        P("grp"),
        P(),
        P("smp", None, None),
        P(("grp", "smp"), None),
        P(("grp", "smp"), None),
        P(),
        P(),
        P(),
        P(),
        P(),
    )
    out_specs = P(("grp", "smp"), None, None)
    return jax.shard_map(
        per_device, mesh=mesh, in_specs=in_specs, out_specs=out_specs, check_vma=False
    )
```

```python
import jax
import jax.numpy as jnp
from jax import lax
from jax.experimental import pallas as pl
from jax.experimental.pallas import tpu as pltpu
from jax.sharding import PartitionSpec as P

HEAD_DIM = 64


masked_score = -1e30


def normed(values):
    wide = values.astype(jnp.float32)
    return (wide * lax.rsqrt(jnp.mean(wide * wide, axis=-1, keepdims=True) + 1e-05)).astype(
        jnp.bfloat16
    )


def attend(queries, key_rows, value_rows, live_tokens):
    samples, latents, head_count, head_size = queries.shape
    spike_scores = jnp.einsum(
        "blhd,bkhd->bhlk", queries, key_rows, preferred_element_type=jnp.float32
    ) * HEAD_DIM ** (-0.5)
    spike_scores = jnp.where(live_tokens[:, None, None, :], spike_scores, masked_score)
    spike_max = jnp.max(spike_scores, axis=-1, keepdims=True)
    spike_exp = jnp.exp(spike_scores - spike_max)
    denominator = jnp.transpose(jnp.sum(spike_exp, axis=-1, keepdims=True), (0, 2, 1, 3))
    spike_mix = (
        jnp.einsum(
            "bhlk,bkhd->blhd",
            spike_exp.astype(jnp.bfloat16),
            value_rows,
            preferred_element_type=jnp.float32,
        )
        / denominator
    )
    return spike_mix.reshape(samples, latents, head_count * head_size).astype(jnp.bfloat16)


def attend_heads(queries, key_rows, value_rows, live_tokens):
    samples, latents, head_count, head_size = queries.shape
    spike_scores = jnp.einsum(
        "blhd,bhkd->bhlk", queries, key_rows, preferred_element_type=jnp.float32
    ) * HEAD_DIM ** (-0.5)
    spike_scores = jnp.where(live_tokens[:, None, None, :], spike_scores, masked_score)
    spike_max = jnp.max(spike_scores, axis=-1, keepdims=True)
    spike_exp = jnp.exp(spike_scores - spike_max)
    denominator = jnp.transpose(jnp.sum(spike_exp, axis=-1, keepdims=True), (0, 2, 1, 3))
    spike_mix = (
        jnp.einsum(
            "bhlk,bhkd->blhd",
            spike_exp.astype(jnp.bfloat16),
            value_rows,
            preferred_element_type=jnp.float32,
        )
        / denominator
    )
    return spike_mix.reshape(samples, latents, head_count * head_size).astype(jnp.bfloat16)


def attend_block(counts_ref, query_ref, key_ref, value_ref, out_ref):
    group = pl.program_id(0)
    latents = query_ref.shape[1]
    tokens = key_ref.shape[1]
    live = lax.broadcasted_iota(jnp.int32, (latents, tokens), 1) < counts_ref[group]
    first_head = lax.broadcasted_iota(jnp.int32, (1, 2 * HEAD_DIM), 1) < HEAD_DIM
    for pair in range(query_ref.shape[2] // (2 * HEAD_DIM)):
        cols = pl.ds(pair * 2 * HEAD_DIM, 2 * HEAD_DIM)
        query = query_ref[0, :, cols]
        key = key_ref[0, :, cols]
        value = value_ref[0, :, cols]
        mixes = []
        for half in (first_head, jnp.logical_not(first_head)):
            scores = lax.dot_general(
                jnp.where(half, query, jnp.zeros_like(query)),
                key,
                (((1,), (1,)), ((), ())),
                preferred_element_type=jnp.float32,
            ) * HEAD_DIM ** (-0.5)
            scores = jnp.where(live, scores, masked_score)
            row_max = jnp.max(scores, axis=1, keepdims=True)
            exponent = jnp.exp(scores - row_max)
            denominator = jnp.sum(exponent, axis=1, keepdims=True)
            mix = jnp.dot(
                exponent.astype(jnp.bfloat16), value, preferred_element_type=jnp.float32
            )
            mixes.append(mix / denominator)
        out_ref[0, :, cols] = jnp.where(first_head, mixes[0], mixes[1]).astype(jnp.bfloat16)


def attend_kernel(queries, key_value, counts):
    groups, latents, width = queries.shape
    tokens = key_value.shape[1]
    return pl.pallas_call(
        attend_block,
        grid_spec=pltpu.PrefetchScalarGridSpec(
            num_scalar_prefetch=1,
            grid=(groups,),
            in_specs=[
                pl.BlockSpec((1, latents, width), lambda g, c: (g, 0, 0)),
                pl.BlockSpec((1, tokens, width), lambda g, c: (g, 0, 0)),
                pl.BlockSpec((1, tokens, width), lambda g, c: (g, 0, 1)),
            ],
            out_specs=pl.BlockSpec((1, latents, width), lambda g, c: (g, 0, 0)),
        ),
        out_shape=jax.ShapeDtypeStruct((groups, latents, width), jnp.bfloat16),
    )(counts, queries, key_value, key_value)


def per_device(
    state,
    unit_slot,
    token_count,
    session,
    session_row,
    unit_count,
    panels,
    memory_key,
    memory_value,
    q1_weight,
    o1_weight,
    kv_weight,
    q2_weight,
    o2_weight,
):
    local_samples, latents, model_width = state.shape
    token_total = unit_slot.shape[1]
    owners = lax.axis_size("smp")
    sess_dev, unit_total = (panels.shape[0], panels.shape[1])
    head_count = model_width // HEAD_DIM
    session_ids = jnp.arange(session_row.shape[0], dtype=jnp.int32)
    panel_row = jnp.sum(
        jnp.where(session[:, None] == session_ids[None, :], session_row[None, :], 0), axis=1
    )
    unit_limit = jnp.sum(
        jnp.where(panel_row[:, None] == session_ids[None, :], unit_count[None, :], 0), axis=1
    )
    owner_rank = panel_row // sess_dev
    token_index = (panel_row % sess_dev * unit_total)[:, None] + unit_slot % unit_limit[:, None]
    slot_pick = owner_rank[None, :] == jnp.arange(owners, dtype=jnp.int32)[:, None]
    request = jnp.sum(jnp.where(slot_pick[:, :, None], token_index[None, :, :], 0), axis=1)
    count_pick = jnp.sum(jnp.where(slot_pick, token_count[None, :], 0), axis=1)
    sample_pick = jnp.sum(
        jnp.where(slot_pick, jnp.arange(local_samples, dtype=jnp.int32)[None, :], 0), axis=1
    )
    served = lax.all_to_all(
        jnp.concatenate([request, count_pick[:, None]], axis=1),
        "smp",
        split_axis=0,
        concat_axis=0,
        tiled=True,
    )
    served_index = served[:, :token_total]
    panel_table = panels.reshape(sess_dev * unit_total, model_width)
    served_embed = panel_table[served_index.reshape(-1)]
    row_total = local_samples * latents
    flat_state = state.reshape(row_total, model_width)
    queries = jnp.dot(normed(flat_state), q1_weight, preferred_element_type=jnp.float32).astype(
        jnp.bfloat16
    )
    memory_pair = jnp.concatenate([memory_key, memory_value], axis=1)
    memory_rows = lax.all_to_all(
        jnp.broadcast_to(memory_pair[None], (owners,) + memory_pair.shape),
        "smp",
        split_axis=0,
        concat_axis=0,
        tiled=True,
    ).reshape(1, -1, 2 * model_width)
    embed_normed = normed(served_embed).reshape(owners, token_total, model_width)
    embed_normed, memory_rows = lax.optimization_barrier((embed_normed, memory_rows))
    memory_total = memory_rows.shape[1]
    read_mem = attend_kernel(
        queries.reshape(1, row_total, model_width),
        memory_rows,
        jnp.full((1,), memory_total, jnp.int32),
    ).reshape(row_total, model_width)
    hidden = (
        flat_state.astype(jnp.float32)
        + jnp.dot(read_mem, o1_weight, preferred_element_type=jnp.float32)
    ).astype(jnp.bfloat16)
    queries2 = jnp.dot(normed(hidden), q2_weight, preferred_element_type=jnp.float32).astype(
        jnp.bfloat16
    )
    queries2 = queries2.reshape(local_samples, latents, model_width)
    served_queries = lax.all_to_all(
        queries2[sample_pick], "smp", split_axis=0, concat_axis=0, tiled=True
    )
    key_value = jnp.einsum(
        "btc,cjhd->jbhtd",
        embed_normed,
        kv_weight.reshape(model_width, 2, head_count, HEAD_DIM),
        preferred_element_type=jnp.float32,
    ).astype(jnp.bfloat16)
    key_rows, value_rows = key_value[0], key_value[1]
    key_rows, value_rows = lax.optimization_barrier((key_rows, value_rows))
    live_tokens = jnp.arange(token_total, dtype=jnp.int32)[None, :] < served[:, token_total:]
    served_read = attend_heads(
        served_queries.reshape(owners, latents, head_count, HEAD_DIM),
        key_rows,
        value_rows,
        live_tokens,
    )
    read_spike = lax.all_to_all(
        served_read.reshape(owners, latents, model_width),
        "smp",
        split_axis=0,
        concat_axis=0,
        tiled=True,
    )[owner_rank]
    result = hidden.astype(jnp.float32) + jnp.dot(
        read_spike.reshape(row_total, model_width), o2_weight, preferred_element_type=jnp.float32
    )
    return result.astype(jnp.bfloat16).reshape(local_samples, latents, model_width)


def solution(mesh):
    in_specs = (
        P(("grp", "smp"), None, None),
        P(("grp", "smp"), None),
        P(("grp", "smp")),
        P(("grp", "smp")),
        P("grp"),
        P(),
        P("smp", None, None),
        P(("grp", "smp"), None),
        P(("grp", "smp"), None),
        P(),
        P(),
        P(),
        P(),
        P(),
    )
    out_specs = P(("grp", "smp"), None, None)
    return jax.shard_map(
        per_device, mesh=mesh, in_specs=in_specs, out_specs=out_specs, check_vma=False
    )
```

```python
import jax
import jax.numpy as jnp
from jax import lax
from jax.experimental import pallas as pl
from jax.experimental.pallas import tpu as pltpu
from jax.sharding import PartitionSpec as P

HEAD_DIM = 64


masked_score = -1e30


def normed(values):
    wide = values.astype(jnp.float32)
    return (wide * lax.rsqrt(jnp.mean(wide * wide, axis=-1, keepdims=True) + 1e-05)).astype(
        jnp.bfloat16
    )


def attend(queries, key_rows, value_rows, live_tokens):
    samples, latents, head_count, head_size = queries.shape
    spike_scores = jnp.einsum(
        "blhd,bkhd->bhlk", queries, key_rows, preferred_element_type=jnp.float32
    ) * HEAD_DIM ** (-0.5)
    spike_scores = jnp.where(live_tokens[:, None, None, :], spike_scores, masked_score)
    spike_max = jnp.max(spike_scores, axis=-1, keepdims=True)
    spike_exp = jnp.exp(spike_scores - spike_max)
    denominator = jnp.transpose(jnp.sum(spike_exp, axis=-1, keepdims=True), (0, 2, 1, 3))
    spike_mix = (
        jnp.einsum(
            "bhlk,bkhd->blhd",
            spike_exp.astype(jnp.bfloat16),
            value_rows,
            preferred_element_type=jnp.float32,
        )
        / denominator
    )
    return spike_mix.reshape(samples, latents, head_count * head_size).astype(jnp.bfloat16)


def attend_heads(queries, key_rows, value_rows, live_tokens):
    samples, latents, head_count, head_size = queries.shape
    spike_scores = jnp.einsum(
        "blhd,bhkd->bhlk", queries, key_rows, preferred_element_type=jnp.float32
    ) * HEAD_DIM ** (-0.5)
    spike_scores = jnp.where(live_tokens[:, None, None, :], spike_scores, masked_score)
    spike_max = jnp.max(spike_scores, axis=-1, keepdims=True)
    spike_exp = jnp.exp(spike_scores - spike_max)
    denominator = jnp.transpose(jnp.sum(spike_exp, axis=-1, keepdims=True), (0, 2, 1, 3))
    spike_mix = (
        jnp.einsum(
            "bhlk,bhkd->blhd",
            spike_exp.astype(jnp.bfloat16),
            value_rows,
            preferred_element_type=jnp.float32,
        )
        / denominator
    )
    return spike_mix.reshape(samples, latents, head_count * head_size).astype(jnp.bfloat16)


def attend_block(counts_ref, query_ref, key_ref, value_ref, out_ref):
    group = pl.program_id(0)
    latents = query_ref.shape[1]
    tokens = key_ref.shape[1]
    live = lax.broadcasted_iota(jnp.int32, (latents, tokens), 1) < counts_ref[group]
    first_head = lax.broadcasted_iota(jnp.int32, (1, 2 * HEAD_DIM), 1) < HEAD_DIM
    for pair in range(query_ref.shape[2] // (2 * HEAD_DIM)):
        cols = pl.ds(pair * 2 * HEAD_DIM, 2 * HEAD_DIM)
        query = query_ref[0, :, cols]
        key = key_ref[0, :, cols]
        value = value_ref[0, :, cols]
        mixes = []
        for half in (first_head, jnp.logical_not(first_head)):
            scores = lax.dot_general(
                jnp.where(half, query, jnp.zeros_like(query)),
                key,
                (((1,), (1,)), ((), ())),
                preferred_element_type=jnp.float32,
            ) * HEAD_DIM ** (-0.5)
            scores = jnp.where(live, scores, masked_score)
            row_max = jnp.max(scores, axis=1, keepdims=True)
            exponent = jnp.exp(scores - row_max)
            denominator = jnp.sum(exponent, axis=1, keepdims=True)
            mix = jnp.dot(
                exponent.astype(jnp.bfloat16), value, preferred_element_type=jnp.float32
            )
            mixes.append(mix / denominator)
        out_ref[0, :, cols] = jnp.where(first_head, mixes[0], mixes[1]).astype(jnp.bfloat16)


def attend_kernel(queries, key_value, counts):
    groups, latents, width = queries.shape
    tokens = key_value.shape[1]
    return pl.pallas_call(
        attend_block,
        grid_spec=pltpu.PrefetchScalarGridSpec(
            num_scalar_prefetch=1,
            grid=(groups,),
            in_specs=[
                pl.BlockSpec((1, latents, width), lambda g, c: (g, 0, 0)),
                pl.BlockSpec((1, tokens, width), lambda g, c: (g, 0, 0)),
                pl.BlockSpec((1, tokens, width), lambda g, c: (g, 0, 1)),
            ],
            out_specs=pl.BlockSpec((1, latents, width), lambda g, c: (g, 0, 0)),
        ),
        out_shape=jax.ShapeDtypeStruct((groups, latents, width), jnp.bfloat16),
    )(counts, queries, key_value, key_value)


def per_device(
    state,
    unit_slot,
    token_count,
    session,
    session_row,
    unit_count,
    panels,
    memory_key,
    memory_value,
    q1_weight,
    o1_weight,
    kv_weight,
    q2_weight,
    o2_weight,
):
    local_samples, latents, model_width = state.shape
    token_total = unit_slot.shape[1]
    owners = lax.axis_size("smp")
    sess_dev, unit_total = (panels.shape[0], panels.shape[1])
    head_count = model_width // HEAD_DIM
    session_ids = jnp.arange(session_row.shape[0], dtype=jnp.int32)
    panel_row = jnp.sum(
        jnp.where(session[:, None] == session_ids[None, :], session_row[None, :], 0), axis=1
    )
    unit_limit = jnp.sum(
        jnp.where(panel_row[:, None] == session_ids[None, :], unit_count[None, :], 0), axis=1
    )
    owner_rank = panel_row // sess_dev
    token_index = (panel_row % sess_dev * unit_total)[:, None] + unit_slot % unit_limit[:, None]
    slot_pick = owner_rank[None, :] == jnp.arange(owners, dtype=jnp.int32)[:, None]
    request = jnp.sum(jnp.where(slot_pick[:, :, None], token_index[None, :, :], 0), axis=1)
    count_pick = jnp.sum(jnp.where(slot_pick, token_count[None, :], 0), axis=1)
    sample_pick = jnp.sum(
        jnp.where(slot_pick, jnp.arange(local_samples, dtype=jnp.int32)[None, :], 0), axis=1
    )
    table = jnp.concatenate([request, count_pick[:, None]], axis=1)
    code_base = 64
    codes = jnp.concatenate([table // code_base, table % code_base], axis=1).astype(jnp.bfloat16)
    memory_pair = jnp.concatenate([memory_key, memory_value], axis=1)
    memory_count = memory_pair.shape[0]
    code_rows = jnp.zeros((owners, 8, 2 * model_width), jnp.bfloat16)
    code_rows = code_rows.at[:, 0, : codes.shape[1]].set(codes)
    arrived = lax.all_to_all(
        jnp.concatenate(
            [jnp.broadcast_to(memory_pair[None], (owners,) + memory_pair.shape), code_rows],
            axis=1,
        ),
        "smp",
        split_axis=0,
        concat_axis=0,
        tiled=True,
    )
    memory_rows = arrived[:, :memory_count].reshape(1, -1, 2 * model_width)
    code_back = arrived[:, memory_count, : codes.shape[1]].astype(jnp.int32)
    served = code_back[:, : table.shape[1]] * code_base + code_back[:, table.shape[1] :]
    served_index = served[:, :token_total]
    panel_table = panels.reshape(sess_dev * unit_total, model_width)
    served_embed = panel_table[served_index.reshape(-1)]
    row_total = local_samples * latents
    flat_state = state.reshape(row_total, model_width)
    queries = jnp.dot(normed(flat_state), q1_weight, preferred_element_type=jnp.float32).astype(
        jnp.bfloat16
    )
    embed_normed = normed(served_embed).reshape(owners, token_total, model_width)
    memory_total = memory_rows.shape[1]
    read_mem = attend_kernel(
        queries.reshape(1, row_total, model_width),
        memory_rows,
        jnp.full((1,), memory_total, jnp.int32),
    ).reshape(row_total, model_width)
    hidden = (
        flat_state.astype(jnp.float32)
        + jnp.dot(read_mem, o1_weight, preferred_element_type=jnp.float32)
    ).astype(jnp.bfloat16)
    queries2 = jnp.dot(normed(hidden), q2_weight, preferred_element_type=jnp.float32).astype(
        jnp.bfloat16
    )
    queries2 = queries2.reshape(local_samples, latents, model_width)
    served_queries = lax.all_to_all(
        queries2[sample_pick], "smp", split_axis=0, concat_axis=0, tiled=True
    )
    key_rows = jnp.einsum(
        "btc,chd->bhtd",
        embed_normed,
        kv_weight[:, :model_width].reshape(model_width, head_count, HEAD_DIM),
        preferred_element_type=jnp.float32,
    ).astype(jnp.bfloat16)
    value_rows = jnp.einsum(
        "btc,chd->bhtd",
        embed_normed,
        kv_weight[:, model_width:].reshape(model_width, head_count, HEAD_DIM),
        preferred_element_type=jnp.float32,
    ).astype(jnp.bfloat16)
    key_rows, value_rows = lax.optimization_barrier((key_rows, value_rows))
    live_tokens = jnp.arange(token_total, dtype=jnp.int32)[None, :] < served[:, token_total:]
    served_read = attend_heads(
        served_queries.reshape(owners, latents, head_count, HEAD_DIM),
        key_rows,
        value_rows,
        live_tokens,
    )
    read_spike = lax.all_to_all(
        served_read.reshape(owners, latents, model_width),
        "smp",
        split_axis=0,
        concat_axis=0,
        tiled=True,
    )[owner_rank]
    result = hidden.astype(jnp.float32) + jnp.dot(
        read_spike.reshape(row_total, model_width), o2_weight, preferred_element_type=jnp.float32
    )
    return result.astype(jnp.bfloat16).reshape(local_samples, latents, model_width)


def solution(mesh):
    in_specs = (
        P(("grp", "smp"), None, None),
        P(("grp", "smp"), None),
        P(("grp", "smp")),
        P(("grp", "smp")),
        P("grp"),
        P(),
        P("smp", None, None),
        P(("grp", "smp"), None),
        P(("grp", "smp"), None),
        P(),
        P(),
        P(),
        P(),
        P(),
    )
    out_specs = P(("grp", "smp"), None, None)
    return jax.shard_map(
        per_device, mesh=mesh, in_specs=in_specs, out_specs=out_specs, check_vma=False
    )
```

```python
import jax
import jax.numpy as jnp
from jax import lax
from jax.experimental import pallas as pl
from jax.experimental.pallas import tpu as pltpu
from jax.sharding import PartitionSpec as P

HEAD_DIM = 64


masked_score = -1e30


def normed(values):
    wide = values.astype(jnp.float32)
    return (wide * lax.rsqrt(jnp.mean(wide * wide, axis=-1, keepdims=True) + 1e-05)).astype(
        jnp.bfloat16
    )


def attend(queries, key_rows, value_rows, live_tokens):
    samples, latents, head_count, head_size = queries.shape
    spike_scores = jnp.einsum(
        "blhd,bkhd->bhlk", queries, key_rows, preferred_element_type=jnp.float32
    ) * HEAD_DIM ** (-0.5)
    spike_scores = jnp.where(live_tokens[:, None, None, :], spike_scores, masked_score)
    spike_max = jnp.max(spike_scores, axis=-1, keepdims=True)
    spike_exp = jnp.exp(spike_scores - spike_max)
    denominator = jnp.transpose(jnp.sum(spike_exp, axis=-1, keepdims=True), (0, 2, 1, 3))
    spike_mix = (
        jnp.einsum(
            "bhlk,bkhd->blhd",
            spike_exp.astype(jnp.bfloat16),
            value_rows,
            preferred_element_type=jnp.float32,
        )
        / denominator
    )
    return spike_mix.reshape(samples, latents, head_count * head_size).astype(jnp.bfloat16)


def attend_heads(queries, key_rows, value_rows, live_tokens):
    samples, latents, head_count, head_size = queries.shape
    spike_scores = jnp.einsum(
        "blhd,bhkd->bhlk", queries, key_rows, preferred_element_type=jnp.float32
    ) * HEAD_DIM ** (-0.5)
    spike_scores = jnp.where(live_tokens[:, None, None, :], spike_scores, masked_score)
    spike_max = jnp.max(spike_scores, axis=-1, keepdims=True)
    spike_exp = jnp.exp(spike_scores - spike_max)
    denominator = jnp.transpose(jnp.sum(spike_exp, axis=-1, keepdims=True), (0, 2, 1, 3))
    spike_mix = (
        jnp.einsum(
            "bhlk,bhkd->blhd",
            spike_exp.astype(jnp.bfloat16),
            value_rows,
            preferred_element_type=jnp.float32,
        )
        / denominator
    )
    return spike_mix.reshape(samples, latents, head_count * head_size).astype(jnp.bfloat16)


def exchange(blocks, axis):
    count = lax.axis_size(axis)
    rank = lax.axis_index(axis)
    pieces = [lax.dynamic_index_in_dim(blocks, rank, 0, keepdims=False)]
    for shift in range(1, count):
        outgoing = lax.dynamic_index_in_dim(blocks, (rank + shift) % count, 0, keepdims=False)
        pieces.append(
            lax.ppermute(outgoing, axis, [(i, (i + shift) % count) for i in range(count)])
        )
    stacked = jnp.stack(pieces)
    return stacked[(rank - jnp.arange(count, dtype=jnp.int32)) % count]


def attend_block(counts_ref, query_ref, key_ref, value_ref, out_ref):
    group = pl.program_id(0)
    latents = query_ref.shape[1]
    tokens = key_ref.shape[1]
    live = lax.broadcasted_iota(jnp.int32, (latents, tokens), 1) < counts_ref[group]
    first_head = lax.broadcasted_iota(jnp.int32, (1, 2 * HEAD_DIM), 1) < HEAD_DIM
    for pair in range(query_ref.shape[2] // (2 * HEAD_DIM)):
        cols = pl.ds(pair * 2 * HEAD_DIM, 2 * HEAD_DIM)
        query = query_ref[0, :, cols]
        key = key_ref[0, :, cols]
        value = value_ref[0, :, cols]
        mixes = []
        for half in (first_head, jnp.logical_not(first_head)):
            scores = lax.dot_general(
                jnp.where(half, query, jnp.zeros_like(query)),
                key,
                (((1,), (1,)), ((), ())),
                preferred_element_type=jnp.float32,
            ) * HEAD_DIM ** (-0.5)
            scores = jnp.where(live, scores, masked_score)
            row_max = jnp.max(scores, axis=1, keepdims=True)
            exponent = jnp.exp(scores - row_max)
            denominator = jnp.sum(exponent, axis=1, keepdims=True)
            mix = jnp.dot(
                exponent.astype(jnp.bfloat16), value, preferred_element_type=jnp.float32
            )
            mixes.append(mix / denominator)
        out_ref[0, :, cols] = jnp.where(first_head, mixes[0], mixes[1]).astype(jnp.bfloat16)


def attend_kernel(queries, key_value, counts):
    groups, latents, width = queries.shape
    tokens = key_value.shape[1]
    return pl.pallas_call(
        attend_block,
        grid_spec=pltpu.PrefetchScalarGridSpec(
            num_scalar_prefetch=1,
            grid=(groups,),
            in_specs=[
                pl.BlockSpec((1, latents, width), lambda g, c: (g, 0, 0)),
                pl.BlockSpec((1, tokens, width), lambda g, c: (g, 0, 0)),
                pl.BlockSpec((1, tokens, width), lambda g, c: (g, 0, 1)),
            ],
            out_specs=pl.BlockSpec((1, latents, width), lambda g, c: (g, 0, 0)),
        ),
        out_shape=jax.ShapeDtypeStruct((groups, latents, width), jnp.bfloat16),
    )(counts, queries, key_value, key_value)


def per_device(
    state,
    unit_slot,
    token_count,
    session,
    session_row,
    unit_count,
    panels,
    memory_key,
    memory_value,
    q1_weight,
    o1_weight,
    kv_weight,
    q2_weight,
    o2_weight,
):
    local_samples, latents, model_width = state.shape
    token_total = unit_slot.shape[1]
    owners = lax.axis_size("smp")
    sess_dev, unit_total = (panels.shape[0], panels.shape[1])
    head_count = model_width // HEAD_DIM
    session_ids = jnp.arange(session_row.shape[0], dtype=jnp.int32)
    panel_row = jnp.sum(
        jnp.where(session[:, None] == session_ids[None, :], session_row[None, :], 0), axis=1
    )
    unit_limit = jnp.sum(
        jnp.where(panel_row[:, None] == session_ids[None, :], unit_count[None, :], 0), axis=1
    )
    owner_rank = panel_row // sess_dev
    token_index = (panel_row % sess_dev * unit_total)[:, None] + unit_slot % unit_limit[:, None]
    slot_pick = owner_rank[None, :] == jnp.arange(owners, dtype=jnp.int32)[:, None]
    request = jnp.sum(jnp.where(slot_pick[:, :, None], token_index[None, :, :], 0), axis=1)
    count_pick = jnp.sum(jnp.where(slot_pick, token_count[None, :], 0), axis=1)
    sample_pick = jnp.sum(
        jnp.where(slot_pick, jnp.arange(local_samples, dtype=jnp.int32)[None, :], 0), axis=1
    )
    served = lax.all_to_all(
        jnp.concatenate([request, count_pick[:, None]], axis=1),
        "smp",
        split_axis=0,
        concat_axis=0,
        tiled=True,
    )
    served_index = served[:, :token_total]
    panel_table = panels.reshape(sess_dev * unit_total, model_width)
    served_embed = panel_table[served_index.reshape(-1)]
    row_total = local_samples * latents
    flat_state = state.reshape(row_total, model_width)
    queries = jnp.dot(normed(flat_state), q1_weight, preferred_element_type=jnp.float32).astype(
        jnp.bfloat16
    )
    memory_pair = jnp.concatenate([memory_key, memory_value], axis=1)
    memory_rows = lax.all_to_all(
        jnp.broadcast_to(memory_pair[None], (owners,) + memory_pair.shape),
        "smp",
        split_axis=0,
        concat_axis=0,
        tiled=True,
    ).reshape(1, -1, 2 * model_width)
    embed_normed = normed(served_embed).reshape(owners, token_total, model_width)
    embed_normed, memory_rows = lax.optimization_barrier((embed_normed, memory_rows))
    memory_total = memory_rows.shape[1]
    read_mem = attend_kernel(
        queries.reshape(1, row_total, model_width),
        memory_rows,
        jnp.full((1,), memory_total, jnp.int32),
    ).reshape(row_total, model_width)
    hidden = (
        flat_state.astype(jnp.float32)
        + jnp.dot(read_mem, o1_weight, preferred_element_type=jnp.float32)
    ).astype(jnp.bfloat16)
    queries2 = jnp.dot(normed(hidden), q2_weight, preferred_element_type=jnp.float32).astype(
        jnp.bfloat16
    )
    queries2 = queries2.reshape(local_samples, latents, model_width)
    served_queries = lax.all_to_all(
        queries2[sample_pick], "smp", split_axis=0, concat_axis=0, tiled=True
    )
    key_rows = jnp.einsum(
        "btc,chd->bhtd",
        embed_normed,
        kv_weight[:, :model_width].reshape(model_width, head_count, HEAD_DIM),
        preferred_element_type=jnp.float32,
    ).astype(jnp.bfloat16)
    value_rows = jnp.einsum(
        "btc,chd->bhtd",
        embed_normed,
        kv_weight[:, model_width:].reshape(model_width, head_count, HEAD_DIM),
        preferred_element_type=jnp.float32,
    ).astype(jnp.bfloat16)
    key_rows, value_rows = lax.optimization_barrier((key_rows, value_rows))
    live_tokens = jnp.arange(token_total, dtype=jnp.int32)[None, :] < served[:, token_total:]
    served_read = attend_heads(
        served_queries.reshape(owners, latents, head_count, HEAD_DIM),
        key_rows,
        value_rows,
        live_tokens,
    )
    read_spike = exchange(served_read.reshape(owners, latents, model_width), "smp")[owner_rank]
    result = hidden.astype(jnp.float32) + jnp.dot(
        read_spike.reshape(row_total, model_width), o2_weight, preferred_element_type=jnp.float32
    )
    return result.astype(jnp.bfloat16).reshape(local_samples, latents, model_width)


def solution(mesh):
    in_specs = (
        P(("grp", "smp"), None, None),
        P(("grp", "smp"), None),
        P(("grp", "smp")),
        P(("grp", "smp")),
        P("grp"),
        P(),
        P("smp", None, None),
        P(("grp", "smp"), None),
        P(("grp", "smp"), None),
        P(),
        P(),
        P(),
        P(),
        P(),
    )
    out_specs = P(("grp", "smp"), None, None)
    return jax.shard_map(
        per_device, mesh=mesh, in_specs=in_specs, out_specs=out_specs, check_vma=False
    )
```

```python
import jax
import jax.numpy as jnp
from jax import lax
from jax.experimental import pallas as pl
from jax.experimental.pallas import tpu as pltpu
from jax.sharding import PartitionSpec as P

HEAD_DIM = 64


masked_score = -1e30


def normed(values):
    wide = values.astype(jnp.float32)
    return (wide * lax.rsqrt(jnp.mean(wide * wide, axis=-1, keepdims=True) + 1e-05)).astype(
        jnp.bfloat16
    )


def attend(queries, key_rows, value_rows, live_tokens):
    samples, latents, head_count, head_size = queries.shape
    spike_scores = jnp.einsum(
        "blhd,bkhd->bhlk", queries, key_rows, preferred_element_type=jnp.float32
    ) * HEAD_DIM ** (-0.5)
    spike_scores = jnp.where(live_tokens[:, None, None, :], spike_scores, masked_score)
    spike_max = jnp.max(spike_scores, axis=-1, keepdims=True)
    spike_exp = jnp.exp(spike_scores - spike_max)
    denominator = jnp.transpose(jnp.sum(spike_exp, axis=-1, keepdims=True), (0, 2, 1, 3))
    spike_mix = (
        jnp.einsum(
            "bhlk,bkhd->blhd",
            spike_exp.astype(jnp.bfloat16),
            value_rows,
            preferred_element_type=jnp.float32,
        )
        / denominator
    )
    return spike_mix.reshape(samples, latents, head_count * head_size).astype(jnp.bfloat16)


def attend_heads(queries, key_rows, value_rows, live_tokens):
    samples, latents, head_count, head_size = queries.shape
    spike_scores = jnp.einsum(
        "blhd,hbkd->bhlk", queries, key_rows, preferred_element_type=jnp.float32
    ) * HEAD_DIM ** (-0.5)
    spike_scores = jnp.where(live_tokens[:, None, None, :], spike_scores, masked_score)
    spike_max = jnp.max(spike_scores, axis=-1, keepdims=True)
    spike_exp = jnp.exp(spike_scores - spike_max)
    denominator = jnp.transpose(jnp.sum(spike_exp, axis=-1, keepdims=True), (0, 2, 1, 3))
    spike_mix = (
        jnp.einsum(
            "bhlk,hbkd->blhd",
            spike_exp.astype(jnp.bfloat16),
            value_rows,
            preferred_element_type=jnp.float32,
        )
        / denominator
    )
    return spike_mix.reshape(samples, latents, head_count * head_size).astype(jnp.bfloat16)


def attend_block(counts_ref, query_ref, key_ref, value_ref, out_ref):
    group = pl.program_id(0)
    latents = query_ref.shape[1]
    tokens = key_ref.shape[1]
    live = lax.broadcasted_iota(jnp.int32, (latents, tokens), 1) < counts_ref[group]
    first_head = lax.broadcasted_iota(jnp.int32, (1, 2 * HEAD_DIM), 1) < HEAD_DIM
    for pair in range(query_ref.shape[2] // (2 * HEAD_DIM)):
        cols = pl.ds(pair * 2 * HEAD_DIM, 2 * HEAD_DIM)
        query = query_ref[0, :, cols]
        key = key_ref[0, :, cols]
        value = value_ref[0, :, cols]
        mixes = []
        for half in (first_head, jnp.logical_not(first_head)):
            scores = lax.dot_general(
                jnp.where(half, query, jnp.zeros_like(query)),
                key,
                (((1,), (1,)), ((), ())),
                preferred_element_type=jnp.float32,
            ) * HEAD_DIM ** (-0.5)
            scores = jnp.where(live, scores, masked_score)
            row_max = jnp.max(scores, axis=1, keepdims=True)
            exponent = jnp.exp(scores - row_max)
            denominator = jnp.sum(exponent, axis=1, keepdims=True)
            mix = jnp.dot(
                exponent.astype(jnp.bfloat16), value, preferred_element_type=jnp.float32
            )
            mixes.append(mix / denominator)
        out_ref[0, :, cols] = jnp.where(first_head, mixes[0], mixes[1]).astype(jnp.bfloat16)


def attend_kernel(queries, key_value, counts):
    groups, latents, width = queries.shape
    tokens = key_value.shape[1]
    return pl.pallas_call(
        attend_block,
        grid_spec=pltpu.PrefetchScalarGridSpec(
            num_scalar_prefetch=1,
            grid=(groups,),
            in_specs=[
                pl.BlockSpec((1, latents, width), lambda g, c: (g, 0, 0)),
                pl.BlockSpec((1, tokens, width), lambda g, c: (g, 0, 0)),
                pl.BlockSpec((1, tokens, width), lambda g, c: (g, 0, 1)),
            ],
            out_specs=pl.BlockSpec((1, latents, width), lambda g, c: (g, 0, 0)),
        ),
        out_shape=jax.ShapeDtypeStruct((groups, latents, width), jnp.bfloat16),
    )(counts, queries, key_value, key_value)


def per_device(
    state,
    unit_slot,
    token_count,
    session,
    session_row,
    unit_count,
    panels,
    memory_key,
    memory_value,
    q1_weight,
    o1_weight,
    kv_weight,
    q2_weight,
    o2_weight,
):
    local_samples, latents, model_width = state.shape
    token_total = unit_slot.shape[1]
    owners = lax.axis_size("smp")
    sess_dev, unit_total = (panels.shape[0], panels.shape[1])
    head_count = model_width // HEAD_DIM
    session_ids = jnp.arange(session_row.shape[0], dtype=jnp.int32)
    panel_row = jnp.sum(
        jnp.where(session[:, None] == session_ids[None, :], session_row[None, :], 0), axis=1
    )
    unit_limit = jnp.sum(
        jnp.where(panel_row[:, None] == session_ids[None, :], unit_count[None, :], 0), axis=1
    )
    owner_rank = panel_row // sess_dev
    token_index = (panel_row % sess_dev * unit_total)[:, None] + unit_slot % unit_limit[:, None]
    slot_pick = owner_rank[None, :] == jnp.arange(owners, dtype=jnp.int32)[:, None]
    request = jnp.sum(jnp.where(slot_pick[:, :, None], token_index[None, :, :], 0), axis=1)
    count_pick = jnp.sum(jnp.where(slot_pick, token_count[None, :], 0), axis=1)
    sample_pick = jnp.sum(
        jnp.where(slot_pick, jnp.arange(local_samples, dtype=jnp.int32)[None, :], 0), axis=1
    )
    panel_table = panels.reshape(sess_dev * unit_total, model_width)
    panel_normed = normed(panel_table)
    key_table = jnp.einsum(
        "pc,chd->hpd",
        panel_normed,
        kv_weight[:, :model_width].reshape(model_width, head_count, HEAD_DIM),
        preferred_element_type=jnp.float32,
    ).astype(jnp.bfloat16)
    value_table = jnp.einsum(
        "pc,chd->hpd",
        panel_normed,
        kv_weight[:, model_width:].reshape(model_width, head_count, HEAD_DIM),
        preferred_element_type=jnp.float32,
    ).astype(jnp.bfloat16)
    row_total = local_samples * latents
    flat_state = state.reshape(row_total, model_width)
    queries = jnp.dot(normed(flat_state), q1_weight, preferred_element_type=jnp.float32).astype(
        jnp.bfloat16
    )
    table = jnp.concatenate([request, count_pick[:, None]], axis=1)
    code_base = 64
    codes = jnp.concatenate([table // code_base, table % code_base], axis=1).astype(jnp.bfloat16)
    memory_pair = jnp.concatenate([memory_key, memory_value], axis=1)
    memory_count = memory_pair.shape[0]
    code_lanes = 2 * HEAD_DIM
    code_block = jnp.pad(codes, ((0, 0), (0, memory_count * code_lanes - codes.shape[1])))
    arrived = lax.all_to_all(
        jnp.concatenate(
            [
                jnp.broadcast_to(memory_pair[None], (owners,) + memory_pair.shape),
                code_block.reshape(owners, memory_count, code_lanes),
            ],
            axis=2,
        ),
        "smp",
        split_axis=0,
        concat_axis=0,
        tiled=True,
    )
    memory_rows = arrived[:, :, : 2 * model_width].reshape(1, -1, 2 * model_width)
    code_back = (
        arrived[:, :, 2 * model_width :].reshape(owners, -1)[:, : codes.shape[1]].astype(jnp.int32)
    )
    served = code_back[:, : table.shape[1]] * code_base + code_back[:, table.shape[1] :]
    served_index = served[:, :token_total]
    memory_total = memory_rows.shape[1]
    read_mem = attend_kernel(
        queries.reshape(1, row_total, model_width),
        memory_rows,
        jnp.full((1,), memory_total, jnp.int32),
    ).reshape(row_total, model_width)
    hidden = (
        flat_state.astype(jnp.float32)
        + jnp.dot(read_mem, o1_weight, preferred_element_type=jnp.float32)
    ).astype(jnp.bfloat16)
    queries2 = jnp.dot(normed(hidden), q2_weight, preferred_element_type=jnp.float32).astype(
        jnp.bfloat16
    )
    queries2 = queries2.reshape(local_samples, latents, model_width)
    served_queries = lax.all_to_all(
        queries2[sample_pick], "smp", split_axis=0, concat_axis=0, tiled=True
    )
    key_rows = key_table[:, served_index]
    value_rows = value_table[:, served_index]
    live_tokens = jnp.arange(token_total, dtype=jnp.int32)[None, :] < served[:, token_total:]
    served_read = attend_heads(
        served_queries.reshape(owners, latents, head_count, HEAD_DIM),
        key_rows,
        value_rows,
        live_tokens,
    )
    read_spike = lax.all_to_all(
        served_read.reshape(owners, latents, model_width),
        "smp",
        split_axis=0,
        concat_axis=0,
        tiled=True,
    )[owner_rank]
    result = hidden.astype(jnp.float32) + jnp.dot(
        read_spike.reshape(row_total, model_width), o2_weight, preferred_element_type=jnp.float32
    )
    return result.astype(jnp.bfloat16).reshape(local_samples, latents, model_width)


def solution(mesh):
    in_specs = (
        P(("grp", "smp"), None, None),
        P(("grp", "smp"), None),
        P(("grp", "smp")),
        P(("grp", "smp")),
        P("grp"),
        P(),
        P("smp", None, None),
        P(("grp", "smp"), None),
        P(("grp", "smp"), None),
        P(),
        P(),
        P(),
        P(),
        P(),
    )
    out_specs = P(("grp", "smp"), None, None)
    return jax.shard_map(
        per_device, mesh=mesh, in_specs=in_specs, out_specs=out_specs, check_vma=False
    )
```

```python
import jax
import jax.numpy as jnp
from jax import lax
from jax.experimental import pallas as pl
from jax.experimental.pallas import tpu as pltpu
from jax.sharding import PartitionSpec as P

HEAD_DIM = 64


masked_score = -1e30


def normed(values):
    wide = values.astype(jnp.float32)
    return (wide * lax.rsqrt(jnp.mean(wide * wide, axis=-1, keepdims=True) + 1e-05)).astype(
        jnp.bfloat16
    )


def attend(queries, key_rows, value_rows, live_tokens):
    samples, latents, head_count, head_size = queries.shape
    spike_scores = jnp.einsum(
        "blhd,bkhd->bhlk", queries, key_rows, preferred_element_type=jnp.float32
    ) * HEAD_DIM ** (-0.5)
    spike_scores = jnp.where(live_tokens[:, None, None, :], spike_scores, masked_score)
    spike_max = jnp.max(spike_scores, axis=-1, keepdims=True)
    spike_exp = jnp.exp(spike_scores - spike_max)
    denominator = jnp.transpose(jnp.sum(spike_exp, axis=-1, keepdims=True), (0, 2, 1, 3))
    spike_mix = (
        jnp.einsum(
            "bhlk,bkhd->blhd",
            spike_exp.astype(jnp.bfloat16),
            value_rows,
            preferred_element_type=jnp.float32,
        )
        / denominator
    )
    return spike_mix.reshape(samples, latents, head_count * head_size).astype(jnp.bfloat16)


def attend_heads(queries, key_rows, value_rows, live_tokens):
    samples, latents, head_count, head_size = queries.shape
    spike_scores = jnp.einsum(
        "blhd,hbkd->bhlk", queries, key_rows, preferred_element_type=jnp.float32
    ) * HEAD_DIM ** (-0.5)
    spike_scores = jnp.where(live_tokens[:, None, None, :], spike_scores, masked_score)
    spike_max = jnp.max(spike_scores, axis=-1, keepdims=True)
    spike_exp = jnp.exp(spike_scores - spike_max)
    denominator = jnp.transpose(jnp.sum(spike_exp, axis=-1, keepdims=True), (0, 2, 1, 3))
    spike_mix = (
        jnp.einsum(
            "bhlk,hbkd->blhd",
            spike_exp.astype(jnp.bfloat16),
            value_rows,
            preferred_element_type=jnp.float32,
        )
        / denominator
    )
    return spike_mix.reshape(samples, latents, head_count * head_size).astype(jnp.bfloat16)


def attend_block(counts_ref, query_ref, key_ref, value_ref, out_ref):
    group = pl.program_id(0)
    latents = query_ref.shape[1]
    tokens = key_ref.shape[1]
    live = lax.broadcasted_iota(jnp.int32, (latents, tokens), 1) < counts_ref[group]
    first_head = lax.broadcasted_iota(jnp.int32, (1, 2 * HEAD_DIM), 1) < HEAD_DIM
    for pair in range(query_ref.shape[2] // (2 * HEAD_DIM)):
        cols = pl.ds(pair * 2 * HEAD_DIM, 2 * HEAD_DIM)
        query = query_ref[0, :, cols]
        key = key_ref[0, :, cols]
        value = value_ref[0, :, cols]
        mixes = []
        for half in (first_head, jnp.logical_not(first_head)):
            scores = lax.dot_general(
                jnp.where(half, query, jnp.zeros_like(query)),
                key,
                (((1,), (1,)), ((), ())),
                preferred_element_type=jnp.float32,
            ) * HEAD_DIM ** (-0.5)
            scores = jnp.where(live, scores, masked_score)
            row_max = jnp.max(scores, axis=1, keepdims=True)
            exponent = jnp.exp(scores - row_max)
            denominator = jnp.sum(exponent, axis=1, keepdims=True)
            mix = jnp.dot(
                exponent.astype(jnp.bfloat16), value, preferred_element_type=jnp.float32
            )
            mixes.append(mix / denominator)
        out_ref[0, :, cols] = jnp.where(first_head, mixes[0], mixes[1]).astype(jnp.bfloat16)


def attend_kernel(queries, key_value, counts):
    groups, latents, width = queries.shape
    tokens = key_value.shape[1]
    return pl.pallas_call(
        attend_block,
        grid_spec=pltpu.PrefetchScalarGridSpec(
            num_scalar_prefetch=1,
            grid=(groups,),
            in_specs=[
                pl.BlockSpec((1, latents, width), lambda g, c: (g, 0, 0)),
                pl.BlockSpec((1, tokens, width), lambda g, c: (g, 0, 0)),
                pl.BlockSpec((1, tokens, width), lambda g, c: (g, 0, 1)),
            ],
            out_specs=pl.BlockSpec((1, latents, width), lambda g, c: (g, 0, 0)),
        ),
        out_shape=jax.ShapeDtypeStruct((groups, latents, width), jnp.bfloat16),
    )(counts, queries, key_value, key_value)


def per_device(
    state,
    unit_slot,
    token_count,
    session,
    session_row,
    unit_count,
    panels,
    memory_key,
    memory_value,
    q1_weight,
    o1_weight,
    kv_weight,
    q2_weight,
    o2_weight,
):
    local_samples, latents, model_width = state.shape
    token_total = unit_slot.shape[1]
    owners = lax.axis_size("smp")
    sess_dev, unit_total = (panels.shape[0], panels.shape[1])
    head_count = model_width // HEAD_DIM
    session_ids = jnp.arange(session_row.shape[0], dtype=jnp.int32)
    panel_row = jnp.sum(
        jnp.where(session[:, None] == session_ids[None, :], session_row[None, :], 0), axis=1
    )
    unit_limit = jnp.sum(
        jnp.where(panel_row[:, None] == session_ids[None, :], unit_count[None, :], 0), axis=1
    )
    owner_rank = panel_row // sess_dev
    token_index = (panel_row % sess_dev * unit_total)[:, None] + unit_slot % unit_limit[:, None]
    slot_pick = owner_rank[None, :] == jnp.arange(owners, dtype=jnp.int32)[:, None]
    request = jnp.sum(jnp.where(slot_pick[:, :, None], token_index[None, :, :], 0), axis=1)
    count_pick = jnp.sum(jnp.where(slot_pick, token_count[None, :], 0), axis=1)
    sample_pick = jnp.sum(
        jnp.where(slot_pick, jnp.arange(local_samples, dtype=jnp.int32)[None, :], 0), axis=1
    )
    panel_table = panels.reshape(sess_dev * unit_total, model_width)
    panel_normed = normed(panel_table)
    key_table = jnp.einsum(
        "pc,chd->hpd",
        panel_normed,
        kv_weight[:, :model_width].reshape(model_width, head_count, HEAD_DIM),
        preferred_element_type=jnp.float32,
    ).astype(jnp.bfloat16)
    value_table = jnp.einsum(
        "pc,chd->hpd",
        panel_normed,
        kv_weight[:, model_width:].reshape(model_width, head_count, HEAD_DIM),
        preferred_element_type=jnp.float32,
    ).astype(jnp.bfloat16)
    row_total = local_samples * latents
    flat_state = state.reshape(row_total, model_width)
    queries = jnp.dot(normed(flat_state), q1_weight, preferred_element_type=jnp.float32).astype(
        jnp.bfloat16
    )
    table = jnp.concatenate([request, count_pick[:, None]], axis=1)
    code_base = 64
    codes = jnp.concatenate([table // code_base, table % code_base], axis=1).astype(jnp.bfloat16)
    memory_pair = jnp.concatenate([memory_key, memory_value], axis=1)
    memory_count = memory_pair.shape[0]
    code_lanes = 2 * HEAD_DIM
    code_block = jnp.pad(codes, ((0, 0), (0, memory_count * code_lanes - codes.shape[1])))
    arrived = lax.all_to_all(
        jnp.concatenate(
            [
                jnp.broadcast_to(memory_pair[None], (owners,) + memory_pair.shape),
                code_block.reshape(owners, memory_count, code_lanes),
            ],
            axis=2,
        ),
        "smp",
        split_axis=0,
        concat_axis=0,
        tiled=True,
    )
    memory_rows = arrived[:, :, : 2 * model_width].reshape(1, -1, 2 * model_width)
    code_back = (
        arrived[:, :, 2 * model_width :].reshape(owners, -1)[:, : codes.shape[1]].astype(jnp.int32)
    )
    served = code_back[:, : table.shape[1]] * code_base + code_back[:, table.shape[1] :]
    served_index = served[:, :token_total]
    memory_total = memory_rows.shape[1]
    read_mem = attend_kernel(
        queries.reshape(1, row_total, model_width),
        memory_rows,
        jnp.full((1,), memory_total, jnp.int32),
    ).reshape(row_total, model_width)
    hidden = (
        flat_state.astype(jnp.float32)
        + jnp.dot(read_mem, o1_weight, preferred_element_type=jnp.float32)
    ).astype(jnp.bfloat16)
    queries2 = jnp.dot(normed(hidden), q2_weight, preferred_element_type=jnp.float32).astype(
        jnp.bfloat16
    )
    queries2 = queries2.reshape(local_samples, latents, model_width)
    served_queries = lax.all_to_all(
        queries2[sample_pick], "smp", split_axis=0, concat_axis=0, tiled=True
    )
    pick = (
        served_index.reshape(-1)[:, None]
        == jnp.arange(key_table.shape[1], dtype=jnp.int32)[None, :]
    ).astype(jnp.bfloat16)
    key_rows = (
        jnp.einsum("np,hpd->hnd", pick, key_table, preferred_element_type=jnp.float32)
        .astype(jnp.bfloat16)
        .reshape(head_count, owners, token_total, HEAD_DIM)
    )
    value_rows = (
        jnp.einsum("np,hpd->hnd", pick, value_table, preferred_element_type=jnp.float32)
        .astype(jnp.bfloat16)
        .reshape(head_count, owners, token_total, HEAD_DIM)
    )
    live_tokens = jnp.arange(token_total, dtype=jnp.int32)[None, :] < served[:, token_total:]
    served_read = attend_heads(
        served_queries.reshape(owners, latents, head_count, HEAD_DIM),
        key_rows,
        value_rows,
        live_tokens,
    )
    read_spike = lax.all_to_all(
        served_read.reshape(owners, latents, model_width),
        "smp",
        split_axis=0,
        concat_axis=0,
        tiled=True,
    )[owner_rank]
    result = hidden.astype(jnp.float32) + jnp.dot(
        read_spike.reshape(row_total, model_width), o2_weight, preferred_element_type=jnp.float32
    )
    return result.astype(jnp.bfloat16).reshape(local_samples, latents, model_width)


def solution(mesh):
    in_specs = (
        P(("grp", "smp"), None, None),
        P(("grp", "smp"), None),
        P(("grp", "smp")),
        P(("grp", "smp")),
        P("grp"),
        P(),
        P("smp", None, None),
        P(("grp", "smp"), None),
        P(("grp", "smp"), None),
        P(),
        P(),
        P(),
        P(),
        P(),
    )
    out_specs = P(("grp", "smp"), None, None)
    return jax.shard_map(
        per_device, mesh=mesh, in_specs=in_specs, out_specs=out_specs, check_vma=False
    )
```

```python
import jax
import jax.numpy as jnp
from jax import lax
from jax.experimental import pallas as pl
from jax.experimental.pallas import tpu as pltpu
from jax.sharding import PartitionSpec as P

HEAD_DIM = 64


masked_score = -1e30


def normed(values):
    wide = values.astype(jnp.float32)
    return (wide * lax.rsqrt(jnp.mean(wide * wide, axis=-1, keepdims=True) + 1e-05)).astype(
        jnp.bfloat16
    )


def attend(queries, key_rows, value_rows, live_tokens):
    samples, latents, head_count, head_size = queries.shape
    spike_scores = jnp.einsum(
        "blhd,bkhd->bhlk", queries, key_rows, preferred_element_type=jnp.float32
    ) * HEAD_DIM ** (-0.5)
    spike_scores = jnp.where(live_tokens[:, None, None, :], spike_scores, masked_score)
    spike_max = jnp.max(spike_scores, axis=-1, keepdims=True)
    spike_exp = jnp.exp(spike_scores - spike_max)
    denominator = jnp.transpose(jnp.sum(spike_exp, axis=-1, keepdims=True), (0, 2, 1, 3))
    spike_mix = (
        jnp.einsum(
            "bhlk,bkhd->blhd",
            spike_exp.astype(jnp.bfloat16),
            value_rows,
            preferred_element_type=jnp.float32,
        )
        / denominator
    )
    return spike_mix.reshape(samples, latents, head_count * head_size).astype(jnp.bfloat16)


def attend_heads(queries, key_rows, value_rows, live_tokens):
    samples, latents, head_count, head_size = queries.shape
    spike_scores = jnp.einsum(
        "blhd,hbkd->bhlk", queries, key_rows, preferred_element_type=jnp.float32
    ) * HEAD_DIM ** (-0.5)
    spike_scores = jnp.where(live_tokens[:, None, None, :], spike_scores, masked_score)
    spike_max = jnp.max(spike_scores, axis=-1, keepdims=True)
    spike_exp = jnp.exp(spike_scores - spike_max)
    denominator = jnp.transpose(jnp.sum(spike_exp, axis=-1, keepdims=True), (0, 2, 1, 3))
    spike_mix = (
        jnp.einsum(
            "bhlk,hbkd->blhd",
            spike_exp.astype(jnp.bfloat16),
            value_rows,
            preferred_element_type=jnp.float32,
        )
        / denominator
    )
    return spike_mix.reshape(samples, latents, head_count * head_size).astype(jnp.bfloat16)


def attend_block(counts_ref, query_ref, key_ref, value_ref, out_ref):
    group = pl.program_id(0)
    latents = query_ref.shape[1]
    tokens = key_ref.shape[1]
    live = lax.broadcasted_iota(jnp.int32, (latents, tokens), 1) < counts_ref[group]
    first_head = lax.broadcasted_iota(jnp.int32, (1, 2 * HEAD_DIM), 1) < HEAD_DIM
    for pair in range(query_ref.shape[2] // (2 * HEAD_DIM)):
        cols = pl.ds(pair * 2 * HEAD_DIM, 2 * HEAD_DIM)
        query = query_ref[0, :, cols]
        key = key_ref[0, :, cols]
        value = value_ref[0, :, cols]
        mixes = []
        for half in (first_head, jnp.logical_not(first_head)):
            scores = lax.dot_general(
                jnp.where(half, query, jnp.zeros_like(query)),
                key,
                (((1,), (1,)), ((), ())),
                preferred_element_type=jnp.float32,
            ) * HEAD_DIM ** (-0.5)
            scores = jnp.where(live, scores, masked_score)
            row_max = jnp.max(scores, axis=1, keepdims=True)
            exponent = jnp.exp(scores - row_max)
            denominator = jnp.sum(exponent, axis=1, keepdims=True)
            mix = jnp.dot(
                exponent.astype(jnp.bfloat16), value, preferred_element_type=jnp.float32
            )
            mixes.append(mix / denominator)
        out_ref[0, :, cols] = jnp.where(first_head, mixes[0], mixes[1]).astype(jnp.bfloat16)


def attend_kernel(queries, key_value, counts):
    groups, latents, width = queries.shape
    tokens = key_value.shape[1]
    return pl.pallas_call(
        attend_block,
        grid_spec=pltpu.PrefetchScalarGridSpec(
            num_scalar_prefetch=1,
            grid=(groups,),
            in_specs=[
                pl.BlockSpec((1, latents, width), lambda g, c: (g, 0, 0)),
                pl.BlockSpec((1, tokens, width), lambda g, c: (g, 0, 0)),
                pl.BlockSpec((1, tokens, width), lambda g, c: (g, 0, 1)),
            ],
            out_specs=pl.BlockSpec((1, latents, width), lambda g, c: (g, 0, 0)),
        ),
        out_shape=jax.ShapeDtypeStruct((groups, latents, width), jnp.bfloat16),
    )(counts, queries, key_value, key_value)


def per_device(
    state,
    unit_slot,
    token_count,
    session,
    session_row,
    unit_count,
    panels,
    memory_key,
    memory_value,
    q1_weight,
    o1_weight,
    kv_weight,
    q2_weight,
    o2_weight,
):
    local_samples, latents, model_width = state.shape
    token_total = unit_slot.shape[1]
    owners = lax.axis_size("smp")
    sess_dev, unit_total = (panels.shape[0], panels.shape[1])
    head_count = model_width // HEAD_DIM
    session_ids = jnp.arange(session_row.shape[0], dtype=jnp.int32)
    panel_row = jnp.sum(
        jnp.where(session[:, None] == session_ids[None, :], session_row[None, :], 0), axis=1
    )
    unit_limit = jnp.sum(
        jnp.where(panel_row[:, None] == session_ids[None, :], unit_count[None, :], 0), axis=1
    )
    owner_rank = panel_row // sess_dev
    token_index = (panel_row % sess_dev * unit_total)[:, None] + unit_slot % unit_limit[:, None]
    slot_pick = owner_rank[None, :] == jnp.arange(owners, dtype=jnp.int32)[:, None]
    request = jnp.sum(jnp.where(slot_pick[:, :, None], token_index[None, :, :], 0), axis=1)
    count_pick = jnp.sum(jnp.where(slot_pick, token_count[None, :], 0), axis=1)
    sample_pick = jnp.sum(
        jnp.where(slot_pick, jnp.arange(local_samples, dtype=jnp.int32)[None, :], 0), axis=1
    )
    panel_table = panels.reshape(sess_dev * unit_total, model_width)
    panel_normed = normed(panel_table)
    key_table = jnp.einsum(
        "pc,chd->hpd",
        panel_normed,
        kv_weight[:, :model_width].reshape(model_width, head_count, HEAD_DIM),
        preferred_element_type=jnp.float32,
    ).astype(jnp.bfloat16)
    value_table = jnp.einsum(
        "pc,chd->hpd",
        panel_normed,
        kv_weight[:, model_width:].reshape(model_width, head_count, HEAD_DIM),
        preferred_element_type=jnp.float32,
    ).astype(jnp.bfloat16)
    row_total = local_samples * latents
    flat_state = state.reshape(row_total, model_width)
    queries = jnp.dot(normed(flat_state), q1_weight, preferred_element_type=jnp.float32).astype(
        jnp.bfloat16
    )
    table = jnp.concatenate([request, count_pick[:, None]], axis=1)
    code_base = 64
    codes = jnp.concatenate([table // code_base, table % code_base], axis=1).astype(jnp.bfloat16)
    memory_pair = jnp.concatenate([memory_key, memory_value], axis=1)
    memory_count = memory_pair.shape[0]
    code_lanes = 2 * HEAD_DIM
    code_block = jnp.pad(codes, ((0, 0), (0, memory_count * code_lanes - codes.shape[1])))
    arrived = lax.all_to_all(
        jnp.concatenate(
            [
                jnp.broadcast_to(memory_pair[None], (owners,) + memory_pair.shape),
                code_block.reshape(owners, memory_count, code_lanes),
            ],
            axis=2,
        ),
        "smp",
        split_axis=0,
        concat_axis=0,
        tiled=True,
    )
    memory_rows = arrived.reshape(1, -1, arrived.shape[2])
    code_back = (
        arrived[:, :, 2 * model_width :].reshape(owners, -1)[:, : codes.shape[1]].astype(jnp.int32)
    )
    served = code_back[:, : table.shape[1]] * code_base + code_back[:, table.shape[1] :]
    served_index = served[:, :token_total]
    memory_total = memory_rows.shape[1]
    read_mem = attend_kernel(
        queries.reshape(1, row_total, model_width),
        memory_rows,
        jnp.full((1,), memory_total, jnp.int32),
    ).reshape(row_total, model_width)
    hidden = (
        flat_state.astype(jnp.float32)
        + jnp.dot(read_mem, o1_weight, preferred_element_type=jnp.float32)
    ).astype(jnp.bfloat16)
    queries2 = jnp.dot(normed(hidden), q2_weight, preferred_element_type=jnp.float32).astype(
        jnp.bfloat16
    )
    queries2 = queries2.reshape(local_samples, latents, model_width)
    served_queries = lax.all_to_all(
        jnp.einsum(
            "ob,bld->old",
            (sample_pick[:, None] == jnp.arange(local_samples, dtype=jnp.int32)[None, :]).astype(
                jnp.bfloat16
            ),
            queries2,
            preferred_element_type=jnp.float32,
        ).astype(jnp.bfloat16),
        "smp",
        split_axis=0,
        concat_axis=0,
        tiled=True,
    )
    key_rows = key_table[:, served_index]
    value_rows = value_table[:, served_index]
    live_tokens = jnp.arange(token_total, dtype=jnp.int32)[None, :] < served[:, token_total:]
    served_read = attend_heads(
        served_queries.reshape(owners, latents, head_count, HEAD_DIM),
        key_rows,
        value_rows,
        live_tokens,
    )
    read_spike = lax.all_to_all(
        served_read.reshape(owners, latents, model_width),
        "smp",
        split_axis=0,
        concat_axis=0,
        tiled=True,
    )[owner_rank]
    result = hidden.astype(jnp.float32) + jnp.dot(
        read_spike.reshape(row_total, model_width), o2_weight, preferred_element_type=jnp.float32
    )
    return result.astype(jnp.bfloat16).reshape(local_samples, latents, model_width)


def solution(mesh):
    in_specs = (
        P(("grp", "smp"), None, None),
        P(("grp", "smp"), None),
        P(("grp", "smp")),
        P(("grp", "smp")),
        P("grp"),
        P(),
        P("smp", None, None),
        P(("grp", "smp"), None),
        P(("grp", "smp"), None),
        P(),
        P(),
        P(),
        P(),
        P(),
    )
    out_specs = P(("grp", "smp"), None, None)
    return jax.shard_map(
        per_device, mesh=mesh, in_specs=in_specs, out_specs=out_specs, check_vma=False
    )
```

```python
import jax
import jax.numpy as jnp
from jax import lax
from jax.experimental import pallas as pl
from jax.experimental.pallas import tpu as pltpu
from jax.sharding import PartitionSpec as P

HEAD_DIM = 64


masked_score = -1e30


def normed(values):
    wide = values.astype(jnp.float32)
    return (wide * lax.rsqrt(jnp.mean(wide * wide, axis=-1, keepdims=True) + 1e-05)).astype(
        jnp.bfloat16
    )


def attend(queries, key_rows, value_rows, live_tokens):
    samples, latents, head_count, head_size = queries.shape
    spike_scores = jnp.einsum(
        "blhd,bkhd->bhlk", queries, key_rows, preferred_element_type=jnp.float32
    ) * HEAD_DIM ** (-0.5)
    spike_scores = jnp.where(live_tokens[:, None, None, :], spike_scores, masked_score)
    spike_max = jnp.max(spike_scores, axis=-1, keepdims=True)
    spike_exp = jnp.exp(spike_scores - spike_max)
    denominator = jnp.transpose(jnp.sum(spike_exp, axis=-1, keepdims=True), (0, 2, 1, 3))
    spike_mix = (
        jnp.einsum(
            "bhlk,bkhd->blhd",
            spike_exp.astype(jnp.bfloat16),
            value_rows,
            preferred_element_type=jnp.float32,
        )
        / denominator
    )
    return spike_mix.reshape(samples, latents, head_count * head_size).astype(jnp.bfloat16)


def attend_heads(queries, key_rows, value_rows, live_tokens):
    samples, latents, head_count, head_size = queries.shape
    spike_scores = jnp.einsum(
        "blhd,bkhd->bhlk", queries, key_rows, preferred_element_type=jnp.float32
    ) * HEAD_DIM ** (-0.5)
    spike_scores = jnp.where(live_tokens[:, None, None, :], spike_scores, masked_score)
    spike_max = jnp.max(spike_scores, axis=-1, keepdims=True)
    spike_exp = jnp.exp(spike_scores - spike_max)
    denominator = jnp.transpose(jnp.sum(spike_exp, axis=-1, keepdims=True), (0, 2, 1, 3))
    spike_mix = (
        jnp.einsum(
            "bhlk,bkhd->blhd",
            spike_exp.astype(jnp.bfloat16),
            value_rows,
            preferred_element_type=jnp.float32,
        )
        / denominator
    )
    return spike_mix.reshape(samples, latents, head_count * head_size).astype(jnp.bfloat16)


def attend_block(counts_ref, query_ref, key_ref, value_ref, out_ref):
    group = pl.program_id(0)
    latents = query_ref.shape[1]
    tokens = key_ref.shape[1]
    live = lax.broadcasted_iota(jnp.int32, (latents, tokens), 1) < counts_ref[group]
    first_head = lax.broadcasted_iota(jnp.int32, (1, 2 * HEAD_DIM), 1) < HEAD_DIM
    for pair in range(query_ref.shape[2] // (2 * HEAD_DIM)):
        cols = pl.ds(pair * 2 * HEAD_DIM, 2 * HEAD_DIM)
        query = query_ref[0, :, cols]
        key = key_ref[0, :, cols]
        value = value_ref[0, :, cols]
        mixes = []
        for half in (first_head, jnp.logical_not(first_head)):
            scores = lax.dot_general(
                jnp.where(half, query, jnp.zeros_like(query)),
                key,
                (((1,), (1,)), ((), ())),
                preferred_element_type=jnp.float32,
            ) * HEAD_DIM ** (-0.5)
            scores = jnp.where(live, scores, masked_score)
            row_max = jnp.max(scores, axis=1, keepdims=True)
            exponent = jnp.exp(scores - row_max)
            denominator = jnp.sum(exponent, axis=1, keepdims=True)
            mix = jnp.dot(
                exponent.astype(jnp.bfloat16), value, preferred_element_type=jnp.float32
            )
            mixes.append(mix / denominator)
        out_ref[0, :, cols] = jnp.where(first_head, mixes[0], mixes[1]).astype(jnp.bfloat16)


def attend_kernel(queries, key_value, counts):
    groups, latents, width = queries.shape
    tokens = key_value.shape[1]
    return pl.pallas_call(
        attend_block,
        grid_spec=pltpu.PrefetchScalarGridSpec(
            num_scalar_prefetch=1,
            grid=(groups,),
            in_specs=[
                pl.BlockSpec((1, latents, width), lambda g, c: (g, 0, 0)),
                pl.BlockSpec((1, tokens, width), lambda g, c: (g, 0, 0)),
                pl.BlockSpec((1, tokens, width), lambda g, c: (g, 0, 1)),
            ],
            out_specs=pl.BlockSpec((1, latents, width), lambda g, c: (g, 0, 0)),
        ),
        out_shape=jax.ShapeDtypeStruct((groups, latents, width), jnp.bfloat16),
    )(counts, queries, key_value, key_value)


def per_device(
    state,
    unit_slot,
    token_count,
    session,
    session_row,
    unit_count,
    panels,
    memory_key,
    memory_value,
    q1_weight,
    o1_weight,
    kv_weight,
    q2_weight,
    o2_weight,
):
    local_samples, latents, model_width = state.shape
    token_total = unit_slot.shape[1]
    owners = lax.axis_size("smp")
    sess_dev, unit_total = (panels.shape[0], panels.shape[1])
    head_count = model_width // HEAD_DIM
    session_ids = jnp.arange(session_row.shape[0], dtype=jnp.int32)
    panel_row = jnp.sum(
        jnp.where(session[:, None] == session_ids[None, :], session_row[None, :], 0), axis=1
    )
    unit_limit = jnp.sum(
        jnp.where(panel_row[:, None] == session_ids[None, :], unit_count[None, :], 0), axis=1
    )
    owner_rank = panel_row // sess_dev
    token_index = (panel_row % sess_dev * unit_total)[:, None] + unit_slot % unit_limit[:, None]
    slot_pick = owner_rank[None, :] == jnp.arange(owners, dtype=jnp.int32)[:, None]
    request = jnp.sum(jnp.where(slot_pick[:, :, None], token_index[None, :, :], 0), axis=1)
    count_pick = jnp.sum(jnp.where(slot_pick, token_count[None, :], 0), axis=1)
    sample_pick = jnp.sum(
        jnp.where(slot_pick, jnp.arange(local_samples, dtype=jnp.int32)[None, :], 0), axis=1
    )
    panel_table = panels.reshape(sess_dev * unit_total, model_width)
    panel_normed = normed(panel_table)
    key_table = jnp.einsum(
        "pc,chd->phd",
        panel_normed,
        kv_weight[:, :model_width].reshape(model_width, head_count, HEAD_DIM),
        preferred_element_type=jnp.float32,
    ).astype(jnp.bfloat16)
    value_table = jnp.einsum(
        "pc,chd->phd",
        panel_normed,
        kv_weight[:, model_width:].reshape(model_width, head_count, HEAD_DIM),
        preferred_element_type=jnp.float32,
    ).astype(jnp.bfloat16)
    row_total = local_samples * latents
    flat_state = state.reshape(row_total, model_width)
    queries = jnp.dot(normed(flat_state), q1_weight, preferred_element_type=jnp.float32).astype(
        jnp.bfloat16
    )
    table = jnp.concatenate([request, count_pick[:, None]], axis=1)
    code_base = 64
    codes = jnp.concatenate([table // code_base, table % code_base], axis=1).astype(jnp.bfloat16)
    memory_pair = jnp.concatenate([memory_key, memory_value], axis=1)
    memory_count = memory_pair.shape[0]
    code_lanes = 2 * HEAD_DIM
    code_block = jnp.pad(codes, ((0, 0), (0, memory_count * code_lanes - codes.shape[1])))
    arrived = lax.all_to_all(
        jnp.concatenate(
            [
                jnp.broadcast_to(memory_pair[None], (owners,) + memory_pair.shape),
                code_block.reshape(owners, memory_count, code_lanes),
            ],
            axis=2,
        ),
        "smp",
        split_axis=0,
        concat_axis=0,
        tiled=True,
    )
    memory_rows = arrived.reshape(1, -1, arrived.shape[2])
    code_back = (
        arrived[:, :, 2 * model_width :].reshape(owners, -1)[:, : codes.shape[1]].astype(jnp.int32)
    )
    served = code_back[:, : table.shape[1]] * code_base + code_back[:, table.shape[1] :]
    served_index = served[:, :token_total]
    memory_total = memory_rows.shape[1]
    read_mem = attend_kernel(
        queries.reshape(1, row_total, model_width),
        memory_rows,
        jnp.full((1,), memory_total, jnp.int32),
    ).reshape(row_total, model_width)
    hidden = (
        flat_state.astype(jnp.float32)
        + jnp.dot(read_mem, o1_weight, preferred_element_type=jnp.float32)
    ).astype(jnp.bfloat16)
    queries2 = jnp.dot(normed(hidden), q2_weight, preferred_element_type=jnp.float32).astype(
        jnp.bfloat16
    )
    queries2 = queries2.reshape(local_samples, latents, model_width)
    served_queries = lax.all_to_all(
        jnp.einsum(
            "ob,bld->old",
            (sample_pick[:, None] == jnp.arange(local_samples, dtype=jnp.int32)[None, :]).astype(
                jnp.bfloat16
            ),
            queries2,
            preferred_element_type=jnp.float32,
        ).astype(jnp.bfloat16),
        "smp",
        split_axis=0,
        concat_axis=0,
        tiled=True,
    )
    key_rows = key_table[served_index]
    value_rows = value_table[served_index]
    live_tokens = jnp.arange(token_total, dtype=jnp.int32)[None, :] < served[:, token_total:]
    served_read = attend_heads(
        served_queries.reshape(owners, latents, head_count, HEAD_DIM),
        key_rows,
        value_rows,
        live_tokens,
    )
    read_spike = lax.all_to_all(
        served_read.reshape(owners, latents, model_width),
        "smp",
        split_axis=0,
        concat_axis=0,
        tiled=True,
    )[owner_rank]
    result = hidden.astype(jnp.float32) + jnp.dot(
        read_spike.reshape(row_total, model_width), o2_weight, preferred_element_type=jnp.float32
    )
    return result.astype(jnp.bfloat16).reshape(local_samples, latents, model_width)


def solution(mesh):
    in_specs = (
        P(("grp", "smp"), None, None),
        P(("grp", "smp"), None),
        P(("grp", "smp")),
        P(("grp", "smp")),
        P("grp"),
        P(),
        P("smp", None, None),
        P(("grp", "smp"), None),
        P(("grp", "smp"), None),
        P(),
        P(),
        P(),
        P(),
        P(),
    )
    out_specs = P(("grp", "smp"), None, None)
    return jax.shard_map(
        per_device, mesh=mesh, in_specs=in_specs, out_specs=out_specs, check_vma=False
    )
```

```python
import jax
import jax.numpy as jnp
from jax import lax
from jax.experimental import pallas as pl
from jax.experimental.pallas import tpu as pltpu
from jax.sharding import PartitionSpec as P

HEAD_DIM = 64


masked_score = -1e30


def normed(values):
    wide = values.astype(jnp.float32)
    return (wide * lax.rsqrt(jnp.mean(wide * wide, axis=-1, keepdims=True) + 1e-05)).astype(
        jnp.bfloat16
    )


def attend(queries, key_rows, value_rows, live_tokens):
    samples, latents, head_count, head_size = queries.shape
    spike_scores = jnp.einsum(
        "blhd,bkhd->bhlk", queries, key_rows, preferred_element_type=jnp.float32
    ) * HEAD_DIM ** (-0.5)
    spike_scores = jnp.where(live_tokens[:, None, None, :], spike_scores, masked_score)
    spike_max = jnp.max(spike_scores, axis=-1, keepdims=True)
    spike_exp = jnp.exp(spike_scores - spike_max)
    denominator = jnp.transpose(jnp.sum(spike_exp, axis=-1, keepdims=True), (0, 2, 1, 3))
    spike_mix = (
        jnp.einsum(
            "bhlk,bkhd->blhd",
            spike_exp.astype(jnp.bfloat16),
            value_rows,
            preferred_element_type=jnp.float32,
        )
        / denominator
    )
    return spike_mix.reshape(samples, latents, head_count * head_size).astype(jnp.bfloat16)


def attend_heads(queries, key_rows, value_rows, live_tokens):
    samples, latents, head_count, head_size = queries.shape
    spike_scores = jnp.einsum(
        "blhd,bkhd->bhlk", queries, key_rows, preferred_element_type=jnp.float32
    ) * HEAD_DIM ** (-0.5)
    spike_scores = jnp.where(live_tokens[:, None, None, :], spike_scores, masked_score)
    spike_max = jnp.max(spike_scores, axis=-1, keepdims=True)
    spike_exp = jnp.exp(spike_scores - spike_max)
    denominator = jnp.transpose(jnp.sum(spike_exp, axis=-1, keepdims=True), (0, 2, 1, 3))
    spike_mix = (
        jnp.einsum(
            "bhlk,bkhd->blhd",
            spike_exp.astype(jnp.bfloat16),
            value_rows,
            preferred_element_type=jnp.float32,
        )
        / denominator
    )
    return spike_mix.reshape(samples, latents, head_count * head_size).astype(jnp.bfloat16)


def attend_pairs(queries, key_rows, value_rows, live_tokens):
    samples, latents, pair_count, pair_width = queries.shape
    halves = (
        lax.broadcasted_iota(jnp.int32, (2, pair_width), 1) // HEAD_DIM
        == lax.broadcasted_iota(jnp.int32, (2, pair_width), 0)
    )
    masked = jnp.where(halves[None, None, None], queries[:, :, :, None, :], 0).astype(jnp.bfloat16)
    scores = jnp.einsum(
        "blqje,btqe->bqjlt", masked, key_rows, preferred_element_type=jnp.float32
    ) * HEAD_DIM ** (-0.5)
    scores = jnp.where(live_tokens[:, None, None, None, :], scores, masked_score)
    row_max = jnp.max(scores, axis=-1, keepdims=True)
    exponent = jnp.exp(scores - row_max)
    denominator = jnp.sum(exponent, axis=-1, keepdims=True)
    mix = jnp.einsum(
        "bqjlt,btqe->bqjle",
        exponent.astype(jnp.bfloat16),
        value_rows,
        preferred_element_type=jnp.float32,
    ) / denominator
    mix = jnp.sum(jnp.where(halves[None, None, :, None, :], mix, 0.0), axis=2)
    return jnp.transpose(mix, (0, 2, 1, 3)).reshape(samples, latents, pair_count * pair_width).astype(
        jnp.bfloat16
    )


def attend_block(counts_ref, query_ref, key_ref, value_ref, out_ref):
    group = pl.program_id(0)
    latents = query_ref.shape[1]
    tokens = key_ref.shape[1]
    live = lax.broadcasted_iota(jnp.int32, (latents, tokens), 1) < counts_ref[group]
    first_head = lax.broadcasted_iota(jnp.int32, (1, 2 * HEAD_DIM), 1) < HEAD_DIM
    for pair in range(query_ref.shape[2] // (2 * HEAD_DIM)):
        cols = pl.ds(pair * 2 * HEAD_DIM, 2 * HEAD_DIM)
        query = query_ref[0, :, cols]
        key = key_ref[0, :, cols]
        value = value_ref[0, :, cols]
        mixes = []
        for half in (first_head, jnp.logical_not(first_head)):
            scores = lax.dot_general(
                jnp.where(half, query, jnp.zeros_like(query)),
                key,
                (((1,), (1,)), ((), ())),
                preferred_element_type=jnp.float32,
            ) * HEAD_DIM ** (-0.5)
            scores = jnp.where(live, scores, masked_score)
            row_max = jnp.max(scores, axis=1, keepdims=True)
            exponent = jnp.exp(scores - row_max)
            denominator = jnp.sum(exponent, axis=1, keepdims=True)
            mix = jnp.dot(
                exponent.astype(jnp.bfloat16), value, preferred_element_type=jnp.float32
            )
            mixes.append(mix / denominator)
        out_ref[0, :, cols] = jnp.where(first_head, mixes[0], mixes[1]).astype(jnp.bfloat16)


def attend_kernel(queries, key_value, counts):
    groups, latents, width = queries.shape
    tokens = key_value.shape[1]
    return pl.pallas_call(
        attend_block,
        grid_spec=pltpu.PrefetchScalarGridSpec(
            num_scalar_prefetch=1,
            grid=(groups,),
            in_specs=[
                pl.BlockSpec((1, latents, width), lambda g, c: (g, 0, 0)),
                pl.BlockSpec((1, tokens, width), lambda g, c: (g, 0, 0)),
                pl.BlockSpec((1, tokens, width), lambda g, c: (g, 0, 1)),
            ],
            out_specs=pl.BlockSpec((1, latents, width), lambda g, c: (g, 0, 0)),
        ),
        out_shape=jax.ShapeDtypeStruct((groups, latents, width), jnp.bfloat16),
    )(counts, queries, key_value, key_value)


def per_device(
    state,
    unit_slot,
    token_count,
    session,
    session_row,
    unit_count,
    panels,
    memory_key,
    memory_value,
    q1_weight,
    o1_weight,
    kv_weight,
    q2_weight,
    o2_weight,
):
    local_samples, latents, model_width = state.shape
    token_total = unit_slot.shape[1]
    owners = lax.axis_size("smp")
    sess_dev, unit_total = (panels.shape[0], panels.shape[1])
    head_count = model_width // HEAD_DIM
    session_ids = jnp.arange(session_row.shape[0], dtype=jnp.int32)
    panel_row = jnp.sum(
        jnp.where(session[:, None] == session_ids[None, :], session_row[None, :], 0), axis=1
    )
    unit_limit = jnp.sum(
        jnp.where(panel_row[:, None] == session_ids[None, :], unit_count[None, :], 0), axis=1
    )
    owner_rank = panel_row // sess_dev
    token_index = (panel_row % sess_dev * unit_total)[:, None] + unit_slot % unit_limit[:, None]
    slot_pick = owner_rank[None, :] == jnp.arange(owners, dtype=jnp.int32)[:, None]
    request = jnp.sum(jnp.where(slot_pick[:, :, None], token_index[None, :, :], 0), axis=1)
    count_pick = jnp.sum(jnp.where(slot_pick, token_count[None, :], 0), axis=1)
    sample_pick = jnp.sum(
        jnp.where(slot_pick, jnp.arange(local_samples, dtype=jnp.int32)[None, :], 0), axis=1
    )
    panel_table = panels.reshape(sess_dev * unit_total, model_width)
    panel_normed = normed(panel_table)
    key_table = jnp.einsum(
        "pc,chd->phd",
        panel_normed,
        kv_weight[:, :model_width].reshape(model_width, head_count // 2, 2 * HEAD_DIM),
        preferred_element_type=jnp.float32,
    ).astype(jnp.bfloat16)
    value_table = jnp.einsum(
        "pc,chd->phd",
        panel_normed,
        kv_weight[:, model_width:].reshape(model_width, head_count // 2, 2 * HEAD_DIM),
        preferred_element_type=jnp.float32,
    ).astype(jnp.bfloat16)
    row_total = local_samples * latents
    flat_state = state.reshape(row_total, model_width)
    queries = jnp.dot(normed(flat_state), q1_weight, preferred_element_type=jnp.float32).astype(
        jnp.bfloat16
    )
    table = jnp.concatenate([request, count_pick[:, None]], axis=1)
    code_base = 64
    codes = jnp.concatenate([table // code_base, table % code_base], axis=1).astype(jnp.bfloat16)
    memory_pair = jnp.concatenate([memory_key, memory_value], axis=1)
    memory_count = memory_pair.shape[0]
    code_lanes = 2 * HEAD_DIM
    code_block = jnp.pad(codes, ((0, 0), (0, memory_count * code_lanes - codes.shape[1])))
    arrived = lax.all_to_all(
        jnp.concatenate(
            [
                jnp.broadcast_to(memory_pair[None], (owners,) + memory_pair.shape),
                code_block.reshape(owners, memory_count, code_lanes),
            ],
            axis=2,
        ),
        "smp",
        split_axis=0,
        concat_axis=0,
        tiled=True,
    )
    memory_rows = arrived.reshape(1, -1, arrived.shape[2])
    code_back = (
        arrived[:, :, 2 * model_width :].reshape(owners, -1)[:, : codes.shape[1]].astype(jnp.int32)
    )
    served = code_back[:, : table.shape[1]] * code_base + code_back[:, table.shape[1] :]
    served_index = served[:, :token_total]
    memory_total = memory_rows.shape[1]
    read_mem = attend_kernel(
        queries.reshape(1, row_total, model_width),
        memory_rows,
        jnp.full((1,), memory_total, jnp.int32),
    ).reshape(row_total, model_width)
    hidden = (
        flat_state.astype(jnp.float32)
        + jnp.dot(read_mem, o1_weight, preferred_element_type=jnp.float32)
    ).astype(jnp.bfloat16)
    queries2 = jnp.dot(normed(hidden), q2_weight, preferred_element_type=jnp.float32).astype(
        jnp.bfloat16
    )
    queries2 = queries2.reshape(local_samples, latents, model_width)
    served_queries = lax.all_to_all(
        jnp.einsum(
            "ob,bld->old",
            (sample_pick[:, None] == jnp.arange(local_samples, dtype=jnp.int32)[None, :]).astype(
                jnp.bfloat16
            ),
            queries2,
            preferred_element_type=jnp.float32,
        ).astype(jnp.bfloat16),
        "smp",
        split_axis=0,
        concat_axis=0,
        tiled=True,
    )
    key_rows = key_table[served_index]
    value_rows = value_table[served_index]
    live_tokens = jnp.arange(token_total, dtype=jnp.int32)[None, :] < served[:, token_total:]
    served_read = attend_pairs(
        served_queries.reshape(owners, latents, head_count // 2, 2 * HEAD_DIM),
        key_rows.reshape(owners, token_total, head_count // 2, 2 * HEAD_DIM),
        value_rows.reshape(owners, token_total, head_count // 2, 2 * HEAD_DIM),
        live_tokens,
    )
    read_spike = lax.all_to_all(
        served_read.reshape(owners, latents, model_width),
        "smp",
        split_axis=0,
        concat_axis=0,
        tiled=True,
    )[owner_rank]
    result = hidden.astype(jnp.float32) + jnp.dot(
        read_spike.reshape(row_total, model_width), o2_weight, preferred_element_type=jnp.float32
    )
    return result.astype(jnp.bfloat16).reshape(local_samples, latents, model_width)


def solution(mesh):
    in_specs = (
        P(("grp", "smp"), None, None),
        P(("grp", "smp"), None),
        P(("grp", "smp")),
        P(("grp", "smp")),
        P("grp"),
        P(),
        P("smp", None, None),
        P(("grp", "smp"), None),
        P(("grp", "smp"), None),
        P(),
        P(),
        P(),
        P(),
        P(),
    )
    out_specs = P(("grp", "smp"), None, None)
    return jax.shard_map(
        per_device, mesh=mesh, in_specs=in_specs, out_specs=out_specs, check_vma=False
    )
```

```python
import jax
import jax.numpy as jnp
from jax import lax
from jax.experimental import pallas as pl
from jax.experimental.pallas import tpu as pltpu
from jax.sharding import PartitionSpec as P

HEAD_DIM = 64


masked_score = -1e30


def normed(values):
    wide = values.astype(jnp.float32)
    return (wide * lax.rsqrt(jnp.mean(wide * wide, axis=-1, keepdims=True) + 1e-05)).astype(
        jnp.bfloat16
    )


def attend(queries, key_rows, value_rows, live_tokens):
    samples, latents, head_count, head_size = queries.shape
    spike_scores = jnp.einsum(
        "blhd,bkhd->bhlk", queries, key_rows, preferred_element_type=jnp.float32
    ) * HEAD_DIM ** (-0.5)
    spike_scores = jnp.where(live_tokens[:, None, None, :], spike_scores, masked_score)
    spike_max = jnp.max(spike_scores, axis=-1, keepdims=True)
    spike_exp = jnp.exp(spike_scores - spike_max)
    denominator = jnp.transpose(jnp.sum(spike_exp, axis=-1, keepdims=True), (0, 2, 1, 3))
    spike_mix = (
        jnp.einsum(
            "bhlk,bkhd->blhd",
            spike_exp.astype(jnp.bfloat16),
            value_rows,
            preferred_element_type=jnp.float32,
        )
        / denominator
    )
    return spike_mix.reshape(samples, latents, head_count * head_size).astype(jnp.bfloat16)


def attend_heads(queries, key_rows, value_rows, live_tokens):
    samples, latents, head_count, head_size = queries.shape
    spike_scores = jnp.einsum(
        "blhd,bkhd->bhlk", queries, key_rows, preferred_element_type=jnp.float32
    ) * HEAD_DIM ** (-0.5)
    spike_scores = jnp.where(live_tokens[:, None, None, :], spike_scores, masked_score)
    spike_max = jnp.max(spike_scores, axis=-1, keepdims=True)
    spike_exp = jnp.exp(spike_scores - spike_max)
    denominator = jnp.transpose(jnp.sum(spike_exp, axis=-1, keepdims=True), (0, 2, 1, 3))
    spike_mix = (
        jnp.einsum(
            "bhlk,bkhd->blhd",
            spike_exp.astype(jnp.bfloat16),
            value_rows,
            preferred_element_type=jnp.float32,
        )
        / denominator
    )
    return spike_mix.reshape(samples, latents, head_count * head_size).astype(jnp.bfloat16)


def attend_pairs(queries, key_rows, value_rows, live_tokens):
    samples, latents, pair_count, pair_width = queries.shape
    halves = (
        lax.broadcasted_iota(jnp.int32, (2, pair_width), 1) // HEAD_DIM
        == lax.broadcasted_iota(jnp.int32, (2, pair_width), 0)
    )
    masked = jnp.where(halves[None, None, None], queries[:, :, :, None, :], 0).astype(jnp.bfloat16)
    scores = jnp.einsum(
        "blqje,btqe->bqjlt", masked, key_rows, preferred_element_type=jnp.float32
    ) * HEAD_DIM ** (-0.5)
    scores = jnp.where(live_tokens[:, None, None, None, :], scores, masked_score)
    row_max = jnp.max(scores, axis=-1, keepdims=True)
    exponent = jnp.exp(scores - row_max)
    denominator = jnp.sum(exponent, axis=-1, keepdims=True)
    mix = jnp.einsum(
        "bqjlt,btqe->bqjle",
        exponent.astype(jnp.bfloat16),
        value_rows,
        preferred_element_type=jnp.float32,
    ) / denominator
    mix = jnp.sum(jnp.where(halves[None, None, :, None, :], mix, 0.0), axis=2)
    return jnp.transpose(mix, (0, 2, 1, 3)).reshape(samples, latents, pair_count * pair_width).astype(
        jnp.bfloat16
    )


def attend_block(counts_ref, query_ref, key_ref, value_ref, out_ref):
    group = pl.program_id(0)
    latents = query_ref.shape[1]
    tokens = key_ref.shape[1]
    live = lax.broadcasted_iota(jnp.int32, (latents, tokens), 1) < counts_ref[group]
    first_head = lax.broadcasted_iota(jnp.int32, (1, 2 * HEAD_DIM), 1) < HEAD_DIM
    for pair in range(query_ref.shape[2] // (2 * HEAD_DIM)):
        cols = pl.ds(pair * 2 * HEAD_DIM, 2 * HEAD_DIM)
        query = query_ref[0, :, cols]
        key = key_ref[0, :, cols]
        value = value_ref[0, :, cols]
        mixes = []
        for half in (first_head, jnp.logical_not(first_head)):
            scores = lax.dot_general(
                jnp.where(half, query, jnp.zeros_like(query)),
                key,
                (((1,), (1,)), ((), ())),
                preferred_element_type=jnp.float32,
            ) * HEAD_DIM ** (-0.5)
            scores = jnp.where(live, scores, masked_score)
            row_max = jnp.max(scores, axis=1, keepdims=True)
            exponent = jnp.exp(scores - row_max)
            denominator = jnp.sum(exponent, axis=1, keepdims=True)
            mix = jnp.dot(
                exponent.astype(jnp.bfloat16), value, preferred_element_type=jnp.float32
            )
            mixes.append(mix / denominator)
        out_ref[0, :, cols] = jnp.where(first_head, mixes[0], mixes[1]).astype(jnp.bfloat16)


def attend_kernel(queries, key_value, counts):
    groups, latents, width = queries.shape
    tokens = key_value.shape[1]
    return pl.pallas_call(
        attend_block,
        grid_spec=pltpu.PrefetchScalarGridSpec(
            num_scalar_prefetch=1,
            grid=(groups,),
            in_specs=[
                pl.BlockSpec((1, latents, width), lambda g, c: (g, 0, 0)),
                pl.BlockSpec((1, tokens, width), lambda g, c: (g, 0, 0)),
                pl.BlockSpec((1, tokens, width), lambda g, c: (g, 0, 1)),
            ],
            out_specs=pl.BlockSpec((1, latents, width), lambda g, c: (g, 0, 0)),
        ),
        out_shape=jax.ShapeDtypeStruct((groups, latents, width), jnp.bfloat16),
    )(counts, queries, key_value, key_value)


def per_device(
    state,
    unit_slot,
    token_count,
    session,
    session_row,
    unit_count,
    panels,
    memory_key,
    memory_value,
    q1_weight,
    o1_weight,
    kv_weight,
    q2_weight,
    o2_weight,
):
    local_samples, latents, model_width = state.shape
    token_total = unit_slot.shape[1]
    owners = lax.axis_size("smp")
    sess_dev, unit_total = (panels.shape[0], panels.shape[1])
    head_count = model_width // HEAD_DIM
    session_ids = jnp.arange(session_row.shape[0], dtype=jnp.int32)
    panel_row = jnp.sum(
        jnp.where(session[:, None] == session_ids[None, :], session_row[None, :], 0), axis=1
    )
    unit_limit = jnp.sum(
        jnp.where(panel_row[:, None] == session_ids[None, :], unit_count[None, :], 0), axis=1
    )
    owner_rank = panel_row // sess_dev
    token_index = (panel_row % sess_dev * unit_total)[:, None] + unit_slot % unit_limit[:, None]
    slot_pick = owner_rank[None, :] == jnp.arange(owners, dtype=jnp.int32)[:, None]
    request = jnp.sum(jnp.where(slot_pick[:, :, None], token_index[None, :, :], 0), axis=1)
    count_pick = jnp.sum(jnp.where(slot_pick, token_count[None, :], 0), axis=1)
    sample_pick = jnp.sum(
        jnp.where(slot_pick, jnp.arange(local_samples, dtype=jnp.int32)[None, :], 0), axis=1
    )
    panel_table = panels.reshape(sess_dev * unit_total, model_width)
    panel_normed = normed(panel_table)
    kv_flat = jnp.dot(panel_normed, kv_weight, preferred_element_type=jnp.float32).astype(
        jnp.bfloat16
    )
    panel_total = kv_flat.shape[0]
    key_table = kv_flat[:, :model_width].reshape(panel_total, head_count // 2, 2 * HEAD_DIM)
    value_table = kv_flat[:, model_width:].reshape(panel_total, head_count // 2, 2 * HEAD_DIM)
    row_total = local_samples * latents
    flat_state = state.reshape(row_total, model_width)
    queries = jnp.dot(normed(flat_state), q1_weight, preferred_element_type=jnp.float32).astype(
        jnp.bfloat16
    )
    table = jnp.concatenate([request, count_pick[:, None]], axis=1)
    code_base = 64
    codes = jnp.concatenate([table // code_base, table % code_base], axis=1).astype(jnp.bfloat16)
    memory_pair = jnp.concatenate([memory_key, memory_value], axis=1)
    memory_count = memory_pair.shape[0]
    code_lanes = 2 * HEAD_DIM
    code_block = jnp.pad(codes, ((0, 0), (0, memory_count * code_lanes - codes.shape[1])))
    arrived = lax.all_to_all(
        jnp.concatenate(
            [
                jnp.broadcast_to(memory_pair[None], (owners,) + memory_pair.shape),
                code_block.reshape(owners, memory_count, code_lanes),
            ],
            axis=2,
        ),
        "smp",
        split_axis=0,
        concat_axis=0,
        tiled=True,
    )
    memory_rows = arrived.reshape(1, -1, arrived.shape[2])
    code_back = (
        arrived[:, :, 2 * model_width :].reshape(owners, -1)[:, : codes.shape[1]].astype(jnp.int32)
    )
    served = code_back[:, : table.shape[1]] * code_base + code_back[:, table.shape[1] :]
    served_index = served[:, :token_total]
    memory_total = memory_rows.shape[1]
    read_mem = attend_kernel(
        queries.reshape(1, row_total, model_width),
        memory_rows,
        jnp.full((1,), memory_total, jnp.int32),
    ).reshape(row_total, model_width)
    hidden = (
        flat_state.astype(jnp.float32)
        + jnp.dot(read_mem, o1_weight, preferred_element_type=jnp.float32)
    ).astype(jnp.bfloat16)
    queries2 = jnp.dot(normed(hidden), q2_weight, preferred_element_type=jnp.float32).astype(
        jnp.bfloat16
    )
    queries2 = queries2.reshape(local_samples, latents, model_width)
    served_queries = lax.all_to_all(
        jnp.einsum(
            "ob,bld->old",
            (sample_pick[:, None] == jnp.arange(local_samples, dtype=jnp.int32)[None, :]).astype(
                jnp.bfloat16
            ),
            queries2,
            preferred_element_type=jnp.float32,
        ).astype(jnp.bfloat16),
        "smp",
        split_axis=0,
        concat_axis=0,
        tiled=True,
    )
    key_rows = key_table[served_index]
    value_rows = value_table[served_index]
    live_tokens = jnp.arange(token_total, dtype=jnp.int32)[None, :] < served[:, token_total:]
    served_read = attend_pairs(
        served_queries.reshape(owners, latents, head_count // 2, 2 * HEAD_DIM),
        key_rows.reshape(owners, token_total, head_count // 2, 2 * HEAD_DIM),
        value_rows.reshape(owners, token_total, head_count // 2, 2 * HEAD_DIM),
        live_tokens,
    )
    read_spike = lax.all_to_all(
        served_read.reshape(owners, latents, model_width),
        "smp",
        split_axis=0,
        concat_axis=0,
        tiled=True,
    )[owner_rank]
    result = hidden.astype(jnp.float32) + jnp.dot(
        read_spike.reshape(row_total, model_width), o2_weight, preferred_element_type=jnp.float32
    )
    return result.astype(jnp.bfloat16).reshape(local_samples, latents, model_width)


def solution(mesh):
    in_specs = (
        P(("grp", "smp"), None, None),
        P(("grp", "smp"), None),
        P(("grp", "smp")),
        P(("grp", "smp")),
        P("grp"),
        P(),
        P("smp", None, None),
        P(("grp", "smp"), None),
        P(("grp", "smp"), None),
        P(),
        P(),
        P(),
        P(),
        P(),
    )
    out_specs = P(("grp", "smp"), None, None)
    return jax.shard_map(
        per_device, mesh=mesh, in_specs=in_specs, out_specs=out_specs, check_vma=False
    )
```

```python
import jax
import jax.numpy as jnp
from jax import lax
from jax.experimental import pallas as pl
from jax.experimental.pallas import tpu as pltpu
from jax.sharding import PartitionSpec as P

HEAD_DIM = 64


masked_score = -1e30


def normed(values):
    wide = values.astype(jnp.float32)
    return (wide * lax.rsqrt(jnp.mean(wide * wide, axis=-1, keepdims=True) + 1e-05)).astype(
        jnp.bfloat16
    )


def attend(queries, key_rows, value_rows, live_tokens):
    samples, latents, head_count, head_size = queries.shape
    spike_scores = jnp.einsum(
        "blhd,bkhd->bhlk", queries, key_rows, preferred_element_type=jnp.float32
    ) * HEAD_DIM ** (-0.5)
    spike_scores = jnp.where(live_tokens[:, None, None, :], spike_scores, masked_score)
    spike_max = jnp.max(spike_scores, axis=-1, keepdims=True)
    spike_exp = jnp.exp(spike_scores - spike_max)
    denominator = jnp.transpose(jnp.sum(spike_exp, axis=-1, keepdims=True), (0, 2, 1, 3))
    spike_mix = (
        jnp.einsum(
            "bhlk,bkhd->blhd",
            spike_exp.astype(jnp.bfloat16),
            value_rows,
            preferred_element_type=jnp.float32,
        )
        / denominator
    )
    return spike_mix.reshape(samples, latents, head_count * head_size).astype(jnp.bfloat16)


def attend_heads(queries, key_rows, value_rows, live_tokens):
    samples, latents, head_count, head_size = queries.shape
    spike_scores = jnp.einsum(
        "blhd,bkhd->bhlk", queries, key_rows, preferred_element_type=jnp.float32
    ) * HEAD_DIM ** (-0.5)
    spike_scores = jnp.where(live_tokens[:, None, None, :], spike_scores, masked_score)
    spike_max = jnp.max(spike_scores, axis=-1, keepdims=True)
    spike_exp = jnp.exp(spike_scores - spike_max)
    denominator = jnp.transpose(jnp.sum(spike_exp, axis=-1, keepdims=True), (0, 2, 1, 3))
    spike_mix = (
        jnp.einsum(
            "bhlk,bkhd->blhd",
            spike_exp.astype(jnp.bfloat16),
            value_rows,
            preferred_element_type=jnp.float32,
        )
        / denominator
    )
    return spike_mix.reshape(samples, latents, head_count * head_size).astype(jnp.bfloat16)


def attend_pairs(queries, key_rows, value_rows, live_tokens):
    samples, latents, pair_count, pair_width = queries.shape
    halves = (
        lax.broadcasted_iota(jnp.int32, (2, pair_width), 1) // HEAD_DIM
        == lax.broadcasted_iota(jnp.int32, (2, pair_width), 0)
    )
    masked = jnp.where(halves[None, None, None], queries[:, :, :, None, :], 0).astype(jnp.bfloat16)
    scores = jnp.einsum(
        "blqje,btqe->bqjlt", masked, key_rows, preferred_element_type=jnp.float32
    ) * HEAD_DIM ** (-0.5)
    scores = jnp.where(live_tokens[:, None, None, None, :], scores, masked_score)
    row_max = jnp.max(scores, axis=-1, keepdims=True)
    exponent = jnp.exp(scores - row_max)
    denominator = jnp.sum(exponent, axis=-1, keepdims=True)
    mix = jnp.einsum(
        "bqjlt,btqe->bqjle",
        exponent.astype(jnp.bfloat16),
        value_rows,
        preferred_element_type=jnp.float32,
    ) / denominator
    mix = jnp.sum(jnp.where(halves[None, None, :, None, :], mix, 0.0), axis=2)
    return jnp.transpose(mix, (0, 2, 1, 3)).reshape(samples, latents, pair_count * pair_width).astype(
        jnp.bfloat16
    )


def attend_block(counts_ref, query_ref, key_ref, value_ref, out_ref):
    group = pl.program_id(0)
    latents = query_ref.shape[1]
    tokens = key_ref.shape[1]
    live = lax.broadcasted_iota(jnp.int32, (latents, tokens), 1) < counts_ref[group]
    first_head = lax.broadcasted_iota(jnp.int32, (1, 2 * HEAD_DIM), 1) < HEAD_DIM
    for pair in range(query_ref.shape[2] // (2 * HEAD_DIM)):
        cols = pl.ds(pair * 2 * HEAD_DIM, 2 * HEAD_DIM)
        query = query_ref[0, :, cols]
        key = key_ref[0, :, cols]
        value = value_ref[0, :, cols]
        mixes = []
        for half in (first_head, jnp.logical_not(first_head)):
            scores = lax.dot_general(
                jnp.where(half, query, jnp.zeros_like(query)),
                key,
                (((1,), (1,)), ((), ())),
                preferred_element_type=jnp.float32,
            ) * HEAD_DIM ** (-0.5)
            scores = jnp.where(live, scores, masked_score)
            row_max = jnp.max(scores, axis=1, keepdims=True)
            exponent = jnp.exp(scores - row_max)
            denominator = jnp.sum(exponent, axis=1, keepdims=True)
            mix = jnp.dot(
                exponent.astype(jnp.bfloat16), value, preferred_element_type=jnp.float32
            )
            mixes.append(mix / denominator)
        out_ref[0, :, cols] = jnp.where(first_head, mixes[0], mixes[1]).astype(jnp.bfloat16)


def attend_kernel(queries, key_value, counts):
    groups, latents, width = queries.shape
    tokens = key_value.shape[1]
    return pl.pallas_call(
        attend_block,
        grid_spec=pltpu.PrefetchScalarGridSpec(
            num_scalar_prefetch=1,
            grid=(groups,),
            in_specs=[
                pl.BlockSpec((1, latents, width), lambda g, c: (g, 0, 0)),
                pl.BlockSpec((1, tokens, width), lambda g, c: (g, 0, 0)),
                pl.BlockSpec((1, tokens, width), lambda g, c: (g, 0, 1)),
            ],
            out_specs=pl.BlockSpec((1, latents, width), lambda g, c: (g, 0, 0)),
        ),
        out_shape=jax.ShapeDtypeStruct((groups, latents, width), jnp.bfloat16),
    )(counts, queries, key_value, key_value)


def per_device(
    state,
    unit_slot,
    token_count,
    session,
    session_row,
    unit_count,
    panels,
    memory_key,
    memory_value,
    q1_weight,
    o1_weight,
    kv_weight,
    q2_weight,
    o2_weight,
):
    local_samples, latents, model_width = state.shape
    token_total = unit_slot.shape[1]
    owners = lax.axis_size("smp")
    sess_dev, unit_total = (panels.shape[0], panels.shape[1])
    head_count = model_width // HEAD_DIM
    session_ids = jnp.arange(session_row.shape[0], dtype=jnp.int32)
    panel_row = jnp.sum(
        jnp.where(session[:, None] == session_ids[None, :], session_row[None, :], 0), axis=1
    )
    unit_limit = jnp.sum(
        jnp.where(panel_row[:, None] == session_ids[None, :], unit_count[None, :], 0), axis=1
    )
    owner_rank = panel_row // sess_dev
    token_index = (panel_row % sess_dev * unit_total)[:, None] + unit_slot % unit_limit[:, None]
    slot_pick = owner_rank[None, :] == jnp.arange(owners, dtype=jnp.int32)[:, None]
    request = jnp.sum(jnp.where(slot_pick[:, :, None], token_index[None, :, :], 0), axis=1)
    count_pick = jnp.sum(jnp.where(slot_pick, token_count[None, :], 0), axis=1)
    sample_pick = jnp.sum(
        jnp.where(slot_pick, jnp.arange(local_samples, dtype=jnp.int32)[None, :], 0), axis=1
    )
    panel_table = panels.reshape(sess_dev * unit_total, model_width)
    panel_normed = normed(panel_table)
    kv_flat = jnp.dot(panel_normed, kv_weight, preferred_element_type=jnp.float32).astype(
        jnp.bfloat16
    )
    panel_total = kv_flat.shape[0]
    kv_table = kv_flat.reshape(panel_total, head_count, 2 * HEAD_DIM)
    row_total = local_samples * latents
    flat_state = state.reshape(row_total, model_width)
    queries = jnp.dot(normed(flat_state), q1_weight, preferred_element_type=jnp.float32).astype(
        jnp.bfloat16
    )
    table = jnp.concatenate([request, count_pick[:, None]], axis=1)
    code_base = 64
    codes = jnp.concatenate([table // code_base, table % code_base], axis=1).astype(jnp.bfloat16)
    memory_pair = jnp.concatenate([memory_key, memory_value], axis=1)
    memory_count = memory_pair.shape[0]
    code_lanes = 2 * HEAD_DIM
    code_block = jnp.pad(codes, ((0, 0), (0, memory_count * code_lanes - codes.shape[1])))
    arrived = lax.all_to_all(
        jnp.concatenate(
            [
                jnp.broadcast_to(memory_pair[None], (owners,) + memory_pair.shape),
                code_block.reshape(owners, memory_count, code_lanes),
            ],
            axis=2,
        ),
        "smp",
        split_axis=0,
        concat_axis=0,
        tiled=True,
    )
    memory_rows = arrived.reshape(1, -1, arrived.shape[2])
    code_back = (
        arrived[:, :, 2 * model_width :].reshape(owners, -1)[:, : codes.shape[1]].astype(jnp.int32)
    )
    served = code_back[:, : table.shape[1]] * code_base + code_back[:, table.shape[1] :]
    served_index = served[:, :token_total]
    memory_total = memory_rows.shape[1]
    read_mem = attend_kernel(
        queries.reshape(1, row_total, model_width),
        memory_rows,
        jnp.full((1,), memory_total, jnp.int32),
    ).reshape(row_total, model_width)
    hidden = (
        flat_state.astype(jnp.float32)
        + jnp.dot(read_mem, o1_weight, preferred_element_type=jnp.float32)
    ).astype(jnp.bfloat16)
    queries2 = jnp.dot(normed(hidden), q2_weight, preferred_element_type=jnp.float32).astype(
        jnp.bfloat16
    )
    queries2 = queries2.reshape(local_samples, latents, model_width)
    served_queries = lax.all_to_all(
        jnp.einsum(
            "ob,bld->old",
            (sample_pick[:, None] == jnp.arange(local_samples, dtype=jnp.int32)[None, :]).astype(
                jnp.bfloat16
            ),
            queries2,
            preferred_element_type=jnp.float32,
        ).astype(jnp.bfloat16),
        "smp",
        split_axis=0,
        concat_axis=0,
        tiled=True,
    )
    kv_rows = kv_table[served_index]
    key_rows = kv_rows[:, :, : head_count // 2]
    value_rows = kv_rows[:, :, head_count // 2 :]
    live_tokens = jnp.arange(token_total, dtype=jnp.int32)[None, :] < served[:, token_total:]
    served_read = attend_pairs(
        served_queries.reshape(owners, latents, head_count // 2, 2 * HEAD_DIM),
        key_rows.reshape(owners, token_total, head_count // 2, 2 * HEAD_DIM),
        value_rows.reshape(owners, token_total, head_count // 2, 2 * HEAD_DIM),
        live_tokens,
    )
    read_spike = lax.all_to_all(
        served_read.reshape(owners, latents, model_width),
        "smp",
        split_axis=0,
        concat_axis=0,
        tiled=True,
    )[owner_rank]
    result = hidden.astype(jnp.float32) + jnp.dot(
        read_spike.reshape(row_total, model_width), o2_weight, preferred_element_type=jnp.float32
    )
    return result.astype(jnp.bfloat16).reshape(local_samples, latents, model_width)


def solution(mesh):
    in_specs = (
        P(("grp", "smp"), None, None),
        P(("grp", "smp"), None),
        P(("grp", "smp")),
        P(("grp", "smp")),
        P("grp"),
        P(),
        P("smp", None, None),
        P(("grp", "smp"), None),
        P(("grp", "smp"), None),
        P(),
        P(),
        P(),
        P(),
        P(),
    )
    out_specs = P(("grp", "smp"), None, None)
    return jax.shard_map(
        per_device, mesh=mesh, in_specs=in_specs, out_specs=out_specs, check_vma=False
    )
```

```python
import jax
import jax.numpy as jnp
from jax import lax
from jax.experimental import pallas as pl
from jax.experimental.pallas import tpu as pltpu
from jax.sharding import PartitionSpec as P

HEAD_DIM = 64


masked_score = -1e30


def normed(values):
    wide = values.astype(jnp.float32)
    return (wide * lax.rsqrt(jnp.mean(wide * wide, axis=-1, keepdims=True) + 1e-05)).astype(
        jnp.bfloat16
    )


def attend(queries, key_rows, value_rows, live_tokens):
    samples, latents, head_count, head_size = queries.shape
    spike_scores = jnp.einsum(
        "blhd,bkhd->bhlk", queries, key_rows, preferred_element_type=jnp.float32
    ) * HEAD_DIM ** (-0.5)
    spike_scores = jnp.where(live_tokens[:, None, None, :], spike_scores, masked_score)
    spike_max = jnp.max(spike_scores, axis=-1, keepdims=True)
    spike_exp = jnp.exp(spike_scores - spike_max)
    denominator = jnp.transpose(jnp.sum(spike_exp, axis=-1, keepdims=True), (0, 2, 1, 3))
    spike_mix = (
        jnp.einsum(
            "bhlk,bkhd->blhd",
            spike_exp.astype(jnp.bfloat16),
            value_rows,
            preferred_element_type=jnp.float32,
        )
        / denominator
    )
    return spike_mix.reshape(samples, latents, head_count * head_size).astype(jnp.bfloat16)


def attend_heads(queries, key_rows, value_rows, live_tokens):
    samples, latents, head_count, head_size = queries.shape
    spike_scores = jnp.einsum(
        "blhd,bkhd->bhlk", queries, key_rows, preferred_element_type=jnp.float32
    ) * HEAD_DIM ** (-0.5)
    spike_scores = jnp.where(live_tokens[:, None, None, :], spike_scores, masked_score)
    spike_max = jnp.max(spike_scores, axis=-1, keepdims=True)
    spike_exp = jnp.exp(spike_scores - spike_max)
    denominator = jnp.transpose(jnp.sum(spike_exp, axis=-1, keepdims=True), (0, 2, 1, 3))
    spike_mix = (
        jnp.einsum(
            "bhlk,bkhd->blhd",
            spike_exp.astype(jnp.bfloat16),
            value_rows,
            preferred_element_type=jnp.float32,
        )
        / denominator
    )
    return spike_mix.reshape(samples, latents, head_count * head_size).astype(jnp.bfloat16)


def attend_pairs(queries, key_rows, value_rows, live_tokens):
    samples, latents, pair_count, pair_width = queries.shape
    halves = (
        lax.broadcasted_iota(jnp.int32, (2, pair_width), 1) // HEAD_DIM
        == lax.broadcasted_iota(jnp.int32, (2, pair_width), 0)
    )
    masked = jnp.where(halves[None, None, None], queries[:, :, :, None, :], 0).astype(jnp.bfloat16)
    scores = jnp.einsum(
        "blqje,btqe->bqjlt", masked, key_rows, preferred_element_type=jnp.float32
    ) * HEAD_DIM ** (-0.5)
    scores = jnp.where(live_tokens[:, None, None, None, :], scores, masked_score)
    row_max = jnp.max(scores, axis=-1, keepdims=True)
    exponent = jnp.exp(scores - row_max)
    denominator = jnp.sum(exponent, axis=-1, keepdims=True)
    mix = jnp.einsum(
        "bqjlt,btqe->bqjle",
        exponent.astype(jnp.bfloat16),
        value_rows,
        preferred_element_type=jnp.float32,
    ) / denominator
    mix = jnp.sum(jnp.where(halves[None, None, :, None, :], mix, 0.0), axis=2)
    return jnp.transpose(mix, (0, 2, 1, 3)).reshape(samples, latents, pair_count * pair_width).astype(
        jnp.bfloat16
    )


def attend_block(counts_ref, query_ref, key_ref, value_ref, out_ref):
    group = pl.program_id(0)
    latents = query_ref.shape[1]
    tokens = key_ref.shape[1]
    live = lax.broadcasted_iota(jnp.int32, (latents, tokens), 1) < counts_ref[group]
    first_head = lax.broadcasted_iota(jnp.int32, (1, 2 * HEAD_DIM), 1) < HEAD_DIM
    for pair in range(query_ref.shape[2] // (2 * HEAD_DIM)):
        cols = pl.ds(pair * 2 * HEAD_DIM, 2 * HEAD_DIM)
        query = query_ref[0, :, cols]
        key = key_ref[0, :, cols]
        value = value_ref[0, :, cols]
        mixes = []
        for half in (first_head, jnp.logical_not(first_head)):
            scores = lax.dot_general(
                jnp.where(half, query, jnp.zeros_like(query)),
                key,
                (((1,), (1,)), ((), ())),
                preferred_element_type=jnp.float32,
            ) * HEAD_DIM ** (-0.5)
            scores = jnp.where(live, scores, masked_score)
            row_max = jnp.max(scores, axis=1, keepdims=True)
            exponent = jnp.exp(scores - row_max)
            denominator = jnp.sum(exponent, axis=1, keepdims=True)
            mix = jnp.dot(
                exponent.astype(jnp.bfloat16), value, preferred_element_type=jnp.float32
            )
            mixes.append(mix / denominator)
        out_ref[0, :, cols] = jnp.where(first_head, mixes[0], mixes[1]).astype(jnp.bfloat16)


def attend_kernel(queries, key_value, counts):
    groups, latents, width = queries.shape
    tokens = key_value.shape[1]
    return pl.pallas_call(
        attend_block,
        grid_spec=pltpu.PrefetchScalarGridSpec(
            num_scalar_prefetch=1,
            grid=(groups,),
            in_specs=[
                pl.BlockSpec((1, latents, width), lambda g, c: (g, 0, 0)),
                pl.BlockSpec((1, tokens, width), lambda g, c: (g, 0, 0)),
                pl.BlockSpec((1, tokens, width), lambda g, c: (g, 0, 1)),
            ],
            out_specs=pl.BlockSpec((1, latents, width), lambda g, c: (g, 0, 0)),
        ),
        out_shape=jax.ShapeDtypeStruct((groups, latents, width), jnp.bfloat16),
    )(counts, queries, key_value, key_value)


def per_device(
    state,
    unit_slot,
    token_count,
    session,
    session_row,
    unit_count,
    panels,
    memory_key,
    memory_value,
    q1_weight,
    o1_weight,
    kv_weight,
    q2_weight,
    o2_weight,
):
    local_samples, latents, model_width = state.shape
    token_total = unit_slot.shape[1]
    owners = lax.axis_size("smp")
    sess_dev, unit_total = (panels.shape[0], panels.shape[1])
    head_count = model_width // HEAD_DIM
    panel_row = session_row[session]
    unit_limit = unit_count[panel_row]
    owner_rank = panel_row // sess_dev
    token_index = (panel_row % sess_dev * unit_total)[:, None] + unit_slot % unit_limit[:, None]
    slot_pick = owner_rank[None, :] == jnp.arange(owners, dtype=jnp.int32)[:, None]
    request = jnp.sum(jnp.where(slot_pick[:, :, None], token_index[None, :, :], 0), axis=1)
    count_pick = jnp.sum(jnp.where(slot_pick, token_count[None, :], 0), axis=1)
    sample_pick = jnp.sum(
        jnp.where(slot_pick, jnp.arange(local_samples, dtype=jnp.int32)[None, :], 0), axis=1
    )
    panel_table = panels.reshape(sess_dev * unit_total, model_width)
    panel_normed = normed(panel_table)
    kv_flat = jnp.dot(panel_normed, kv_weight, preferred_element_type=jnp.float32).astype(
        jnp.bfloat16
    )
    panel_total = kv_flat.shape[0]
    kv_table = kv_flat.reshape(panel_total, head_count, 2 * HEAD_DIM)
    row_total = local_samples * latents
    flat_state = state.reshape(row_total, model_width)
    queries = jnp.dot(normed(flat_state), q1_weight, preferred_element_type=jnp.float32).astype(
        jnp.bfloat16
    )
    table = jnp.concatenate([request, count_pick[:, None]], axis=1)
    code_base = 64
    codes = jnp.concatenate([table // code_base, table % code_base], axis=1).astype(jnp.bfloat16)
    memory_pair = jnp.concatenate([memory_key, memory_value], axis=1)
    memory_count = memory_pair.shape[0]
    code_lanes = 2 * HEAD_DIM
    code_block = jnp.pad(codes, ((0, 0), (0, memory_count * code_lanes - codes.shape[1])))
    arrived = lax.all_to_all(
        jnp.concatenate(
            [
                jnp.broadcast_to(memory_pair[None], (owners,) + memory_pair.shape),
                code_block.reshape(owners, memory_count, code_lanes),
            ],
            axis=2,
        ),
        "smp",
        split_axis=0,
        concat_axis=0,
        tiled=True,
    )
    memory_rows = arrived.reshape(1, -1, arrived.shape[2])
    code_back = (
        arrived[:, :, 2 * model_width :].reshape(owners, -1)[:, : codes.shape[1]].astype(jnp.int32)
    )
    served = code_back[:, : table.shape[1]] * code_base + code_back[:, table.shape[1] :]
    served_index = served[:, :token_total]
    memory_total = memory_rows.shape[1]
    read_mem = attend_kernel(
        queries.reshape(1, row_total, model_width),
        memory_rows,
        jnp.full((1,), memory_total, jnp.int32),
    ).reshape(row_total, model_width)
    hidden = (
        flat_state.astype(jnp.float32)
        + jnp.dot(read_mem, o1_weight, preferred_element_type=jnp.float32)
    ).astype(jnp.bfloat16)
    queries2 = jnp.dot(normed(hidden), q2_weight, preferred_element_type=jnp.float32).astype(
        jnp.bfloat16
    )
    queries2 = queries2.reshape(local_samples, latents, model_width)
    served_queries = lax.all_to_all(
        jnp.einsum(
            "ob,bld->old",
            (sample_pick[:, None] == jnp.arange(local_samples, dtype=jnp.int32)[None, :]).astype(
                jnp.bfloat16
            ),
            queries2,
            preferred_element_type=jnp.float32,
        ).astype(jnp.bfloat16),
        "smp",
        split_axis=0,
        concat_axis=0,
        tiled=True,
    )
    kv_rows = kv_table[served_index]
    key_rows = kv_rows[:, :, : head_count // 2]
    value_rows = kv_rows[:, :, head_count // 2 :]
    live_tokens = jnp.arange(token_total, dtype=jnp.int32)[None, :] < served[:, token_total:]
    served_read = attend_pairs(
        served_queries.reshape(owners, latents, head_count // 2, 2 * HEAD_DIM),
        key_rows.reshape(owners, token_total, head_count // 2, 2 * HEAD_DIM),
        value_rows.reshape(owners, token_total, head_count // 2, 2 * HEAD_DIM),
        live_tokens,
    )
    read_spike = lax.all_to_all(
        served_read.reshape(owners, latents, model_width),
        "smp",
        split_axis=0,
        concat_axis=0,
        tiled=True,
    )[owner_rank]
    result = hidden.astype(jnp.float32) + jnp.dot(
        read_spike.reshape(row_total, model_width), o2_weight, preferred_element_type=jnp.float32
    )
    return result.astype(jnp.bfloat16).reshape(local_samples, latents, model_width)


def solution(mesh):
    in_specs = (
        P(("grp", "smp"), None, None),
        P(("grp", "smp"), None),
        P(("grp", "smp")),
        P(("grp", "smp")),
        P("grp"),
        P(),
        P("smp", None, None),
        P(("grp", "smp"), None),
        P(("grp", "smp"), None),
        P(),
        P(),
        P(),
        P(),
        P(),
    )
    out_specs = P(("grp", "smp"), None, None)
    return jax.shard_map(
        per_device, mesh=mesh, in_specs=in_specs, out_specs=out_specs, check_vma=False
    )
```

```python
import jax
import jax.numpy as jnp
from jax import lax
from jax.experimental import pallas as pl
from jax.experimental.pallas import tpu as pltpu
from jax.sharding import PartitionSpec as P

HEAD_DIM = 64


masked_score = -1e30


def normed(values):
    wide = values.astype(jnp.float32)
    return (wide * lax.rsqrt(jnp.mean(wide * wide, axis=-1, keepdims=True) + 1e-05)).astype(
        jnp.bfloat16
    )


def attend(queries, key_rows, value_rows, live_tokens):
    samples, latents, head_count, head_size = queries.shape
    spike_scores = jnp.einsum(
        "blhd,bkhd->bhlk", queries, key_rows, preferred_element_type=jnp.float32
    ) * HEAD_DIM ** (-0.5)
    spike_scores = jnp.where(live_tokens[:, None, None, :], spike_scores, masked_score)
    spike_max = jnp.max(spike_scores, axis=-1, keepdims=True)
    spike_exp = jnp.exp(spike_scores - spike_max)
    denominator = jnp.transpose(jnp.sum(spike_exp, axis=-1, keepdims=True), (0, 2, 1, 3))
    spike_mix = (
        jnp.einsum(
            "bhlk,bkhd->blhd",
            spike_exp.astype(jnp.bfloat16),
            value_rows,
            preferred_element_type=jnp.float32,
        )
        / denominator
    )
    return spike_mix.reshape(samples, latents, head_count * head_size).astype(jnp.bfloat16)


def attend_heads(queries, key_rows, value_rows, live_tokens):
    samples, latents, head_count, head_size = queries.shape
    spike_scores = jnp.einsum(
        "blhd,bkhd->bhlk", queries, key_rows, preferred_element_type=jnp.float32
    ) * HEAD_DIM ** (-0.5)
    spike_scores = jnp.where(live_tokens[:, None, None, :], spike_scores, masked_score)
    spike_max = jnp.max(spike_scores, axis=-1, keepdims=True)
    spike_exp = jnp.exp(spike_scores - spike_max)
    denominator = jnp.transpose(jnp.sum(spike_exp, axis=-1, keepdims=True), (0, 2, 1, 3))
    spike_mix = (
        jnp.einsum(
            "bhlk,bkhd->blhd",
            spike_exp.astype(jnp.bfloat16),
            value_rows,
            preferred_element_type=jnp.float32,
        )
        / denominator
    )
    return spike_mix.reshape(samples, latents, head_count * head_size).astype(jnp.bfloat16)


def attend_pairs(queries, key_rows, value_rows, live_tokens):
    samples, latents, pair_count, pair_width = queries.shape
    halves = (
        lax.broadcasted_iota(jnp.int32, (2, pair_width), 1) // HEAD_DIM
        == lax.broadcasted_iota(jnp.int32, (2, pair_width), 0)
    )
    masked = jnp.where(halves[None, None, None], queries[:, :, :, None, :], 0).astype(jnp.bfloat16)
    scores = jnp.einsum(
        "blqje,btqe->bqjlt", masked, key_rows, preferred_element_type=jnp.float32
    ) * HEAD_DIM ** (-0.5)
    scores = jnp.where(live_tokens[:, None, None, None, :], scores, masked_score)
    row_max = jnp.max(scores, axis=-1, keepdims=True)
    exponent = jnp.exp(scores - row_max)
    denominator = jnp.sum(exponent, axis=-1, keepdims=True)
    mix = jnp.einsum(
        "bqjlt,btqe->bqjle",
        exponent.astype(jnp.bfloat16),
        value_rows,
        preferred_element_type=jnp.float32,
    ) / denominator
    mix = jnp.sum(jnp.where(halves[None, None, :, None, :], mix, 0.0), axis=2)
    return jnp.transpose(mix, (0, 2, 1, 3)).reshape(samples, latents, pair_count * pair_width).astype(
        jnp.bfloat16
    )


def attend_stacked(queries, kv_rows, live_tokens):
    samples, latents, pair_count, pair_width = queries.shape
    halves = (
        lax.broadcasted_iota(jnp.int32, (2, pair_width), 1) // HEAD_DIM
        == lax.broadcasted_iota(jnp.int32, (2, pair_width), 0)
    )
    masked = jnp.where(halves[None, None, None], queries[:, :, :, None, :], 0).astype(jnp.bfloat16)
    masked = jnp.concatenate([masked, jnp.zeros_like(masked)], axis=2)
    scores = jnp.einsum(
        "blqje,btqe->bqjlt", masked, kv_rows, preferred_element_type=jnp.float32
    )[:, :pair_count] * HEAD_DIM ** (-0.5)
    scores = jnp.where(live_tokens[:, None, None, None, :], scores, masked_score)
    row_max = jnp.max(scores, axis=-1, keepdims=True)
    exponent = jnp.exp(scores - row_max)
    denominator = jnp.sum(exponent, axis=-1, keepdims=True)
    weights = exponent.astype(jnp.bfloat16)
    weights = jnp.concatenate([jnp.zeros_like(weights), weights], axis=1)
    mix = jnp.einsum(
        "bqjlt,btqe->bqjle", weights, kv_rows, preferred_element_type=jnp.float32
    )[:, pair_count:] / denominator
    mix = jnp.sum(jnp.where(halves[None, None, :, None, :], mix, 0.0), axis=2)
    return jnp.transpose(mix, (0, 2, 1, 3)).reshape(samples, latents, pair_count * pair_width).astype(
        jnp.bfloat16
    )


def attend_block(counts_ref, query_ref, key_ref, value_ref, out_ref):
    group = pl.program_id(0)
    latents = query_ref.shape[1]
    tokens = key_ref.shape[1]
    live = lax.broadcasted_iota(jnp.int32, (latents, tokens), 1) < counts_ref[group]
    first_head = lax.broadcasted_iota(jnp.int32, (1, 2 * HEAD_DIM), 1) < HEAD_DIM
    for pair in range(query_ref.shape[2] // (2 * HEAD_DIM)):
        cols = pl.ds(pair * 2 * HEAD_DIM, 2 * HEAD_DIM)
        query = query_ref[0, :, cols]
        key = key_ref[0, :, cols]
        value = value_ref[0, :, cols]
        mixes = []
        for half in (first_head, jnp.logical_not(first_head)):
            scores = lax.dot_general(
                jnp.where(half, query, jnp.zeros_like(query)),
                key,
                (((1,), (1,)), ((), ())),
                preferred_element_type=jnp.float32,
            ) * HEAD_DIM ** (-0.5)
            scores = jnp.where(live, scores, masked_score)
            row_max = jnp.max(scores, axis=1, keepdims=True)
            exponent = jnp.exp(scores - row_max)
            denominator = jnp.sum(exponent, axis=1, keepdims=True)
            mix = jnp.dot(
                exponent.astype(jnp.bfloat16), value, preferred_element_type=jnp.float32
            )
            mixes.append(mix / denominator)
        out_ref[0, :, cols] = jnp.where(first_head, mixes[0], mixes[1]).astype(jnp.bfloat16)


def attend_kernel(queries, key_value, counts):
    groups, latents, width = queries.shape
    tokens = key_value.shape[1]
    return pl.pallas_call(
        attend_block,
        grid_spec=pltpu.PrefetchScalarGridSpec(
            num_scalar_prefetch=1,
            grid=(groups,),
            in_specs=[
                pl.BlockSpec((1, latents, width), lambda g, c: (g, 0, 0)),
                pl.BlockSpec((1, tokens, width), lambda g, c: (g, 0, 0)),
                pl.BlockSpec((1, tokens, width), lambda g, c: (g, 0, 1)),
            ],
            out_specs=pl.BlockSpec((1, latents, width), lambda g, c: (g, 0, 0)),
        ),
        out_shape=jax.ShapeDtypeStruct((groups, latents, width), jnp.bfloat16),
    )(counts, queries, key_value, key_value)


def per_device(
    state,
    unit_slot,
    token_count,
    session,
    session_row,
    unit_count,
    panels,
    memory_key,
    memory_value,
    q1_weight,
    o1_weight,
    kv_weight,
    q2_weight,
    o2_weight,
):
    local_samples, latents, model_width = state.shape
    token_total = unit_slot.shape[1]
    owners = lax.axis_size("smp")
    sess_dev, unit_total = (panels.shape[0], panels.shape[1])
    head_count = model_width // HEAD_DIM
    session_ids = jnp.arange(session_row.shape[0], dtype=jnp.int32)
    panel_row = jnp.sum(
        jnp.where(session[:, None] == session_ids[None, :], session_row[None, :], 0), axis=1
    )
    unit_limit = jnp.sum(
        jnp.where(panel_row[:, None] == session_ids[None, :], unit_count[None, :], 0), axis=1
    )
    owner_rank = panel_row // sess_dev
    token_index = (panel_row % sess_dev * unit_total)[:, None] + unit_slot % unit_limit[:, None]
    slot_pick = owner_rank[None, :] == jnp.arange(owners, dtype=jnp.int32)[:, None]
    request = jnp.sum(jnp.where(slot_pick[:, :, None], token_index[None, :, :], 0), axis=1)
    count_pick = jnp.sum(jnp.where(slot_pick, token_count[None, :], 0), axis=1)
    sample_pick = jnp.sum(
        jnp.where(slot_pick, jnp.arange(local_samples, dtype=jnp.int32)[None, :], 0), axis=1
    )
    panel_table = panels.reshape(sess_dev * unit_total, model_width)
    panel_normed = normed(panel_table)
    kv_flat = jnp.dot(panel_normed, kv_weight, preferred_element_type=jnp.float32).astype(
        jnp.bfloat16
    )
    panel_total = kv_flat.shape[0]
    kv_table = kv_flat.reshape(panel_total, head_count, 2 * HEAD_DIM)
    row_total = local_samples * latents
    flat_state = state.reshape(row_total, model_width)
    queries = jnp.dot(normed(flat_state), q1_weight, preferred_element_type=jnp.float32).astype(
        jnp.bfloat16
    )
    table = jnp.concatenate([request, count_pick[:, None]], axis=1)
    code_base = 64
    codes = jnp.concatenate([table // code_base, table % code_base], axis=1).astype(jnp.bfloat16)
    memory_pair = jnp.concatenate([memory_key, memory_value], axis=1)
    memory_count = memory_pair.shape[0]
    code_lanes = 2 * HEAD_DIM
    code_block = jnp.pad(codes, ((0, 0), (0, memory_count * code_lanes - codes.shape[1])))
    arrived = lax.all_to_all(
        jnp.concatenate(
            [
                jnp.broadcast_to(memory_pair[None], (owners,) + memory_pair.shape),
                code_block.reshape(owners, memory_count, code_lanes),
            ],
            axis=2,
        ),
        "smp",
        split_axis=0,
        concat_axis=0,
        tiled=True,
    )
    memory_rows = arrived.reshape(1, -1, arrived.shape[2])
    code_back = (
        arrived[:, :, 2 * model_width :].reshape(owners, -1)[:, : codes.shape[1]].astype(jnp.int32)
    )
    served = code_back[:, : table.shape[1]] * code_base + code_back[:, table.shape[1] :]
    served_index = served[:, :token_total]
    memory_total = memory_rows.shape[1]
    read_mem = attend_kernel(
        queries.reshape(1, row_total, model_width),
        memory_rows,
        jnp.full((1,), memory_total, jnp.int32),
    ).reshape(row_total, model_width)
    hidden = (
        flat_state.astype(jnp.float32)
        + jnp.dot(read_mem, o1_weight, preferred_element_type=jnp.float32)
    ).astype(jnp.bfloat16)
    queries2 = jnp.dot(normed(hidden), q2_weight, preferred_element_type=jnp.float32).astype(
        jnp.bfloat16
    )
    queries2 = queries2.reshape(local_samples, latents, model_width)
    served_queries = lax.all_to_all(
        jnp.einsum(
            "ob,bld->old",
            (sample_pick[:, None] == jnp.arange(local_samples, dtype=jnp.int32)[None, :]).astype(
                jnp.bfloat16
            ),
            queries2,
            preferred_element_type=jnp.float32,
        ).astype(jnp.bfloat16),
        "smp",
        split_axis=0,
        concat_axis=0,
        tiled=True,
    )
    kv_rows = kv_table[served_index]
    live_tokens = jnp.arange(token_total, dtype=jnp.int32)[None, :] < served[:, token_total:]
    served_read = attend_stacked(
        served_queries.reshape(owners, latents, head_count // 2, 2 * HEAD_DIM),
        kv_rows.reshape(owners, token_total, head_count, 2 * HEAD_DIM),
        live_tokens,
    )
    read_spike = lax.all_to_all(
        served_read.reshape(owners, latents, model_width),
        "smp",
        split_axis=0,
        concat_axis=0,
        tiled=True,
    )[owner_rank]
    result = hidden.astype(jnp.float32) + jnp.dot(
        read_spike.reshape(row_total, model_width), o2_weight, preferred_element_type=jnp.float32
    )
    return result.astype(jnp.bfloat16).reshape(local_samples, latents, model_width)


def solution(mesh):
    in_specs = (
        P(("grp", "smp"), None, None),
        P(("grp", "smp"), None),
        P(("grp", "smp")),
        P(("grp", "smp")),
        P("grp"),
        P(),
        P("smp", None, None),
        P(("grp", "smp"), None),
        P(("grp", "smp"), None),
        P(),
        P(),
        P(),
        P(),
        P(),
    )
    out_specs = P(("grp", "smp"), None, None)
    return jax.shard_map(
        per_device, mesh=mesh, in_specs=in_specs, out_specs=out_specs, check_vma=False
    )
```

```python
import functools

import jax
import jax.numpy as jnp
from jax import lax
from jax.experimental import pallas as pl
from jax.experimental.pallas import tpu as pltpu
from jax.sharding import PartitionSpec as P

HEAD_DIM = 64


masked_score = -1e30


def normed(values):
    wide = values.astype(jnp.float32)
    return (wide * lax.rsqrt(jnp.mean(wide * wide, axis=-1, keepdims=True) + 1e-05)).astype(
        jnp.bfloat16
    )


def attend(queries, key_rows, value_rows, live_tokens):
    samples, latents, head_count, head_size = queries.shape
    spike_scores = jnp.einsum(
        "blhd,bkhd->bhlk", queries, key_rows, preferred_element_type=jnp.float32
    ) * HEAD_DIM ** (-0.5)
    spike_scores = jnp.where(live_tokens[:, None, None, :], spike_scores, masked_score)
    spike_max = jnp.max(spike_scores, axis=-1, keepdims=True)
    spike_exp = jnp.exp(spike_scores - spike_max)
    denominator = jnp.transpose(jnp.sum(spike_exp, axis=-1, keepdims=True), (0, 2, 1, 3))
    spike_mix = (
        jnp.einsum(
            "bhlk,bkhd->blhd",
            spike_exp.astype(jnp.bfloat16),
            value_rows,
            preferred_element_type=jnp.float32,
        )
        / denominator
    )
    return spike_mix.reshape(samples, latents, head_count * head_size).astype(jnp.bfloat16)


def attend_heads(queries, key_rows, value_rows, live_tokens):
    samples, latents, head_count, head_size = queries.shape
    spike_scores = jnp.einsum(
        "blhd,bkhd->bhlk", queries, key_rows, preferred_element_type=jnp.float32
    ) * HEAD_DIM ** (-0.5)
    spike_scores = jnp.where(live_tokens[:, None, None, :], spike_scores, masked_score)
    spike_max = jnp.max(spike_scores, axis=-1, keepdims=True)
    spike_exp = jnp.exp(spike_scores - spike_max)
    denominator = jnp.transpose(jnp.sum(spike_exp, axis=-1, keepdims=True), (0, 2, 1, 3))
    spike_mix = (
        jnp.einsum(
            "bhlk,bkhd->blhd",
            spike_exp.astype(jnp.bfloat16),
            value_rows,
            preferred_element_type=jnp.float32,
        )
        / denominator
    )
    return spike_mix.reshape(samples, latents, head_count * head_size).astype(jnp.bfloat16)


def attend_pairs(queries, key_rows, value_rows, live_tokens):
    samples, latents, pair_count, pair_width = queries.shape
    halves = (
        lax.broadcasted_iota(jnp.int32, (2, pair_width), 1) // HEAD_DIM
        == lax.broadcasted_iota(jnp.int32, (2, pair_width), 0)
    )
    masked = jnp.where(halves[None, None, None], queries[:, :, :, None, :], 0).astype(jnp.bfloat16)
    scores = jnp.einsum(
        "blqje,btqe->bqjlt", masked, key_rows, preferred_element_type=jnp.float32
    ) * HEAD_DIM ** (-0.5)
    scores = jnp.where(live_tokens[:, None, None, None, :], scores, masked_score)
    row_max = jnp.max(scores, axis=-1, keepdims=True)
    exponent = jnp.exp(scores - row_max)
    denominator = jnp.sum(exponent, axis=-1, keepdims=True)
    mix = jnp.einsum(
        "bqjlt,btqe->bqjle",
        exponent.astype(jnp.bfloat16),
        value_rows,
        preferred_element_type=jnp.float32,
    ) / denominator
    mix = jnp.sum(jnp.where(halves[None, None, :, None, :], mix, 0.0), axis=2)
    return jnp.transpose(mix, (0, 2, 1, 3)).reshape(samples, latents, pair_count * pair_width).astype(
        jnp.bfloat16
    )


def attend_block(counts_ref, query_ref, key_ref, value_ref, out_ref, all_live=False):
    group = pl.program_id(0)
    latents = query_ref.shape[1]
    tokens = key_ref.shape[1]
    live = lax.broadcasted_iota(jnp.int32, (latents, tokens), 1) < counts_ref[group]
    first_head = lax.broadcasted_iota(jnp.int32, (1, 2 * HEAD_DIM), 1) < HEAD_DIM
    for pair in range(query_ref.shape[2] // (2 * HEAD_DIM)):
        cols = pl.ds(pair * 2 * HEAD_DIM, 2 * HEAD_DIM)
        query = query_ref[0, :, cols]
        key = key_ref[0, :, cols]
        value = value_ref[0, :, cols]
        mixes = []
        for half in (first_head, jnp.logical_not(first_head)):
            scores = lax.dot_general(
                jnp.where(half, query, jnp.zeros_like(query)),
                key,
                (((1,), (1,)), ((), ())),
                preferred_element_type=jnp.float32,
            ) * HEAD_DIM ** (-0.5)
            if not all_live:
                scores = jnp.where(live, scores, masked_score)
            row_max = jnp.max(scores, axis=1, keepdims=True)
            exponent = jnp.exp(scores - row_max)
            denominator = jnp.sum(exponent, axis=1, keepdims=True)
            mix = jnp.dot(
                exponent.astype(jnp.bfloat16), value, preferred_element_type=jnp.float32
            )
            mixes.append(mix / denominator)
        out_ref[0, :, cols] = jnp.where(first_head, mixes[0], mixes[1]).astype(jnp.bfloat16)


def attend_kernel(queries, key_value, counts, all_live=False):
    groups, latents, width = queries.shape
    tokens = key_value.shape[1]
    return pl.pallas_call(
        functools.partial(attend_block, all_live=all_live),
        grid_spec=pltpu.PrefetchScalarGridSpec(
            num_scalar_prefetch=1,
            grid=(groups,),
            in_specs=[
                pl.BlockSpec((1, latents, width), lambda g, c: (g, 0, 0)),
                pl.BlockSpec((1, tokens, width), lambda g, c: (g, 0, 0)),
                pl.BlockSpec((1, tokens, width), lambda g, c: (g, 0, 1)),
            ],
            out_specs=pl.BlockSpec((1, latents, width), lambda g, c: (g, 0, 0)),
        ),
        out_shape=jax.ShapeDtypeStruct((groups, latents, width), jnp.bfloat16),
    )(counts, queries, key_value, key_value)


def per_device(
    state,
    unit_slot,
    token_count,
    session,
    session_row,
    unit_count,
    panels,
    memory_key,
    memory_value,
    q1_weight,
    o1_weight,
    kv_weight,
    q2_weight,
    o2_weight,
):
    local_samples, latents, model_width = state.shape
    token_total = unit_slot.shape[1]
    owners = lax.axis_size("smp")
    sess_dev, unit_total = (panels.shape[0], panels.shape[1])
    head_count = model_width // HEAD_DIM
    session_ids = jnp.arange(session_row.shape[0], dtype=jnp.int32)
    panel_row = jnp.sum(
        jnp.where(session[:, None] == session_ids[None, :], session_row[None, :], 0), axis=1
    )
    unit_limit = jnp.sum(
        jnp.where(panel_row[:, None] == session_ids[None, :], unit_count[None, :], 0), axis=1
    )
    owner_rank = panel_row // sess_dev
    token_index = (panel_row % sess_dev * unit_total)[:, None] + unit_slot % unit_limit[:, None]
    slot_pick = owner_rank[None, :] == jnp.arange(owners, dtype=jnp.int32)[:, None]
    request = jnp.sum(jnp.where(slot_pick[:, :, None], token_index[None, :, :], 0), axis=1)
    count_pick = jnp.sum(jnp.where(slot_pick, token_count[None, :], 0), axis=1)
    sample_pick = jnp.sum(
        jnp.where(slot_pick, jnp.arange(local_samples, dtype=jnp.int32)[None, :], 0), axis=1
    )
    panel_table = panels.reshape(sess_dev * unit_total, model_width)
    panel_normed = normed(panel_table)
    kv_flat = jnp.dot(panel_normed, kv_weight, preferred_element_type=jnp.float32).astype(
        jnp.bfloat16
    )
    panel_total = kv_flat.shape[0]
    kv_table = kv_flat.reshape(panel_total, head_count, 2 * HEAD_DIM)
    row_total = local_samples * latents
    flat_state = state.reshape(row_total, model_width)
    queries = jnp.dot(normed(flat_state), q1_weight, preferred_element_type=jnp.float32).astype(
        jnp.bfloat16
    )
    table = jnp.concatenate([request, count_pick[:, None]], axis=1)
    code_base = 64
    codes = jnp.concatenate([table // code_base, table % code_base], axis=1).astype(jnp.bfloat16)
    memory_pair = jnp.concatenate([memory_key, memory_value], axis=1)
    memory_count = memory_pair.shape[0]
    code_lanes = 2 * HEAD_DIM
    code_block = jnp.pad(codes, ((0, 0), (0, memory_count * code_lanes - codes.shape[1])))
    arrived = lax.all_to_all(
        jnp.concatenate(
            [
                jnp.broadcast_to(memory_pair[None], (owners,) + memory_pair.shape),
                code_block.reshape(owners, memory_count, code_lanes),
            ],
            axis=2,
        ),
        "smp",
        split_axis=0,
        concat_axis=0,
        tiled=True,
    )
    memory_rows = arrived.reshape(1, -1, arrived.shape[2])
    code_back = (
        arrived[:, :, 2 * model_width :].reshape(owners, -1)[:, : codes.shape[1]].astype(jnp.int32)
    )
    served = code_back[:, : table.shape[1]] * code_base + code_back[:, table.shape[1] :]
    served_index = served[:, :token_total]
    memory_total = memory_rows.shape[1]
    read_mem = attend_kernel(
        queries.reshape(1, row_total, model_width),
        memory_rows,
        jnp.full((1,), memory_total, jnp.int32),
        all_live=True,
    ).reshape(row_total, model_width)
    hidden = (
        flat_state.astype(jnp.float32)
        + jnp.dot(read_mem, o1_weight, preferred_element_type=jnp.float32)
    ).astype(jnp.bfloat16)
    queries2 = jnp.dot(normed(hidden), q2_weight, preferred_element_type=jnp.float32).astype(
        jnp.bfloat16
    )
    queries2 = queries2.reshape(local_samples, latents, model_width)
    served_queries = lax.all_to_all(
        jnp.einsum(
            "ob,bld->old",
            (sample_pick[:, None] == jnp.arange(local_samples, dtype=jnp.int32)[None, :]).astype(
                jnp.bfloat16
            ),
            queries2,
            preferred_element_type=jnp.float32,
        ).astype(jnp.bfloat16),
        "smp",
        split_axis=0,
        concat_axis=0,
        tiled=True,
    )
    kv_rows = kv_table[served_index]
    key_rows = kv_rows[:, :, : head_count // 2]
    value_rows = kv_rows[:, :, head_count // 2 :]
    live_tokens = jnp.arange(token_total, dtype=jnp.int32)[None, :] < served[:, token_total:]
    served_read = attend_pairs(
        served_queries.reshape(owners, latents, head_count // 2, 2 * HEAD_DIM),
        key_rows.reshape(owners, token_total, head_count // 2, 2 * HEAD_DIM),
        value_rows.reshape(owners, token_total, head_count // 2, 2 * HEAD_DIM),
        live_tokens,
    )
    read_spike = lax.all_to_all(
        served_read.reshape(owners, latents, model_width),
        "smp",
        split_axis=0,
        concat_axis=0,
        tiled=True,
    )[owner_rank]
    result = hidden.astype(jnp.float32) + jnp.dot(
        read_spike.reshape(row_total, model_width), o2_weight, preferred_element_type=jnp.float32
    )
    return result.astype(jnp.bfloat16).reshape(local_samples, latents, model_width)


def solution(mesh):
    in_specs = (
        P(("grp", "smp"), None, None),
        P(("grp", "smp"), None),
        P(("grp", "smp")),
        P(("grp", "smp")),
        P("grp"),
        P(),
        P("smp", None, None),
        P(("grp", "smp"), None),
        P(("grp", "smp"), None),
        P(),
        P(),
        P(),
        P(),
        P(),
    )
    out_specs = P(("grp", "smp"), None, None)
    return jax.shard_map(
        per_device, mesh=mesh, in_specs=in_specs, out_specs=out_specs, check_vma=False
    )
```

```python
import jax
import jax.numpy as jnp
from jax import lax
from jax.experimental import pallas as pl
from jax.experimental.pallas import tpu as pltpu
from jax.sharding import PartitionSpec as P

HEAD_DIM = 64


masked_score = -1e30


def normed(values):
    wide = values.astype(jnp.float32)
    return (wide * lax.rsqrt(jnp.mean(wide * wide, axis=-1, keepdims=True) + 1e-05)).astype(
        jnp.bfloat16
    )


def attend(queries, key_rows, value_rows, live_tokens):
    samples, latents, head_count, head_size = queries.shape
    spike_scores = jnp.einsum(
        "blhd,bkhd->bhlk", queries, key_rows, preferred_element_type=jnp.float32
    ) * HEAD_DIM ** (-0.5)
    spike_scores = jnp.where(live_tokens[:, None, None, :], spike_scores, masked_score)
    spike_max = jnp.max(spike_scores, axis=-1, keepdims=True)
    spike_exp = jnp.exp(spike_scores - spike_max)
    denominator = jnp.transpose(jnp.sum(spike_exp, axis=-1, keepdims=True), (0, 2, 1, 3))
    spike_mix = (
        jnp.einsum(
            "bhlk,bkhd->blhd",
            spike_exp.astype(jnp.bfloat16),
            value_rows,
            preferred_element_type=jnp.float32,
        )
        / denominator
    )
    return spike_mix.reshape(samples, latents, head_count * head_size).astype(jnp.bfloat16)


def attend_heads(queries, key_rows, value_rows, live_tokens):
    samples, latents, head_count, head_size = queries.shape
    spike_scores = jnp.einsum(
        "blhd,bkhd->bhlk", queries, key_rows, preferred_element_type=jnp.float32
    ) * HEAD_DIM ** (-0.5)
    spike_scores = jnp.where(live_tokens[:, None, None, :], spike_scores, masked_score)
    spike_max = jnp.max(spike_scores, axis=-1, keepdims=True)
    spike_exp = jnp.exp(spike_scores - spike_max)
    denominator = jnp.transpose(jnp.sum(spike_exp, axis=-1, keepdims=True), (0, 2, 1, 3))
    spike_mix = (
        jnp.einsum(
            "bhlk,bkhd->blhd",
            spike_exp.astype(jnp.bfloat16),
            value_rows,
            preferred_element_type=jnp.float32,
        )
        / denominator
    )
    return spike_mix.reshape(samples, latents, head_count * head_size).astype(jnp.bfloat16)


def attend_pairs(queries, key_rows, value_rows, live_tokens):
    samples, latents, pair_count, pair_width = queries.shape
    halves = (
        lax.broadcasted_iota(jnp.int32, (2, pair_width), 1) // HEAD_DIM
        == lax.broadcasted_iota(jnp.int32, (2, pair_width), 0)
    )
    masked = jnp.where(halves[None, None, None], queries[:, :, :, None, :], 0).astype(jnp.bfloat16)
    scores = jnp.einsum(
        "blqje,btqe->bqjlt", masked, key_rows, preferred_element_type=jnp.float32
    ) * HEAD_DIM ** (-0.5)
    scores = jnp.where(live_tokens[:, None, None, None, :], scores, masked_score)
    row_max = jnp.max(scores, axis=-1, keepdims=True)
    exponent = jnp.exp(scores - row_max)
    denominator = jnp.sum(exponent, axis=-1, keepdims=True)
    mix = jnp.einsum(
        "bqjlt,btqe->bqjle",
        exponent.astype(jnp.bfloat16),
        value_rows,
        preferred_element_type=jnp.float32,
    ) / denominator
    mix = jnp.sum(jnp.where(halves[None, None, :, None, :], mix, 0.0), axis=2)
    return jnp.transpose(mix, (0, 2, 1, 3)).reshape(samples, latents, pair_count * pair_width).astype(
        jnp.bfloat16
    )


def attend_block(counts_ref, query_ref, key_ref, value_ref, out_ref):
    group = pl.program_id(0)
    latents = query_ref.shape[1]
    tokens = key_ref.shape[1]
    live = lax.broadcasted_iota(jnp.int32, (latents, tokens), 1) < counts_ref[group]
    first_head = lax.broadcasted_iota(jnp.int32, (1, 2 * HEAD_DIM), 1) < HEAD_DIM
    for pair in range(query_ref.shape[2] // (2 * HEAD_DIM)):
        cols = pl.ds(pair * 2 * HEAD_DIM, 2 * HEAD_DIM)
        query = query_ref[0, :, cols]
        key = key_ref[0, :, cols]
        value = value_ref[0, :, cols]
        mixes = []
        for half in (first_head, jnp.logical_not(first_head)):
            scores = lax.dot_general(
                jnp.where(half, query, jnp.zeros_like(query)),
                key,
                (((1,), (1,)), ((), ())),
                preferred_element_type=jnp.float32,
            ) * HEAD_DIM ** (-0.5)
            scores = jnp.where(live, scores, masked_score)
            row_max = jnp.max(scores, axis=1, keepdims=True)
            exponent = jnp.exp(scores - row_max)
            denominator = jnp.sum(exponent, axis=1, keepdims=True)
            mix = jnp.dot(
                exponent.astype(jnp.bfloat16), value, preferred_element_type=jnp.float32
            )
            mixes.append(mix / denominator)
        out_ref[0, :, cols] = jnp.where(first_head, mixes[0], mixes[1]).astype(jnp.bfloat16)


def attend_kernel(queries, key_value, counts):
    groups, latents, width = queries.shape
    tokens = key_value.shape[1]
    return pl.pallas_call(
        attend_block,
        grid_spec=pltpu.PrefetchScalarGridSpec(
            num_scalar_prefetch=1,
            grid=(groups,),
            in_specs=[
                pl.BlockSpec((1, latents, width), lambda g, c: (g, 0, 0)),
                pl.BlockSpec((1, tokens, width), lambda g, c: (g, 0, 0)),
                pl.BlockSpec((1, tokens, width), lambda g, c: (g, 0, 1)),
            ],
            out_specs=pl.BlockSpec((1, latents, width), lambda g, c: (g, 0, 0)),
        ),
        out_shape=jax.ShapeDtypeStruct((groups, latents, width), jnp.bfloat16),
    )(counts, queries, key_value, key_value)


def per_device(
    state,
    unit_slot,
    token_count,
    session,
    session_row,
    unit_count,
    panels,
    memory_key,
    memory_value,
    q1_weight,
    o1_weight,
    kv_weight,
    q2_weight,
    o2_weight,
):
    local_samples, latents, model_width = state.shape
    token_total = unit_slot.shape[1]
    owners = lax.axis_size("smp")
    sess_dev, unit_total = (panels.shape[0], panels.shape[1])
    head_count = model_width // HEAD_DIM
    session_ids = jnp.arange(session_row.shape[0], dtype=jnp.int32)
    panel_row = jnp.sum(
        jnp.where(session[:, None] == session_ids[None, :], session_row[None, :], 0), axis=1
    )
    unit_limit = jnp.sum(
        jnp.where(panel_row[:, None] == session_ids[None, :], unit_count[None, :], 0), axis=1
    )
    owner_rank = panel_row // sess_dev
    token_index = (panel_row % sess_dev * unit_total)[:, None] + unit_slot % unit_limit[:, None]
    slot_pick = owner_rank[None, :] == jnp.arange(owners, dtype=jnp.int32)[:, None]
    request = jnp.sum(jnp.where(slot_pick[:, :, None], token_index[None, :, :], 0), axis=1)
    count_pick = jnp.sum(jnp.where(slot_pick, token_count[None, :], 0), axis=1)
    sample_pick = jnp.sum(
        jnp.where(slot_pick, jnp.arange(local_samples, dtype=jnp.int32)[None, :], 0), axis=1
    )
    panel_table = panels.reshape(sess_dev * unit_total, model_width)
    panel_normed = normed(panel_table)
    kv_flat = jnp.dot(panel_normed, kv_weight, preferred_element_type=jnp.float32).astype(
        jnp.bfloat16
    )
    panel_total = kv_flat.shape[0]
    kv_table = kv_flat.reshape(panel_total, head_count, 2 * HEAD_DIM)
    slot_onehot = (
        sample_pick[:, None] == jnp.arange(local_samples, dtype=jnp.int32)[None, :]
    ).astype(jnp.bfloat16)
    slot_state = jnp.einsum(
        "ob,bld->old", slot_onehot, state, preferred_element_type=jnp.float32
    ).astype(jnp.bfloat16)
    row_total = owners * latents
    flat_state = slot_state.reshape(row_total, model_width)
    queries = jnp.dot(normed(flat_state), q1_weight, preferred_element_type=jnp.float32).astype(
        jnp.bfloat16
    )
    table = jnp.concatenate([request, count_pick[:, None]], axis=1)
    code_base = 64
    codes = jnp.concatenate([table // code_base, table % code_base], axis=1).astype(jnp.bfloat16)
    memory_pair = jnp.concatenate([memory_key, memory_value], axis=1)
    memory_count = memory_pair.shape[0]
    code_lanes = 2 * HEAD_DIM
    code_block = jnp.pad(codes, ((0, 0), (0, memory_count * code_lanes - codes.shape[1])))
    arrived = lax.all_to_all(
        jnp.concatenate(
            [
                jnp.broadcast_to(memory_pair[None], (owners,) + memory_pair.shape),
                code_block.reshape(owners, memory_count, code_lanes),
            ],
            axis=2,
        ),
        "smp",
        split_axis=0,
        concat_axis=0,
        tiled=True,
    )
    memory_rows = arrived.reshape(1, -1, arrived.shape[2])
    code_back = (
        arrived[:, :, 2 * model_width :].reshape(owners, -1)[:, : codes.shape[1]].astype(jnp.int32)
    )
    served = code_back[:, : table.shape[1]] * code_base + code_back[:, table.shape[1] :]
    served_index = served[:, :token_total]
    memory_total = memory_rows.shape[1]
    read_mem = attend_kernel(
        queries.reshape(1, row_total, model_width),
        memory_rows,
        jnp.full((1,), memory_total, jnp.int32),
    ).reshape(row_total, model_width)
    hidden = (
        flat_state.astype(jnp.float32)
        + jnp.dot(read_mem, o1_weight, preferred_element_type=jnp.float32)
    ).astype(jnp.bfloat16)
    queries2 = jnp.dot(normed(hidden), q2_weight, preferred_element_type=jnp.float32).astype(
        jnp.bfloat16
    )
    served_queries = lax.all_to_all(
        queries2.reshape(owners, latents, model_width),
        "smp",
        split_axis=0,
        concat_axis=0,
        tiled=True,
    )
    kv_rows = kv_table[served_index]
    key_rows = kv_rows[:, :, : head_count // 2]
    value_rows = kv_rows[:, :, head_count // 2 :]
    live_tokens = jnp.arange(token_total, dtype=jnp.int32)[None, :] < served[:, token_total:]
    served_read = attend_pairs(
        served_queries.reshape(owners, latents, head_count // 2, 2 * HEAD_DIM),
        key_rows.reshape(owners, token_total, head_count // 2, 2 * HEAD_DIM),
        value_rows.reshape(owners, token_total, head_count // 2, 2 * HEAD_DIM),
        live_tokens,
    )
    read_spike = lax.all_to_all(
        served_read.reshape(owners, latents, model_width),
        "smp",
        split_axis=0,
        concat_axis=0,
        tiled=True,
    )
    result = (
        hidden.astype(jnp.float32)
        + jnp.dot(
            read_spike.reshape(row_total, model_width), o2_weight, preferred_element_type=jnp.float32
        )
    ).astype(jnp.bfloat16)
    return result.reshape(owners, latents, model_width)[owner_rank]


def solution(mesh):
    in_specs = (
        P(("grp", "smp"), None, None),
        P(("grp", "smp"), None),
        P(("grp", "smp")),
        P(("grp", "smp")),
        P("grp"),
        P(),
        P("smp", None, None),
        P(("grp", "smp"), None),
        P(("grp", "smp"), None),
        P(),
        P(),
        P(),
        P(),
        P(),
    )
    out_specs = P(("grp", "smp"), None, None)
    return jax.shard_map(
        per_device, mesh=mesh, in_specs=in_specs, out_specs=out_specs, check_vma=False
    )
```

```python
import functools

import jax
import jax.numpy as jnp
from jax import lax
from jax.experimental import pallas as pl
from jax.experimental.pallas import tpu as pltpu
from jax.sharding import PartitionSpec as P

HEAD_DIM = 64


masked_score = -1e30


def normed(values):
    wide = values.astype(jnp.float32)
    return (wide * lax.rsqrt(jnp.mean(wide * wide, axis=-1, keepdims=True) + 1e-05)).astype(
        jnp.bfloat16
    )


def attend(queries, key_rows, value_rows, live_tokens):
    samples, latents, head_count, head_size = queries.shape
    spike_scores = jnp.einsum(
        "blhd,bkhd->bhlk", queries, key_rows, preferred_element_type=jnp.float32
    ) * HEAD_DIM ** (-0.5)
    spike_scores = jnp.where(live_tokens[:, None, None, :], spike_scores, masked_score)
    spike_max = jnp.max(spike_scores, axis=-1, keepdims=True)
    spike_exp = jnp.exp(spike_scores - spike_max)
    denominator = jnp.transpose(jnp.sum(spike_exp, axis=-1, keepdims=True), (0, 2, 1, 3))
    spike_mix = (
        jnp.einsum(
            "bhlk,bkhd->blhd",
            spike_exp.astype(jnp.bfloat16),
            value_rows,
            preferred_element_type=jnp.float32,
        )
        / denominator
    )
    return spike_mix.reshape(samples, latents, head_count * head_size).astype(jnp.bfloat16)


def attend_heads(queries, key_rows, value_rows, live_tokens):
    samples, latents, head_count, head_size = queries.shape
    spike_scores = jnp.einsum(
        "blhd,bkhd->bhlk", queries, key_rows, preferred_element_type=jnp.float32
    ) * HEAD_DIM ** (-0.5)
    spike_scores = jnp.where(live_tokens[:, None, None, :], spike_scores, masked_score)
    spike_max = jnp.max(spike_scores, axis=-1, keepdims=True)
    spike_exp = jnp.exp(spike_scores - spike_max)
    denominator = jnp.transpose(jnp.sum(spike_exp, axis=-1, keepdims=True), (0, 2, 1, 3))
    spike_mix = (
        jnp.einsum(
            "bhlk,bkhd->blhd",
            spike_exp.astype(jnp.bfloat16),
            value_rows,
            preferred_element_type=jnp.float32,
        )
        / denominator
    )
    return spike_mix.reshape(samples, latents, head_count * head_size).astype(jnp.bfloat16)


def attend_pairs(queries, key_rows, value_rows, live_tokens):
    samples, latents, pair_count, pair_width = queries.shape
    halves = (
        lax.broadcasted_iota(jnp.int32, (2, pair_width), 1) // HEAD_DIM
        == lax.broadcasted_iota(jnp.int32, (2, pair_width), 0)
    )
    masked = jnp.where(halves[None, None, None], queries[:, :, :, None, :], 0).astype(jnp.bfloat16)
    scores = jnp.einsum(
        "blqje,btqe->bqjlt", masked, key_rows, preferred_element_type=jnp.float32
    ) * HEAD_DIM ** (-0.5)
    scores = jnp.where(live_tokens[:, None, None, None, :], scores, masked_score)
    row_max = jnp.max(scores, axis=-1, keepdims=True)
    exponent = jnp.exp(scores - row_max)
    denominator = jnp.sum(exponent, axis=-1, keepdims=True)
    mix = jnp.einsum(
        "bqjlt,btqe->bqjle",
        exponent.astype(jnp.bfloat16),
        value_rows,
        preferred_element_type=jnp.float32,
    ) / denominator
    mix = jnp.sum(jnp.where(halves[None, None, :, None, :], mix, 0.0), axis=2)
    return jnp.transpose(mix, (0, 2, 1, 3)).reshape(samples, latents, pair_count * pair_width).astype(
        jnp.bfloat16
    )


def attend_stacked(queries, kv_rows, live_tokens):
    samples, latents, pair_count, pair_width = queries.shape
    halves = (
        lax.broadcasted_iota(jnp.int32, (2, pair_width), 1) // HEAD_DIM
        == lax.broadcasted_iota(jnp.int32, (2, pair_width), 0)
    )
    masked = jnp.where(halves[None, None, None], queries[:, :, :, None, :], 0).astype(jnp.bfloat16)
    masked = jnp.concatenate([masked, jnp.zeros_like(masked)], axis=2)
    scores = jnp.einsum(
        "blqje,btqe->bqjlt", masked, kv_rows, preferred_element_type=jnp.float32
    )[:, :pair_count] * HEAD_DIM ** (-0.5)
    scores = jnp.where(live_tokens[:, None, None, None, :], scores, masked_score)
    row_max = jnp.max(scores, axis=-1, keepdims=True)
    exponent = jnp.exp(scores - row_max)
    denominator = jnp.sum(exponent, axis=-1, keepdims=True)
    weights = exponent.astype(jnp.bfloat16)
    weights = jnp.concatenate([jnp.zeros_like(weights), weights], axis=1)
    mix = jnp.einsum(
        "bqjlt,btqe->bqjle", weights, kv_rows, preferred_element_type=jnp.float32
    )[:, pair_count:] / denominator
    mix = jnp.sum(jnp.where(halves[None, None, :, None, :], mix, 0.0), axis=2)
    return jnp.transpose(mix, (0, 2, 1, 3)).reshape(samples, latents, pair_count * pair_width).astype(
        jnp.bfloat16
    )


def attend_block(counts_ref, query_ref, key_ref, value_ref, out_ref, all_live=False):
    group = pl.program_id(0)
    latents = query_ref.shape[1]
    tokens = key_ref.shape[1]
    live = lax.broadcasted_iota(jnp.int32, (latents, tokens), 1) < counts_ref[group]
    first_head = lax.broadcasted_iota(jnp.int32, (1, 2 * HEAD_DIM), 1) < HEAD_DIM
    for pair in range(query_ref.shape[2] // (2 * HEAD_DIM)):
        cols = pl.ds(pair * 2 * HEAD_DIM, 2 * HEAD_DIM)
        query = query_ref[0, :, cols]
        key = key_ref[0, :, cols]
        value = value_ref[0, :, cols]
        mixes = []
        for half in (first_head, jnp.logical_not(first_head)):
            scores = lax.dot_general(
                jnp.where(half, query, jnp.zeros_like(query)),
                key,
                (((1,), (1,)), ((), ())),
                preferred_element_type=jnp.float32,
            ) * HEAD_DIM ** (-0.5)
            if not all_live:
                scores = jnp.where(live, scores, masked_score)
            row_max = jnp.max(scores, axis=1, keepdims=True)
            exponent = jnp.exp(scores - row_max)
            denominator = jnp.sum(exponent, axis=1, keepdims=True)
            mix = jnp.dot(
                exponent.astype(jnp.bfloat16), value, preferred_element_type=jnp.float32
            )
            mixes.append(mix / denominator)
        out_ref[0, :, cols] = jnp.where(first_head, mixes[0], mixes[1]).astype(jnp.bfloat16)


def attend_kernel(queries, key_value, counts, all_live=False):
    groups, latents, width = queries.shape
    tokens = key_value.shape[1]
    return pl.pallas_call(
        functools.partial(attend_block, all_live=all_live),
        grid_spec=pltpu.PrefetchScalarGridSpec(
            num_scalar_prefetch=1,
            grid=(groups,),
            in_specs=[
                pl.BlockSpec((1, latents, width), lambda g, c: (g, 0, 0)),
                pl.BlockSpec((1, tokens, width), lambda g, c: (g, 0, 0)),
                pl.BlockSpec((1, tokens, width), lambda g, c: (g, 0, 1)),
            ],
            out_specs=pl.BlockSpec((1, latents, width), lambda g, c: (g, 0, 0)),
        ),
        out_shape=jax.ShapeDtypeStruct((groups, latents, width), jnp.bfloat16),
    )(counts, queries, key_value, key_value)


def per_device(
    state,
    unit_slot,
    token_count,
    session,
    session_row,
    unit_count,
    panels,
    memory_key,
    memory_value,
    q1_weight,
    o1_weight,
    kv_weight,
    q2_weight,
    o2_weight,
):
    local_samples, latents, model_width = state.shape
    token_total = unit_slot.shape[1]
    owners = lax.axis_size("smp")
    sess_dev, unit_total = (panels.shape[0], panels.shape[1])
    head_count = model_width // HEAD_DIM
    session_ids = jnp.arange(session_row.shape[0], dtype=jnp.int32)
    panel_row = jnp.sum(
        jnp.where(session[:, None] == session_ids[None, :], session_row[None, :], 0), axis=1
    )
    unit_limit = jnp.sum(
        jnp.where(panel_row[:, None] == session_ids[None, :], unit_count[None, :], 0), axis=1
    )
    owner_rank = panel_row // sess_dev
    token_index = (panel_row % sess_dev * unit_total)[:, None] + unit_slot % unit_limit[:, None]
    slot_pick = owner_rank[None, :] == jnp.arange(owners, dtype=jnp.int32)[:, None]
    request = jnp.sum(jnp.where(slot_pick[:, :, None], token_index[None, :, :], 0), axis=1)
    count_pick = jnp.sum(jnp.where(slot_pick, token_count[None, :], 0), axis=1)
    sample_pick = jnp.sum(
        jnp.where(slot_pick, jnp.arange(local_samples, dtype=jnp.int32)[None, :], 0), axis=1
    )
    panel_table = panels.reshape(sess_dev * unit_total, model_width)
    panel_normed = normed(panel_table)
    kv_flat = jnp.dot(panel_normed, kv_weight, preferred_element_type=jnp.float32).astype(
        jnp.bfloat16
    )
    panel_total = kv_flat.shape[0]
    kv_table = kv_flat.reshape(panel_total, head_count, 2 * HEAD_DIM)
    row_total = local_samples * latents
    flat_state = state.reshape(row_total, model_width)
    queries = jnp.dot(normed(flat_state), q1_weight, preferred_element_type=jnp.float32).astype(
        jnp.bfloat16
    )
    table = jnp.concatenate([request, count_pick[:, None]], axis=1)
    code_base = 64
    codes = jnp.concatenate([table // code_base, table % code_base], axis=1).astype(jnp.bfloat16)
    memory_pair = jnp.concatenate([memory_key, memory_value], axis=1)
    memory_count = memory_pair.shape[0]
    code_lanes = 2 * HEAD_DIM
    code_block = jnp.pad(codes, ((0, 0), (0, memory_count * code_lanes - codes.shape[1])))
    arrived = lax.all_to_all(
        jnp.concatenate(
            [
                jnp.broadcast_to(memory_pair[None], (owners,) + memory_pair.shape),
                code_block.reshape(owners, memory_count, code_lanes),
            ],
            axis=2,
        ),
        "smp",
        split_axis=0,
        concat_axis=0,
        tiled=True,
    )
    memory_rows = arrived.reshape(1, -1, arrived.shape[2])
    code_back = (
        arrived[:, :, 2 * model_width :].reshape(owners, -1)[:, : codes.shape[1]].astype(jnp.int32)
    )
    served = code_back[:, : table.shape[1]] * code_base + code_back[:, table.shape[1] :]
    served_index = served[:, :token_total]
    memory_total = memory_rows.shape[1]
    read_mem = attend_kernel(
        queries.reshape(1, row_total, model_width),
        memory_rows,
        jnp.full((1,), memory_total, jnp.int32),
        all_live=True,
    ).reshape(row_total, model_width)
    hidden = (
        flat_state.astype(jnp.float32)
        + jnp.dot(read_mem, o1_weight, preferred_element_type=jnp.float32)
    ).astype(jnp.bfloat16)
    queries2 = jnp.dot(normed(hidden), q2_weight, preferred_element_type=jnp.float32).astype(
        jnp.bfloat16
    )
    queries2 = queries2.reshape(local_samples, latents, model_width)
    served_queries = lax.all_to_all(
        jnp.einsum(
            "ob,bld->old",
            (sample_pick[:, None] == jnp.arange(local_samples, dtype=jnp.int32)[None, :]).astype(
                jnp.bfloat16
            ),
            queries2,
            preferred_element_type=jnp.float32,
        ).astype(jnp.bfloat16),
        "smp",
        split_axis=0,
        concat_axis=0,
        tiled=True,
    )
    kv_rows = kv_table[served_index]
    live_tokens = jnp.arange(token_total, dtype=jnp.int32)[None, :] < served[:, token_total:]
    served_read = attend_stacked(
        served_queries.reshape(owners, latents, head_count // 2, 2 * HEAD_DIM),
        kv_rows.reshape(owners, token_total, head_count, 2 * HEAD_DIM),
        live_tokens,
    )
    read_spike = lax.all_to_all(
        served_read.reshape(owners, latents, model_width),
        "smp",
        split_axis=0,
        concat_axis=0,
        tiled=True,
    )[owner_rank]
    result = hidden.astype(jnp.float32) + jnp.dot(
        read_spike.reshape(row_total, model_width), o2_weight, preferred_element_type=jnp.float32
    )
    return result.astype(jnp.bfloat16).reshape(local_samples, latents, model_width)


def solution(mesh):
    in_specs = (
        P(("grp", "smp"), None, None),
        P(("grp", "smp"), None),
        P(("grp", "smp")),
        P(("grp", "smp")),
        P("grp"),
        P(),
        P("smp", None, None),
        P(("grp", "smp"), None),
        P(("grp", "smp"), None),
        P(),
        P(),
        P(),
        P(),
        P(),
    )
    out_specs = P(("grp", "smp"), None, None)
    return jax.shard_map(
        per_device, mesh=mesh, in_specs=in_specs, out_specs=out_specs, check_vma=False
    )
```
